32 devices in a mesh: dev: 32 (over z, y, x, core).
Axes of the slice: x: 2, y: 2, z: 4, core: 2. Of those that a mesh axis runs over, the one named last changes fastest.
Arguments:
- tiles: bfloat16 [64, 128, 4096], P('dev'), may hold values from -6 to 6
- footprint: int32 [32, 21, 3], P('dev'), may hold values from 0 to 4032, as said below
- classes: int32 [32], P('dev'), may hold values from 0 to 15
- rotations: int32 [32], P('dev'), may hold values from 0 to 31
- references: bfloat16 [1024, 512], P('dev'), may hold values from -6 to 6
Outputs:
- scores: float32 [32, 512], P('dev')
- class_sums: float32 [1024, 512], P('dev')
The draws below stay inside these ranges and needn't reach their ends.
Inputs may be any that keep to these rules, and one draw needn't show every extreme that they name: Rows and columns of a footprint lie inside the tile (64 and 4032 at most). Of the footprints of one device's particles at most 2 lie in the tiles held by any one device, and one device holds exactly 2 footprints of every device's particles.
All inputs are finite; a program needn't handle non-finite values.
Results may differ from the reference program's by a relative error of at most 0.0047.
Values may be sent and summed in bfloat16 or wider, within the bound.
No kernel may reach another device: no remote copies, remote signals or barrier semaphores. Data moves between devices by JAX's collectives and lax.ppermute only.
A program may use at most 128 MiB of HBM per device.

```python
import jax
import jax.numpy as jnp
from jax import lax

W = 4096
TILE_ROWS = 128
TILTS = 21
BOX = 64
CYCLES = 16
ROTS = 32
CLASSES = 16
TILES_DEV = 2
P_DEV = 1
TILES = 64
PARTICLES = 32
CAP = 2
N_DEV = 32


def draw_footprint(key, part):
    shared = jax.random.fold_in(key, 11)
    hotspot = jax.random.randint(shared, (), 0, N_DEV)
    count = P_DEV * TILTS

    def one_device(subkey):
        keys = jax.random.split(subkey, 5)
        bumps = jax.random.randint(keys[0], (count,), 0, 2)
        bumps = jnp.where(jnp.arange(count) < CAP, 0, bumps)
        place = jnp.arange(count) + jnp.cumsum(bumps)
        group = place // CAP
        order = jnp.concatenate([jnp.zeros((1,), jnp.int32), 1 + jax.random.permutation(keys[1], N_DEV - 1).astype(jnp.int32)])
        owner = (hotspot + order[group]) % N_DEV
        local = jax.random.randint(keys[2], (count,), 0, TILES_DEV)
        rows = jax.random.randint(keys[3], (count,), 0, TILE_ROWS - BOX + 1)
        cols = jax.random.randint(keys[4], (count,), 0, W - BOX + 1)
        return jnp.stack([owner * TILES_DEV + local, rows, cols], axis=-1).astype(jnp.int32)
    keys = jax.random.split(jax.random.fold_in(key, 5), N_DEV)
    return jax.vmap(one_device)(keys).reshape(PARTICLES, TILTS, 3)


def place_ends(drawn, key, smallest, top_value):
    dims = drawn.shape
    spot = [jax.random.randint(jax.random.fold_in(key, axis), (), 0, dims[axis]) for axis in range(len(dims))]
    drawn = drawn.at[tuple(spot)].set(smallest)
    longest = dims.index(max(dims))
    spot[longest] = (spot[longest] + 1) % dims[longest]
    return drawn.at[tuple(spot)].set(top_value)


def block_scale(stream_key, dims, pieces, low, top_value):
    factor_of, own = 1.0, jax.random.fold_in(stream_key, 6)
    for axis_at, shards_of in pieces:
        steps = jnp.exp(jax.random.uniform(jax.random.fold_in(own, axis_at), (shards_of,), jnp.float32, low / len(pieces), top_value / len(pieces)))
        factor_of = factor_of * jnp.repeat(steps, dims[axis_at] // shards_of).reshape([-1 if axis == axis_at else 1 for axis in range(len(dims))])
    return factor_of


def bell_draw(key, shape, width, limit, pieces=(), held_as=jnp.bfloat16):
    loudness = block_scale(key, shape, pieces, -0.22, 0.18) if pieces else 1.0
    entries = jax.random.normal(key, shape, jnp.float32) * width * loudness
    return jnp.minimum(jnp.maximum(entries, -limit), limit).astype(held_as)


def setup_inputs(seed: int = 0) -> dict:
    key_list = jax.random.split(jax.random.key(seed), 6)
    tiles = bell_draw(key_list[0], (TILES, TILE_ROWS, W), 1.0, 6.0, ((0, 32),))
    footprint = draw_footprint(jax.random.fold_in(key_list[5], 71), 0)
    classes = place_ends(jax.random.randint(key_list[2], (PARTICLES,), 0, CLASSES), jax.random.fold_in(key_list[2], 1), 0, CLASSES - 1).astype(jnp.int32)
    rotations = place_ends(jax.random.randint(key_list[3], (PARTICLES,), 0, ROTS), jax.random.fold_in(key_list[3], 1), 0, ROTS - 1).astype(jnp.int32)
    references = bell_draw(key_list[4], (CLASSES * BOX, ROTS * CYCLES), 1.0, 6.0, ((0, 32),))
    return {"tiles": tiles, "footprint": footprint, "classes": classes, "rotations": rotations, "references": references}


def back_matrix(count):
    center = (BOX - 1) / 2.0
    tilt = jnp.arange(count, dtype=jnp.float32)[:, None, None, None]
    pixel = jnp.arange(BOX, dtype=jnp.float32)[None, :, None, None]
    xpos = jnp.arange(BOX, dtype=jnp.float32)[None, None, :, None]
    zpos = jnp.arange(BOX, dtype=jnp.float32)[None, None, None, :]
    theta = (-60.0 + 120.0 * tilt / (TILTS - 1)) * (jnp.pi / 180.0)
    place = (xpos - center) * jnp.cos(theta) + (zpos - center) * jnp.sin(theta) + center
    weight = jnp.maximum(0.0, 1.0 - jnp.abs(place - pixel))
    weight = jnp.where(tilt < TILTS, weight, 0.0) / TILTS
    return weight.reshape(count * BOX, BOX * BOX).astype(jnp.bfloat16)

def cyl_matrix():
    center = (BOX - 1) / 2.0
    xpos = jnp.arange(BOX, dtype=jnp.float32)[:, None, None, None]
    zpos = jnp.arange(BOX, dtype=jnp.float32)[None, :, None, None]
    angle = jnp.arange(ROTS, dtype=jnp.float32)[None, None, :, None] * (2.0 * jnp.pi / ROTS)
    radius = (jnp.arange(CYCLES, dtype=jnp.float32)[None, None, None, :] + 0.5) * (BOX / (2.0 * CYCLES))
    wx = jnp.maximum(0.0, 1.0 - jnp.abs(xpos - center - radius * jnp.cos(angle)))
    wz = jnp.maximum(0.0, 1.0 - jnp.abs(zpos - center - radius * jnp.sin(angle)))
    return (wx * wz).reshape(BOX * BOX, ROTS * CYCLES).astype(jnp.bfloat16)

def shift_table():
    steps = jnp.arange(ROTS, dtype=jnp.int32)
    want = (steps[None, :, None] - steps[:, None, None]) % ROTS
    return (steps[None, None, :] == want).astype(jnp.float32)

def reference(tiles, footprint, classes, rotations, references):
    back = back_matrix(TILTS)
    sample = cyl_matrix()
    shifts = shift_table()
    ref_three = references.reshape(CLASSES, BOX, ROTS, CYCLES).transpose(0, 2, 1, 3).reshape(CLASSES, ROTS, BOX * CYCLES)
    ref_float = references.astype(jnp.float32).reshape(CLASSES, BOX * ROTS * CYCLES)
    ref_power = lax.optimization_barrier(jnp.mean(ref_float * ref_float, axis=1))
    total = BOX * ROTS * CYCLES
    blocks = PARTICLES // P_DEV
    columns = jnp.arange(ROTS * CYCLES, dtype=jnp.int32)
    labels = jnp.arange(CLASSES, dtype=jnp.int32)

    def cut(item):
        return lax.dynamic_slice(tiles, (item[0], item[1], item[2]), (1, BOX, BOX)).reshape(BOX, BOX)

    def step(carry, inputs):
        foot, label, turn = inputs
        patch = jax.vmap(jax.vmap(cut))(foot)
        pmat = patch.transpose(0, 2, 1, 3).reshape(P_DEV * BOX, TILTS * BOX)
        volume = jnp.dot(pmat, back, preferred_element_type=jnp.float32).astype(jnp.bfloat16)
        cyl = jnp.dot(volume, sample, preferred_element_type=jnp.float32).astype(jnp.bfloat16)
        cyl = cyl.reshape(P_DEV, BOX, ROTS * CYCLES)
        cyl_three = cyl.reshape(P_DEV, BOX, ROTS, CYCLES).transpose(0, 2, 1, 3).reshape(P_DEV, ROTS, BOX * CYCLES)
        corr = jnp.einsum('pfm,cgm->pcfg', cyl_three.astype(jnp.float32), ref_three.astype(jnp.float32))
        raw = jnp.einsum('pcfg,kfg->pck', corr, shifts, precision=lax.Precision.HIGHEST)
        cyl_float = cyl.astype(jnp.float32)
        power = lax.optimization_barrier(jnp.mean(cyl_float.reshape(P_DEV, -1) ** 2, axis=1))
        score = raw / jnp.sqrt(total * (power[:, None, None] + 1e-06) * (ref_power[None, :, None] + 1e-06))
        index = (columns[None, :] + turn[:, None] * CYCLES) % (ROTS * CYCLES)
        turned = jnp.take_along_axis(cyl_float, index[:, None, :], axis=2)
        member = (label[:, None] == labels[None, :]).astype(jnp.float32)
        term = jnp.einsum('pc,pyv->cyv', member, turned, precision=lax.Precision.HIGHEST)
        return (carry + term, score.reshape(P_DEV, CLASSES * ROTS))
    start = jnp.zeros((CLASSES, BOX, ROTS * CYCLES), jnp.float32)
    inputs = (footprint.reshape(blocks, P_DEV, TILTS, 3), classes.reshape(blocks, P_DEV), rotations.reshape(blocks, P_DEV))
    sums, scores = lax.scan(step, start, inputs)
    return (scores.reshape(PARTICLES, CLASSES * ROTS), sums.reshape(CLASSES * BOX, ROTS * CYCLES))
```

```python
import functools

import jax
import jax.numpy as jnp
import ml_dtypes
import numpy as np
from jax import lax
from jax.experimental import pallas as pl
from jax.experimental.pallas import tpu as pltpu
from jax.sharding import PartitionSpec as P

TILTS = 21
BOX = 64
CYCLES = 16
ROTS = 32
CLASSES = 16
WIN = 256


def back_matrix_np(count):
    f32 = np.float32
    center = f32((BOX - 1) / 2.0)
    tilt = np.arange(count, dtype=f32)[:, None, None, None]
    pixel = np.arange(BOX, dtype=f32)[None, :, None, None]
    xpos = np.arange(BOX, dtype=f32)[None, None, :, None]
    zpos = np.arange(BOX, dtype=f32)[None, None, None, :]
    theta = (f32(-60.0) + f32(120.0) * tilt / f32(TILTS - 1)) * f32(np.pi / 180.0)
    place = (xpos - center) * np.cos(theta) + (zpos - center) * np.sin(theta) + center
    weight = np.maximum(f32(0.0), f32(1.0) - np.abs(place - pixel))
    weight = np.where(tilt < TILTS, weight, f32(0.0)) / f32(TILTS)
    weight = weight.astype(f32).astype(ml_dtypes.bfloat16)
    return weight.reshape(count * BOX, BOX * BOX)


def cyl_matrix_np():
    f32 = np.float32
    center = f32((BOX - 1) / 2.0)
    xpos = np.arange(BOX, dtype=f32)[:, None, None, None]
    zpos = np.arange(BOX, dtype=f32)[None, :, None, None]
    angle = np.arange(ROTS, dtype=f32)[None, None, :, None] * f32(2.0 * np.pi / ROTS)
    radius = (np.arange(CYCLES, dtype=f32)[None, None, None, :] + f32(0.5)) * f32(
        BOX / (2.0 * CYCLES)
    )
    wx = np.maximum(f32(0.0), f32(1.0) - np.abs(xpos - center - radius * np.cos(angle)))
    wz = np.maximum(f32(0.0), f32(1.0) - np.abs(zpos - center - radius * np.sin(angle)))
    sample = (wx * wz).astype(f32).astype(ml_dtypes.bfloat16)
    return sample.reshape(BOX * BOX, ROTS * CYCLES)


@functools.lru_cache(maxsize=None)
def folded_matrix(count):
    back = back_matrix_np(count).astype(np.float64)
    sample = cyl_matrix_np().astype(np.float64)
    full = back @ sample
    high = full.astype(ml_dtypes.bfloat16)
    low = (full - high.astype(np.float64)).astype(ml_dtypes.bfloat16)
    return np.asarray(high), np.asarray(low)


def shift_table():
    steps = jnp.arange(ROTS, dtype=jnp.int32)
    want = (steps[None, :, None] - steps[:, None, None]) % ROTS
    return (steps[None, None, :] == want).astype(jnp.float32)


def cut_kernel(req_ref, tiles_ref, out_ref):
    count = out_ref.shape[0]
    width = tiles_ref.shape[2]
    rows = tiles_ref.shape[1]
    row_i = lax.broadcasted_iota(jnp.int32, (BOX, rows), 0)
    row_j = lax.broadcasted_iota(jnp.int32, (BOX, rows), 1)
    col_v = lax.broadcasted_iota(jnp.int32, (WIN, BOX), 0)
    col_u = lax.broadcasted_iota(jnp.int32, (WIN, BOX), 1)

    def body(k, carry):
        t = req_ref[3 * k]
        r = req_ref[3 * k + 1]
        c = req_ref[3 * k + 2]
        c0 = jnp.minimum((c // 128) * 128, width - WIN)
        c0 = pl.multiple_of(c0, 128)
        win = tiles_ref[t, :, pl.ds(c0, WIN)]
        pick_rows = (row_j == row_i + r).astype(jnp.bfloat16)
        part = jnp.dot(pick_rows, win, preferred_element_type=jnp.float32)
        pick_cols = (col_v == col_u + (c - c0)).astype(jnp.bfloat16)
        cut = jnp.dot(part.astype(jnp.bfloat16), pick_cols, preferred_element_type=jnp.float32)
        out_ref[k] = cut.astype(out_ref.dtype)
        return carry

    lax.fori_loop(0, count, body, 0)


def cut_patches(tiles, req):
    count = req.shape[0]
    flat = req.reshape(-1)
    return pl.pallas_call(
        cut_kernel,
        out_shape=jax.ShapeDtypeStruct((count, BOX, BOX), tiles.dtype),
        grid_spec=pltpu.PrefetchScalarGridSpec(
            num_scalar_prefetch=1,
            grid=(1,),
            in_specs=[pl.BlockSpec(tiles.shape, lambda i, q: (0, 0, 0))],
            out_specs=pl.BlockSpec((count, BOX, BOX), lambda i, q: (0, 0, 0)),
        ),
    )(flat, tiles)


def per_device(tiles, footprint, classes, rotations, references):
    ndev = lax.axis_size("dev")
    count = footprint.shape[0]
    asks = count * TILTS
    cap = (2 * asks + ndev - 1) // ndev
    held = tiles.shape[0]
    flat = footprint.reshape(asks, 3)
    owner = flat[:, 0] // held
    local = flat[:, 0] - owner * held
    hits = (owner[:, None] == jnp.arange(ndev, dtype=jnp.int32)[None, :]).astype(jnp.int32)
    slot = jnp.sum((jnp.cumsum(hits, axis=0) - hits) * hits, axis=1)
    wanted = (
        jnp.zeros((ndev, cap, 3), jnp.int32)
        .at[owner, slot]
        .set(jnp.stack([local, flat[:, 1], flat[:, 2]], axis=-1))
    )
    asked = lax.all_to_all(wanted, "dev", split_axis=0, concat_axis=0, tiled=True)
    patches_cut = cut_patches(tiles, asked.reshape(ndev * cap, 3)).reshape(ndev, cap, BOX, BOX)
    arrived = lax.all_to_all(patches_cut, "dev", split_axis=0, concat_axis=0, tiled=True)
    patch = arrived[owner, slot].reshape(count, TILTS, BOX, BOX)
    padded = TILTS + TILTS % 2
    pmat = patch.transpose(0, 2, 1, 3)
    pmat = jnp.pad(pmat, ((0, 0), (0, 0), (0, padded - TILTS), (0, 0))).reshape(
        count * BOX, padded * BOX
    )
    high, low = folded_matrix(padded)
    cyl = jnp.dot(pmat, jnp.asarray(high), preferred_element_type=jnp.float32) + jnp.dot(
        pmat, jnp.asarray(low), preferred_element_type=jnp.float32
    )
    cyl = cyl.astype(jnp.bfloat16).reshape(count, BOX, ROTS * CYCLES)
    whole_refs = lax.all_gather(references, "dev", axis=0, tiled=True)
    ref_three = (
        whole_refs.reshape(CLASSES, BOX, ROTS, CYCLES)
        .transpose(0, 2, 1, 3)
        .reshape(CLASSES, ROTS, BOX * CYCLES)
    )
    ref_float = whole_refs.astype(jnp.float32).reshape(CLASSES, BOX * ROTS * CYCLES)
    ref_power = jnp.mean(ref_float * ref_float, axis=1)
    cyl_three = (
        cyl.reshape(count, BOX, ROTS, CYCLES)
        .transpose(0, 2, 1, 3)
        .reshape(count, ROTS, BOX * CYCLES)
    )
    corr = jnp.einsum("pfm,cgm->pcfg", cyl_three, ref_three, preferred_element_type=jnp.float32)
    raw = jnp.einsum("pcfg,kfg->pck", corr, shift_table(), precision=lax.Precision.HIGHEST)
    cyl_float = cyl.astype(jnp.float32)
    power = jnp.mean(cyl_float.reshape(count, -1) ** 2, axis=1)
    total = BOX * ROTS * CYCLES
    scores = raw / jnp.sqrt(
        total * (power[:, None, None] + 1e-06) * (ref_power[None, :, None] + 1e-06)
    )
    scores = scores.reshape(count, CLASSES * ROTS)
    columns = jnp.arange(ROTS * CYCLES, dtype=jnp.int32)
    index = (columns[None, :] + rotations[:, None] * CYCLES) % (ROTS * CYCLES)
    turned = jnp.take_along_axis(cyl, index[:, None, :], axis=2)
    member = (classes[:, None] == jnp.arange(CLASSES, dtype=jnp.int32)[None, :]).astype(
        jnp.bfloat16
    )
    owned = CLASSES * BOX // ndev
    placed = member[:, :, None, None] * turned[:, None, :, :]
    placed = placed.reshape(count, ndev, owned, ROTS * CYCLES)
    landed = lax.all_to_all(placed, "dev", split_axis=1, concat_axis=0, tiled=True)
    class_sums = jnp.sum(landed.astype(jnp.float32), axis=(0, 1))
    return (scores, class_sums)


def solution(mesh):
    in_specs = (P("dev", None, None), P("dev", None, None), P("dev"), P("dev"), P("dev", None))
    out_specs = (P("dev", None), P("dev", None))
    return jax.shard_map(
        per_device, mesh=mesh, in_specs=in_specs, out_specs=out_specs, check_vma=False
    )
```

```python
import functools

import jax
import jax.numpy as jnp
import ml_dtypes
import numpy as np
from jax import lax
from jax.experimental import pallas as pl
from jax.experimental.pallas import tpu as pltpu
from jax.sharding import PartitionSpec as P

TILTS = 21
BOX = 64
CYCLES = 16
ROTS = 32
CLASSES = 16
WIN = 256


def back_matrix_np(count):
    f32 = np.float32
    center = f32((BOX - 1) / 2.0)
    tilt = np.arange(count, dtype=f32)[:, None, None, None]
    pixel = np.arange(BOX, dtype=f32)[None, :, None, None]
    xpos = np.arange(BOX, dtype=f32)[None, None, :, None]
    zpos = np.arange(BOX, dtype=f32)[None, None, None, :]
    theta = (f32(-60.0) + f32(120.0) * tilt / f32(TILTS - 1)) * f32(np.pi / 180.0)
    place = (xpos - center) * np.cos(theta) + (zpos - center) * np.sin(theta) + center
    weight = np.maximum(f32(0.0), f32(1.0) - np.abs(place - pixel))
    weight = np.where(tilt < TILTS, weight, f32(0.0)) / f32(TILTS)
    weight = weight.astype(f32).astype(ml_dtypes.bfloat16)
    return weight.reshape(count * BOX, BOX * BOX)


def cyl_matrix_np():
    f32 = np.float32
    center = f32((BOX - 1) / 2.0)
    xpos = np.arange(BOX, dtype=f32)[:, None, None, None]
    zpos = np.arange(BOX, dtype=f32)[None, :, None, None]
    angle = np.arange(ROTS, dtype=f32)[None, None, :, None] * f32(2.0 * np.pi / ROTS)
    radius = (np.arange(CYCLES, dtype=f32)[None, None, None, :] + f32(0.5)) * f32(
        BOX / (2.0 * CYCLES)
    )
    wx = np.maximum(f32(0.0), f32(1.0) - np.abs(xpos - center - radius * np.cos(angle)))
    wz = np.maximum(f32(0.0), f32(1.0) - np.abs(zpos - center - radius * np.sin(angle)))
    sample = (wx * wz).astype(f32).astype(ml_dtypes.bfloat16)
    return sample.reshape(BOX * BOX, ROTS * CYCLES)


@functools.lru_cache(maxsize=None)
def touched_points():
    sample = cyl_matrix_np().astype(np.float32)
    used = np.nonzero(np.abs(sample).sum(axis=1))[0]
    size = -(-len(used) // 128) * 128
    xs = np.full((size,), -100.0, np.float32)
    zs = np.full((size,), -100.0, np.float32)
    xs[: len(used)] = used // BOX
    zs[: len(used)] = used % BOX
    return xs, zs


def back_points(count, xs, zs):
    center = (BOX - 1) / 2.0
    tilt = jnp.arange(count, dtype=jnp.float32)[:, None, None]
    pixel = jnp.arange(BOX, dtype=jnp.float32)[None, :, None]
    theta = (-60.0 + 120.0 * tilt / (TILTS - 1)) * (jnp.pi / 180.0)
    place = (xs[None, None, :] - center) * jnp.cos(theta) + (zs[None, None, :] - center) * jnp.sin(
        theta
    ) + center
    weight = jnp.maximum(0.0, 1.0 - jnp.abs(place - pixel))
    weight = jnp.where(tilt < TILTS, weight, 0.0) / TILTS
    return weight.reshape(count * BOX, xs.shape[0]).astype(jnp.bfloat16)


def sample_points(xs, zs):
    center = (BOX - 1) / 2.0
    angle = jnp.arange(ROTS, dtype=jnp.float32)[None, :, None] * (2.0 * jnp.pi / ROTS)
    radius = (jnp.arange(CYCLES, dtype=jnp.float32)[None, None, :] + 0.5) * (BOX / (2.0 * CYCLES))
    wx = jnp.maximum(0.0, 1.0 - jnp.abs(xs[:, None, None] - center - radius * jnp.cos(angle)))
    wz = jnp.maximum(0.0, 1.0 - jnp.abs(zs[:, None, None] - center - radius * jnp.sin(angle)))
    return (wx * wz).reshape(xs.shape[0], ROTS * CYCLES).astype(jnp.bfloat16)


def shift_table():
    steps = jnp.arange(ROTS, dtype=jnp.int32)
    want = (steps[None, :, None] - steps[:, None, None]) % ROTS
    return (steps[None, None, :] == want).astype(jnp.float32)


def cut_kernel(req_ref, tiles_ref, out_ref):
    count = out_ref.shape[0]
    width = tiles_ref.shape[2]
    rows = tiles_ref.shape[1]
    row_i = lax.broadcasted_iota(jnp.int32, (BOX, rows), 0)
    row_j = lax.broadcasted_iota(jnp.int32, (BOX, rows), 1)
    col_v = lax.broadcasted_iota(jnp.int32, (WIN, BOX), 0)
    col_u = lax.broadcasted_iota(jnp.int32, (WIN, BOX), 1)

    def body(k, carry):
        t = req_ref[3 * k]
        r = req_ref[3 * k + 1]
        c = req_ref[3 * k + 2]
        c0 = jnp.minimum((c // 128) * 128, width - WIN)
        c0 = pl.multiple_of(c0, 128)
        win = tiles_ref[t, :, pl.ds(c0, WIN)]
        pick_rows = (row_j == row_i + r).astype(jnp.bfloat16)
        part = jnp.dot(pick_rows, win, preferred_element_type=jnp.float32)
        pick_cols = (col_v == col_u + (c - c0)).astype(jnp.bfloat16)
        cut = jnp.dot(part.astype(jnp.bfloat16), pick_cols, preferred_element_type=jnp.float32)
        out_ref[k] = cut.astype(out_ref.dtype)
        return carry

    lax.fori_loop(0, count, body, 0)


def cut_patches(tiles, req):
    count = req.shape[0]
    flat = req.reshape(-1)
    return pl.pallas_call(
        cut_kernel,
        out_shape=jax.ShapeDtypeStruct((count, BOX, BOX), tiles.dtype),
        grid_spec=pltpu.PrefetchScalarGridSpec(
            num_scalar_prefetch=1,
            grid=(1,),
            in_specs=[pl.BlockSpec(tiles.shape, lambda i, q: (0, 0, 0))],
            out_specs=pl.BlockSpec((count, BOX, BOX), lambda i, q: (0, 0, 0)),
        ),
        cost_estimate=pl.CostEstimate(
            flops=count * 2 * BOX * WIN * (tiles.shape[1] + BOX),
            transcendentals=0,
            bytes_accessed=tiles.size * 2 + count * BOX * BOX * 2,
        ),
    )(flat, tiles)


def per_device(tiles, footprint, classes, rotations, references):
    ndev = lax.axis_size("dev")
    count = footprint.shape[0]
    asks = count * TILTS
    cap = (2 * asks + ndev - 1) // ndev
    held = tiles.shape[0]
    flat = footprint.reshape(asks, 3)
    owner = flat[:, 0] // held
    local = flat[:, 0] - owner * held
    hits = (owner[:, None] == jnp.arange(ndev, dtype=jnp.int32)[None, :]).astype(jnp.int32)
    slot = jnp.sum((jnp.cumsum(hits, axis=0) - hits) * hits, axis=1)
    wanted = (
        jnp.zeros((ndev, cap, 3), jnp.int32)
        .at[owner, slot]
        .set(jnp.stack([local, flat[:, 1], flat[:, 2]], axis=-1))
    )
    asked = lax.all_to_all(wanted, "dev", split_axis=0, concat_axis=0, tiled=True)
    patches_cut = cut_patches(tiles, asked.reshape(ndev * cap, 3)).reshape(ndev, cap, BOX, BOX)
    arrived = lax.all_to_all(patches_cut, "dev", split_axis=0, concat_axis=0, tiled=True)
    patch = arrived[owner, slot].reshape(count, TILTS, BOX, BOX)
    padded = TILTS + TILTS % 2
    pmat = patch.transpose(0, 2, 1, 3)
    pmat = jnp.pad(pmat, ((0, 0), (0, 0), (0, padded - TILTS), (0, 0))).reshape(
        count * BOX, padded * BOX
    )
    xs_np, zs_np = touched_points()
    xs, zs = jnp.asarray(xs_np), jnp.asarray(zs_np)
    volume = jnp.dot(pmat, back_points(padded, xs, zs), preferred_element_type=jnp.float32)
    volume = volume.astype(jnp.bfloat16)
    cyl = jnp.dot(volume, sample_points(xs, zs), preferred_element_type=jnp.float32)
    cyl = cyl.astype(jnp.bfloat16).reshape(count, BOX, ROTS * CYCLES)
    owned = references.shape[0]
    local_t = references.reshape(owned, ROTS, CYCLES).transpose(1, 0, 2).reshape(ROTS, owned * CYCLES)
    gathered = lax.all_gather(local_t, "dev", axis=1, tiled=True).reshape(
        ROTS, CLASSES, BOX * CYCLES
    )
    ref_float = gathered.astype(jnp.float32)
    ref_power = jnp.mean(ref_float * ref_float, axis=(0, 2))
    cyl_three = (
        cyl.reshape(count, BOX, ROTS, CYCLES)
        .transpose(0, 2, 1, 3)
        .reshape(count, ROTS, BOX * CYCLES)
    )
    corr = jnp.einsum("pfm,gcm->pfgc", cyl_three, gathered, preferred_element_type=jnp.float32)
    raw = jnp.einsum("pfgc,kfg->pck", corr, shift_table(), precision=lax.Precision.HIGHEST)
    cyl_float = cyl.astype(jnp.float32)
    power = jnp.mean(cyl_float.reshape(count, -1) ** 2, axis=1)
    total = BOX * ROTS * CYCLES
    scores = raw / jnp.sqrt(
        total * (power[:, None, None] + 1e-06) * (ref_power[None, :, None] + 1e-06)
    )
    scores = scores.reshape(count, CLASSES * ROTS)
    columns = jnp.arange(ROTS * CYCLES, dtype=jnp.int32)
    index = (columns[None, :] + rotations[:, None] * CYCLES) % (ROTS * CYCLES)
    turned = jnp.take_along_axis(cyl, index[:, None, :], axis=2)
    member = (classes[:, None] == jnp.arange(CLASSES, dtype=jnp.int32)[None, :]).astype(
        jnp.bfloat16
    )
    placed = member[:, :, None, None] * turned[:, None, :, :]
    placed = placed.reshape(count, ndev, owned, ROTS * CYCLES)
    landed = lax.all_to_all(placed, "dev", split_axis=1, concat_axis=0, tiled=True)
    class_sums = jnp.sum(landed.astype(jnp.float32), axis=(0, 1))
    return (scores, class_sums)


def solution(mesh):
    in_specs = (P("dev", None, None), P("dev", None, None), P("dev"), P("dev"), P("dev", None))
    out_specs = (P("dev", None), P("dev", None))
    return jax.shard_map(
        per_device, mesh=mesh, in_specs=in_specs, out_specs=out_specs, check_vma=False
    )
```

```python
import functools

import jax
import jax.numpy as jnp
import ml_dtypes
import numpy as np
from jax import lax
from jax.experimental import pallas as pl
from jax.experimental.pallas import tpu as pltpu
from jax.sharding import PartitionSpec as P

TILTS = 21
BOX = 64
CYCLES = 16
ROTS = 32
CLASSES = 16
WIN = 256


def back_matrix_np(count):
    f32 = np.float32
    center = f32((BOX - 1) / 2.0)
    tilt = np.arange(count, dtype=f32)[:, None, None, None]
    pixel = np.arange(BOX, dtype=f32)[None, :, None, None]
    xpos = np.arange(BOX, dtype=f32)[None, None, :, None]
    zpos = np.arange(BOX, dtype=f32)[None, None, None, :]
    theta = (f32(-60.0) + f32(120.0) * tilt / f32(TILTS - 1)) * f32(np.pi / 180.0)
    place = (xpos - center) * np.cos(theta) + (zpos - center) * np.sin(theta) + center
    weight = np.maximum(f32(0.0), f32(1.0) - np.abs(place - pixel))
    weight = np.where(tilt < TILTS, weight, f32(0.0)) / f32(TILTS)
    weight = weight.astype(f32).astype(ml_dtypes.bfloat16)
    return weight.reshape(count * BOX, BOX * BOX)


def cyl_matrix_np():
    f32 = np.float32
    center = f32((BOX - 1) / 2.0)
    xpos = np.arange(BOX, dtype=f32)[:, None, None, None]
    zpos = np.arange(BOX, dtype=f32)[None, :, None, None]
    angle = np.arange(ROTS, dtype=f32)[None, None, :, None] * f32(2.0 * np.pi / ROTS)
    radius = (np.arange(CYCLES, dtype=f32)[None, None, None, :] + f32(0.5)) * f32(
        BOX / (2.0 * CYCLES)
    )
    wx = np.maximum(f32(0.0), f32(1.0) - np.abs(xpos - center - radius * np.cos(angle)))
    wz = np.maximum(f32(0.0), f32(1.0) - np.abs(zpos - center - radius * np.sin(angle)))
    sample = (wx * wz).astype(f32).astype(ml_dtypes.bfloat16)
    return sample.reshape(BOX * BOX, ROTS * CYCLES)


@functools.lru_cache(maxsize=None)
def touched_points():
    sample = cyl_matrix_np().astype(np.float32)
    used = np.nonzero(np.abs(sample).sum(axis=1))[0]
    size = -(-len(used) // 128) * 128
    xs = np.full((size,), -100.0, np.float32)
    zs = np.full((size,), -100.0, np.float32)
    xs[: len(used)] = used // BOX
    zs[: len(used)] = used % BOX
    return xs, zs


def back_points(count, xs, zs):
    center = (BOX - 1) / 2.0
    tilt = jnp.arange(count, dtype=jnp.float32)[:, None, None]
    pixel = jnp.arange(BOX, dtype=jnp.float32)[None, :, None]
    theta = (-60.0 + 120.0 * tilt / (TILTS - 1)) * (jnp.pi / 180.0)
    place = (xs[None, None, :] - center) * jnp.cos(theta) + (zs[None, None, :] - center) * jnp.sin(
        theta
    ) + center
    weight = jnp.maximum(0.0, 1.0 - jnp.abs(place - pixel))
    weight = jnp.where(tilt < TILTS, weight, 0.0) / TILTS
    return weight.reshape(count * BOX, xs.shape[0]).astype(jnp.bfloat16)


def sample_points(xs, zs):
    center = (BOX - 1) / 2.0
    angle = jnp.arange(ROTS, dtype=jnp.float32)[None, :, None] * (2.0 * jnp.pi / ROTS)
    radius = (jnp.arange(CYCLES, dtype=jnp.float32)[None, None, :] + 0.5) * (BOX / (2.0 * CYCLES))
    wx = jnp.maximum(0.0, 1.0 - jnp.abs(xs[:, None, None] - center - radius * jnp.cos(angle)))
    wz = jnp.maximum(0.0, 1.0 - jnp.abs(zs[:, None, None] - center - radius * jnp.sin(angle)))
    return (wx * wz).reshape(xs.shape[0], ROTS * CYCLES).astype(jnp.bfloat16)


def shift_table():
    steps = jnp.arange(ROTS, dtype=jnp.int32)
    want = (steps[None, :, None] - steps[:, None, None]) % ROTS
    return (steps[None, None, :] == want).astype(jnp.float32)


def cut_kernel(req_ref, tiles_ref, out_ref):
    count = out_ref.shape[0]
    width = tiles_ref.shape[2]
    rows = tiles_ref.shape[1]
    span = BOX + 16

    def body(k, carry):
        t = req_ref[3 * k]
        r = req_ref[3 * k + 1]
        c = req_ref[3 * k + 2]
        r0 = pl.multiple_of(jnp.minimum((r // 16) * 16, rows - span), 16)
        c0 = pl.multiple_of(jnp.minimum((c // 128) * 128, width - WIN), 128)
        win = tiles_ref[t, pl.ds(r0, span), pl.ds(c0, WIN)].astype(jnp.float32)
        win = pltpu.roll(win, (span - (r - r0)) % span, 0)
        win = pltpu.roll(win, (WIN - (c - c0)) % WIN, 1)
        out_ref[k] = win[:BOX, :BOX].astype(out_ref.dtype)
        return carry

    lax.fori_loop(0, count, body, 0)


def cut_patches(tiles, req):
    count = req.shape[0]
    flat = req.reshape(-1)
    return pl.pallas_call(
        cut_kernel,
        out_shape=jax.ShapeDtypeStruct((count, BOX, BOX), tiles.dtype),
        grid_spec=pltpu.PrefetchScalarGridSpec(
            num_scalar_prefetch=1,
            grid=(1,),
            in_specs=[pl.BlockSpec(tiles.shape, lambda i, q: (0, 0, 0))],
            out_specs=pl.BlockSpec((count, BOX, BOX), lambda i, q: (0, 0, 0)),
        ),
        cost_estimate=pl.CostEstimate(
            flops=count * BOX * WIN * 64,
            transcendentals=0,
            bytes_accessed=tiles.size * 2 + count * BOX * BOX * 2,
        ),
    )(flat, tiles)


def per_device(tiles, footprint, classes, rotations, references):
    ndev = lax.axis_size("dev")
    count = footprint.shape[0]
    asks = count * TILTS
    cap = (2 * asks + ndev - 1) // ndev
    held = tiles.shape[0]
    flat = footprint.reshape(asks, 3)
    owner = flat[:, 0] // held
    local = flat[:, 0] - owner * held
    hits = (owner[:, None] == jnp.arange(ndev, dtype=jnp.int32)[None, :]).astype(jnp.int32)
    slot = jnp.sum((jnp.cumsum(hits, axis=0) - hits) * hits, axis=1)
    values = jnp.stack([local, flat[:, 1], flat[:, 2]], axis=-1)
    spot = (owner[None, None, :] == jnp.arange(ndev, dtype=jnp.int32)[:, None, None]) & (
        slot[None, None, :] == jnp.arange(cap, dtype=jnp.int32)[None, :, None]
    )
    wanted = jnp.sum(jnp.where(spot[..., None], values[None, None], 0), axis=2)
    asked = lax.all_to_all(wanted, "dev", split_axis=0, concat_axis=0, tiled=True)
    patches_cut = cut_patches(tiles, asked.reshape(ndev * cap, 3)).reshape(ndev, cap * BOX, BOX)
    arrived = lax.all_to_all(patches_cut, "dev", split_axis=0, concat_axis=0, tiled=True)
    arrived = arrived.reshape(ndev, cap, BOX, BOX)
    patch = arrived[owner, slot].reshape(count, TILTS, BOX, BOX)
    padded = TILTS + TILTS % 2
    pmat = patch.transpose(0, 2, 1, 3)
    pmat = jnp.pad(pmat, ((0, 0), (0, 0), (0, padded - TILTS), (0, 0))).reshape(
        count * BOX, padded * BOX
    )
    xs_np, zs_np = touched_points()
    xs, zs = jnp.asarray(xs_np), jnp.asarray(zs_np)
    volume = jnp.dot(pmat, back_points(padded, xs, zs), preferred_element_type=jnp.float32)
    volume = volume.astype(jnp.bfloat16)
    cyl = jnp.dot(volume, sample_points(xs, zs), preferred_element_type=jnp.float32)
    cyl = cyl.astype(jnp.bfloat16).reshape(count, BOX, ROTS * CYCLES)
    owned = references.shape[0]
    local_t = references.reshape(owned, ROTS, CYCLES).transpose(1, 0, 2).reshape(ROTS, owned * CYCLES)
    gathered = lax.all_gather(local_t, "dev", axis=1, tiled=True).reshape(
        ROTS, CLASSES, BOX * CYCLES
    )
    ref_float = gathered.astype(jnp.float32)
    ref_power = jnp.mean(ref_float * ref_float, axis=(0, 2))
    cyl_three = (
        cyl.reshape(count, BOX, ROTS, CYCLES)
        .transpose(0, 2, 1, 3)
        .reshape(count, ROTS, BOX * CYCLES)
    )
    corr = jnp.einsum("pfm,gcm->pfgc", cyl_three, gathered, preferred_element_type=jnp.float32)
    raw = jnp.einsum("pfgc,kfg->pck", corr, shift_table(), precision=lax.Precision.HIGHEST)
    cyl_float = cyl.astype(jnp.float32)
    power = jnp.mean(cyl_float.reshape(count, -1) ** 2, axis=1)
    total = BOX * ROTS * CYCLES
    scores = raw / jnp.sqrt(
        total * (power[:, None, None] + 1e-06) * (ref_power[None, :, None] + 1e-06)
    )
    scores = scores.reshape(count, CLASSES * ROTS)
    columns = jnp.arange(ROTS * CYCLES, dtype=jnp.int32)
    index = (columns[None, :] + rotations[:, None] * CYCLES) % (ROTS * CYCLES)
    turned = jnp.take_along_axis(cyl, index[:, None, :], axis=2)
    member = (classes[:, None] == jnp.arange(CLASSES, dtype=jnp.int32)[None, :]).astype(
        jnp.bfloat16
    )
    placed = member[:, :, None, None] * turned[:, None, :, :]
    placed = placed.reshape(count, ndev, owned, ROTS * CYCLES)
    landed = lax.all_to_all(placed, "dev", split_axis=1, concat_axis=0, tiled=True)
    class_sums = jnp.sum(landed.astype(jnp.float32), axis=(0, 1))
    return (scores, class_sums)


def solution(mesh):
    in_specs = (P("dev", None, None), P("dev", None, None), P("dev"), P("dev"), P("dev", None))
    out_specs = (P("dev", None), P("dev", None))
    return jax.shard_map(
        per_device, mesh=mesh, in_specs=in_specs, out_specs=out_specs, check_vma=False
    )
```

```python
import functools

import jax
import jax.numpy as jnp
import ml_dtypes
import numpy as np
from jax import lax
from jax.experimental import pallas as pl
from jax.experimental.pallas import tpu as pltpu
from jax.sharding import PartitionSpec as P

TILTS = 21
BOX = 64
CYCLES = 16
ROTS = 32
CLASSES = 16
WIN = 256


def back_matrix_np(count):
    f32 = np.float32
    center = f32((BOX - 1) / 2.0)
    tilt = np.arange(count, dtype=f32)[:, None, None, None]
    pixel = np.arange(BOX, dtype=f32)[None, :, None, None]
    xpos = np.arange(BOX, dtype=f32)[None, None, :, None]
    zpos = np.arange(BOX, dtype=f32)[None, None, None, :]
    theta = (f32(-60.0) + f32(120.0) * tilt / f32(TILTS - 1)) * f32(np.pi / 180.0)
    place = (xpos - center) * np.cos(theta) + (zpos - center) * np.sin(theta) + center
    weight = np.maximum(f32(0.0), f32(1.0) - np.abs(place - pixel))
    weight = np.where(tilt < TILTS, weight, f32(0.0)) / f32(TILTS)
    weight = weight.astype(f32).astype(ml_dtypes.bfloat16)
    return weight.reshape(count * BOX, BOX * BOX)


def cyl_matrix_np():
    f32 = np.float32
    center = f32((BOX - 1) / 2.0)
    xpos = np.arange(BOX, dtype=f32)[:, None, None, None]
    zpos = np.arange(BOX, dtype=f32)[None, :, None, None]
    angle = np.arange(ROTS, dtype=f32)[None, None, :, None] * f32(2.0 * np.pi / ROTS)
    radius = (np.arange(CYCLES, dtype=f32)[None, None, None, :] + f32(0.5)) * f32(
        BOX / (2.0 * CYCLES)
    )
    wx = np.maximum(f32(0.0), f32(1.0) - np.abs(xpos - center - radius * np.cos(angle)))
    wz = np.maximum(f32(0.0), f32(1.0) - np.abs(zpos - center - radius * np.sin(angle)))
    sample = (wx * wz).astype(f32).astype(ml_dtypes.bfloat16)
    return sample.reshape(BOX * BOX, ROTS * CYCLES)


@functools.lru_cache(maxsize=None)
def touched_points():
    sample = cyl_matrix_np().astype(np.float32)
    used = np.nonzero(np.abs(sample).sum(axis=1))[0]
    size = -(-len(used) // 128) * 128
    xs = np.full((size,), -100.0, np.float32)
    zs = np.full((size,), -100.0, np.float32)
    xs[: len(used)] = used // BOX
    zs[: len(used)] = used % BOX
    return xs, zs


def back_points(count, xs, zs):
    center = (BOX - 1) / 2.0
    tilt = jnp.arange(count, dtype=jnp.float32)[:, None, None]
    pixel = jnp.arange(BOX, dtype=jnp.float32)[None, :, None]
    theta = (-60.0 + 120.0 * tilt / (TILTS - 1)) * (jnp.pi / 180.0)
    place = (xs[None, None, :] - center) * jnp.cos(theta) + (zs[None, None, :] - center) * jnp.sin(
        theta
    ) + center
    weight = jnp.maximum(0.0, 1.0 - jnp.abs(place - pixel))
    weight = jnp.where(tilt < TILTS, weight, 0.0) / TILTS
    return weight.reshape(count * BOX, xs.shape[0]).astype(jnp.bfloat16)


def sample_points(xs, zs):
    center = (BOX - 1) / 2.0
    angle = jnp.arange(ROTS, dtype=jnp.float32)[None, :, None] * (2.0 * jnp.pi / ROTS)
    radius = (jnp.arange(CYCLES, dtype=jnp.float32)[None, None, :] + 0.5) * (BOX / (2.0 * CYCLES))
    wx = jnp.maximum(0.0, 1.0 - jnp.abs(xs[:, None, None] - center - radius * jnp.cos(angle)))
    wz = jnp.maximum(0.0, 1.0 - jnp.abs(zs[:, None, None] - center - radius * jnp.sin(angle)))
    return (wx * wz).reshape(xs.shape[0], ROTS * CYCLES).astype(jnp.bfloat16)


def shift_table():
    steps = jnp.arange(ROTS, dtype=jnp.int32)
    want = (steps[None, :, None] - steps[:, None, None]) % ROTS
    return (steps[None, None, :] == want).astype(jnp.float32)


def cut_kernel(req_ref, tiles_ref, out_ref):
    count = out_ref.shape[0]
    width = tiles_ref.shape[2]
    rows = tiles_ref.shape[1]
    span = BOX + 16

    def body(k, carry):
        t = req_ref[3 * k]
        r = req_ref[3 * k + 1]
        c = req_ref[3 * k + 2]
        r0 = pl.multiple_of(jnp.minimum((r // 16) * 16, rows - span), 16)
        c0 = pl.multiple_of(jnp.minimum((c // 128) * 128, width - WIN), 128)
        win = tiles_ref[t, pl.ds(r0, span), pl.ds(c0, WIN)].astype(jnp.float32)
        win = pltpu.roll(win, (span - (r - r0)) % span, 0)
        win = pltpu.roll(win, (WIN - (c - c0)) % WIN, 1)
        out_ref[k] = win[:BOX, :BOX].astype(out_ref.dtype)
        return carry

    lax.fori_loop(0, count, body, 0)


def cut_patches(tiles, req):
    count = req.shape[0]
    flat = req.reshape(-1)
    return pl.pallas_call(
        cut_kernel,
        out_shape=jax.ShapeDtypeStruct((count, BOX, BOX), tiles.dtype),
        grid_spec=pltpu.PrefetchScalarGridSpec(
            num_scalar_prefetch=1,
            grid=(1,),
            in_specs=[pl.BlockSpec(tiles.shape, lambda i, q: (0, 0, 0))],
            out_specs=pl.BlockSpec((count, BOX, BOX), lambda i, q: (0, 0, 0)),
        ),
        cost_estimate=pl.CostEstimate(
            flops=count * BOX * WIN * 64,
            transcendentals=0,
            bytes_accessed=tiles.size * 2 + count * BOX * BOX * 2,
        ),
    )(flat, tiles)


def per_device(tiles, footprint, classes, rotations, references):
    ndev = lax.axis_size("dev")
    count = footprint.shape[0]
    asks = count * TILTS
    cap = (2 * asks + ndev - 1) // ndev
    held = tiles.shape[0]
    flat = footprint.reshape(asks, 3)
    owner = flat[:, 0] // held
    local = flat[:, 0] - owner * held
    hits = (owner[:, None] == jnp.arange(ndev, dtype=jnp.int32)[None, :]).astype(jnp.int32)
    slot = jnp.sum((jnp.cumsum(hits, axis=0) - hits) * hits, axis=1)
    values = jnp.stack([local, flat[:, 1], flat[:, 2]], axis=-1)
    spot = (owner[None, None, :] == jnp.arange(ndev, dtype=jnp.int32)[:, None, None]) & (
        slot[None, None, :] == jnp.arange(cap, dtype=jnp.int32)[None, :, None]
    )
    wanted = jnp.sum(jnp.where(spot[..., None], values[None, None], 0), axis=2)
    asked = lax.all_to_all(wanted, "dev", split_axis=0, concat_axis=0, tiled=True)
    patches_cut = cut_patches(tiles, asked.reshape(ndev * cap, 3)).reshape(ndev, cap * BOX, BOX)
    arrived = lax.all_to_all(patches_cut, "dev", split_axis=0, concat_axis=0, tiled=True)
    arrived = arrived.reshape(ndev, cap, BOX, BOX)
    patch = arrived[owner, slot].reshape(count, TILTS, BOX, BOX)
    padded = TILTS + TILTS % 2
    pmat = patch.transpose(0, 2, 1, 3)
    pmat = jnp.pad(pmat, ((0, 0), (0, 0), (0, padded - TILTS), (0, 0))).reshape(
        count * BOX, padded * BOX
    )
    xs_np, zs_np = touched_points()
    xs, zs = jnp.asarray(xs_np), jnp.asarray(zs_np)
    volume = jnp.dot(pmat, back_points(padded, xs, zs), preferred_element_type=jnp.float32)
    volume = volume.astype(jnp.bfloat16)
    cyl = jnp.dot(volume, sample_points(xs, zs), preferred_element_type=jnp.float32)
    cyl = cyl.astype(jnp.bfloat16).reshape(count, BOX, ROTS * CYCLES)
    owned = references.shape[0]
    parts = BOX // owned
    local_t = references.reshape(owned, ROTS, CYCLES).transpose(1, 0, 2).reshape(ROTS, owned * CYCLES)
    gathered = lax.all_gather(local_t[None], "dev", axis=0, tiled=True)
    gathered = gathered.reshape(CLASSES, parts, ROTS, owned * CYCLES)
    ref_float = gathered.astype(jnp.float32)
    ref_power = jnp.mean(ref_float * ref_float, axis=(1, 2, 3))
    cyl_three = (
        cyl.reshape(count, BOX, ROTS, CYCLES)
        .transpose(0, 2, 1, 3)
        .reshape(count, ROTS, parts, owned * CYCLES)
    )
    corr = sum(
        jnp.einsum(
            "pfm,cgm->pfgc", cyl_three[:, :, q], gathered[:, q], preferred_element_type=jnp.float32
        )
        for q in range(parts)
    )
    raw = jnp.einsum("pfgc,kfg->pck", corr, shift_table(), precision=lax.Precision.HIGHEST)
    cyl_float = cyl.astype(jnp.float32)
    power = jnp.mean(cyl_float.reshape(count, -1) ** 2, axis=1)
    total = BOX * ROTS * CYCLES
    scores = raw / jnp.sqrt(
        total * (power[:, None, None] + 1e-06) * (ref_power[None, :, None] + 1e-06)
    )
    scores = scores.reshape(count, CLASSES * ROTS)
    columns = jnp.arange(ROTS * CYCLES, dtype=jnp.int32)
    index = (columns[None, :] + rotations[:, None] * CYCLES) % (ROTS * CYCLES)
    turned = jnp.take_along_axis(cyl, index[:, None, :], axis=2)
    member = (classes[:, None] == jnp.arange(CLASSES, dtype=jnp.int32)[None, :]).astype(
        jnp.bfloat16
    )
    placed = member[:, :, None, None] * turned[:, None, :, :]
    placed = placed.reshape(count, ndev, owned, ROTS * CYCLES)
    landed = lax.all_to_all(placed, "dev", split_axis=1, concat_axis=0, tiled=True)
    class_sums = jnp.sum(landed.astype(jnp.float32), axis=(0, 1))
    return (scores, class_sums)


def solution(mesh):
    in_specs = (P("dev", None, None), P("dev", None, None), P("dev"), P("dev"), P("dev", None))
    out_specs = (P("dev", None), P("dev", None))
    return jax.shard_map(
        per_device, mesh=mesh, in_specs=in_specs, out_specs=out_specs, check_vma=False
    )
```

```python
import functools

import jax
import jax.numpy as jnp
import ml_dtypes
import numpy as np
from jax import lax
from jax.experimental import pallas as pl
from jax.experimental.pallas import tpu as pltpu
from jax.sharding import PartitionSpec as P

TILTS = 21
BOX = 64
CYCLES = 16
ROTS = 32
CLASSES = 16
WIN = 256


def back_matrix_np(count):
    f32 = np.float32
    center = f32((BOX - 1) / 2.0)
    tilt = np.arange(count, dtype=f32)[:, None, None, None]
    pixel = np.arange(BOX, dtype=f32)[None, :, None, None]
    xpos = np.arange(BOX, dtype=f32)[None, None, :, None]
    zpos = np.arange(BOX, dtype=f32)[None, None, None, :]
    theta = (f32(-60.0) + f32(120.0) * tilt / f32(TILTS - 1)) * f32(np.pi / 180.0)
    place = (xpos - center) * np.cos(theta) + (zpos - center) * np.sin(theta) + center
    weight = np.maximum(f32(0.0), f32(1.0) - np.abs(place - pixel))
    weight = np.where(tilt < TILTS, weight, f32(0.0)) / f32(TILTS)
    weight = weight.astype(f32).astype(ml_dtypes.bfloat16)
    return weight.reshape(count * BOX, BOX * BOX)


def cyl_matrix_np():
    f32 = np.float32
    center = f32((BOX - 1) / 2.0)
    xpos = np.arange(BOX, dtype=f32)[:, None, None, None]
    zpos = np.arange(BOX, dtype=f32)[None, :, None, None]
    angle = np.arange(ROTS, dtype=f32)[None, None, :, None] * f32(2.0 * np.pi / ROTS)
    radius = (np.arange(CYCLES, dtype=f32)[None, None, None, :] + f32(0.5)) * f32(
        BOX / (2.0 * CYCLES)
    )
    wx = np.maximum(f32(0.0), f32(1.0) - np.abs(xpos - center - radius * np.cos(angle)))
    wz = np.maximum(f32(0.0), f32(1.0) - np.abs(zpos - center - radius * np.sin(angle)))
    sample = (wx * wz).astype(f32).astype(ml_dtypes.bfloat16)
    return sample.reshape(BOX * BOX, ROTS * CYCLES)


@functools.lru_cache(maxsize=None)
def touched_points():
    sample = cyl_matrix_np().astype(np.float32)
    used = np.nonzero(np.abs(sample).sum(axis=1))[0]
    size = -(-len(used) // 128) * 128
    xs = np.full((size,), -100.0, np.float32)
    zs = np.full((size,), -100.0, np.float32)
    xs[: len(used)] = used // BOX
    zs[: len(used)] = used % BOX
    return xs, zs


def back_points(count, xs, zs):
    center = (BOX - 1) / 2.0
    tilt = jnp.arange(count, dtype=jnp.float32)[:, None, None]
    pixel = jnp.arange(BOX, dtype=jnp.float32)[None, :, None]
    theta = (-60.0 + 120.0 * tilt / (TILTS - 1)) * (jnp.pi / 180.0)
    place = (xs[None, None, :] - center) * jnp.cos(theta) + (zs[None, None, :] - center) * jnp.sin(
        theta
    ) + center
    weight = jnp.maximum(0.0, 1.0 - jnp.abs(place - pixel))
    weight = jnp.where(tilt < TILTS, weight, 0.0) / TILTS
    return weight.reshape(count * BOX, xs.shape[0]).astype(jnp.bfloat16)


def sample_points(xs, zs):
    center = (BOX - 1) / 2.0
    angle = jnp.arange(ROTS, dtype=jnp.float32)[None, :, None] * (2.0 * jnp.pi / ROTS)
    radius = (jnp.arange(CYCLES, dtype=jnp.float32)[None, None, :] + 0.5) * (BOX / (2.0 * CYCLES))
    wx = jnp.maximum(0.0, 1.0 - jnp.abs(xs[:, None, None] - center - radius * jnp.cos(angle)))
    wz = jnp.maximum(0.0, 1.0 - jnp.abs(zs[:, None, None] - center - radius * jnp.sin(angle)))
    return (wx * wz).reshape(xs.shape[0], ROTS * CYCLES).astype(jnp.bfloat16)


def shift_table():
    steps = jnp.arange(ROTS, dtype=jnp.int32)
    want = (steps[None, :, None] - steps[:, None, None]) % ROTS
    return (steps[None, None, :] == want).astype(jnp.float32)


def cut_kernel(req_ref, tiles_ref, out_ref):
    count = out_ref.shape[0]
    width = tiles_ref.shape[2]
    rows = tiles_ref.shape[1]
    span = BOX + 16

    def body(k, carry):
        t = req_ref[3 * k]
        r = req_ref[3 * k + 1]
        c = req_ref[3 * k + 2]
        r0 = pl.multiple_of(jnp.minimum((r // 16) * 16, rows - span), 16)
        c0 = pl.multiple_of(jnp.minimum((c // 128) * 128, width - WIN), 128)
        win = tiles_ref[t, pl.ds(r0, span), pl.ds(c0, WIN)].astype(jnp.float32)
        win = pltpu.roll(win, (WIN - (c - c0)) % WIN, 1)[:, :128]
        win = pltpu.roll(win, (span - (r - r0)) % span, 0)
        out_ref[k] = win[:BOX, :BOX].astype(out_ref.dtype)
        return carry

    lax.fori_loop(0, count, body, 0, unroll=2)


def cut_patches(tiles, req):
    count = req.shape[0]
    flat = req.reshape(-1)
    return pl.pallas_call(
        cut_kernel,
        out_shape=jax.ShapeDtypeStruct((count, BOX, BOX), tiles.dtype),
        grid_spec=pltpu.PrefetchScalarGridSpec(
            num_scalar_prefetch=1,
            grid=(1,),
            in_specs=[pl.BlockSpec(tiles.shape, lambda i, q: (0, 0, 0))],
            out_specs=pl.BlockSpec((count, BOX, BOX), lambda i, q: (0, 0, 0)),
        ),
        cost_estimate=pl.CostEstimate(
            flops=count * BOX * WIN * 64,
            transcendentals=0,
            bytes_accessed=tiles.size * 2 + count * BOX * BOX * 2,
        ),
    )(flat, tiles)


def per_device(tiles, footprint, classes, rotations, references):
    ndev = lax.axis_size("dev")
    count = footprint.shape[0]
    asks = count * TILTS
    cap = (2 * asks + ndev - 1) // ndev
    held = tiles.shape[0]
    flat = footprint.reshape(asks, 3)
    owner = flat[:, 0] // held
    local = flat[:, 0] - owner * held
    hits = (owner[:, None] == jnp.arange(ndev, dtype=jnp.int32)[None, :]).astype(jnp.int32)
    slot = jnp.sum((jnp.cumsum(hits, axis=0) - hits) * hits, axis=1)
    values = jnp.stack([local, flat[:, 1], flat[:, 2]], axis=-1)
    spot = (owner[None, None, :] == jnp.arange(ndev, dtype=jnp.int32)[:, None, None]) & (
        slot[None, None, :] == jnp.arange(cap, dtype=jnp.int32)[None, :, None]
    )
    wanted = jnp.sum(jnp.where(spot[..., None], values[None, None], 0), axis=2)
    asked = lax.all_to_all(wanted, "dev", split_axis=0, concat_axis=0, tiled=True)
    patches_cut = cut_patches(tiles, asked.reshape(ndev * cap, 3)).reshape(ndev, cap * BOX, BOX)
    arrived = lax.all_to_all(patches_cut, "dev", split_axis=0, concat_axis=0, tiled=True)
    arrived = arrived.reshape(ndev, cap, BOX, BOX)
    patch = arrived[owner, slot].reshape(count, TILTS, BOX, BOX)
    padded = TILTS + TILTS % 2
    pmat = patch.transpose(0, 2, 1, 3)
    pmat = jnp.pad(pmat, ((0, 0), (0, 0), (0, padded - TILTS), (0, 0))).reshape(
        count * BOX, padded * BOX
    )
    xs_np, zs_np = touched_points()
    xs, zs = jnp.asarray(xs_np), jnp.asarray(zs_np)
    volume = jnp.dot(pmat, back_points(padded, xs, zs), preferred_element_type=jnp.float32)
    volume = volume.astype(jnp.bfloat16)
    sample = lax.optimization_barrier(sample_points(xs, zs))
    cyl = jnp.dot(volume, sample, preferred_element_type=jnp.float32)
    cyl = cyl.astype(jnp.bfloat16).reshape(count, BOX, ROTS * CYCLES)
    owned = references.shape[0]
    parts = BOX // owned
    local_t = references.reshape(owned, ROTS, CYCLES).transpose(1, 0, 2).reshape(ROTS, owned * CYCLES)
    gathered = lax.all_gather(local_t[None], "dev", axis=0, tiled=True)
    gathered = gathered.reshape(CLASSES, parts, ROTS, owned * CYCLES)
    ref_float = gathered.astype(jnp.float32)
    ref_power = jnp.mean(ref_float * ref_float, axis=(1, 2, 3))
    cyl_three = (
        cyl.reshape(count, BOX, ROTS, CYCLES)
        .transpose(0, 2, 1, 3)
        .reshape(count, ROTS, parts, owned * CYCLES)
    )
    corr = sum(
        jnp.einsum(
            "pfm,cgm->pfgc", cyl_three[:, :, q], gathered[:, q], preferred_element_type=jnp.float32
        )
        for q in range(parts)
    )
    raw = jnp.einsum("pfgc,kfg->pck", corr, shift_table(), precision=lax.Precision.HIGHEST)
    cyl_float = cyl.astype(jnp.float32)
    power = jnp.mean(cyl_float.reshape(count, -1) ** 2, axis=1)
    total = BOX * ROTS * CYCLES
    scores = raw / jnp.sqrt(
        total * (power[:, None, None] + 1e-06) * (ref_power[None, :, None] + 1e-06)
    )
    scores = scores.reshape(count, CLASSES * ROTS)
    columns = jnp.arange(ROTS * CYCLES, dtype=jnp.int32)
    index = (columns[None, :] + rotations[:, None] * CYCLES) % (ROTS * CYCLES)
    turned = jnp.take_along_axis(cyl, index[:, None, :], axis=2)
    member = (classes[:, None] == jnp.arange(CLASSES, dtype=jnp.int32)[None, :]).astype(
        jnp.bfloat16
    )
    placed = member[:, :, None, None] * turned[:, None, :, :]
    placed = placed.reshape(count, ndev, owned, ROTS * CYCLES)
    landed = lax.all_to_all(placed, "dev", split_axis=1, concat_axis=0, tiled=True)
    class_sums = jnp.sum(landed.astype(jnp.float32), axis=(0, 1))
    return (scores, class_sums)


def solution(mesh):
    in_specs = (P("dev", None, None), P("dev", None, None), P("dev"), P("dev"), P("dev", None))
    out_specs = (P("dev", None), P("dev", None))
    return jax.shard_map(
        per_device, mesh=mesh, in_specs=in_specs, out_specs=out_specs, check_vma=False
    )
```

```python
import functools

import jax
import jax.numpy as jnp
import ml_dtypes
import numpy as np
from jax import lax
from jax.experimental import pallas as pl
from jax.experimental.pallas import tpu as pltpu
from jax.sharding import PartitionSpec as P

TILTS = 21
BOX = 64
CYCLES = 16
ROTS = 32
CLASSES = 16
WIN = 256


def back_matrix_np(count):
    f32 = np.float32
    center = f32((BOX - 1) / 2.0)
    tilt = np.arange(count, dtype=f32)[:, None, None, None]
    pixel = np.arange(BOX, dtype=f32)[None, :, None, None]
    xpos = np.arange(BOX, dtype=f32)[None, None, :, None]
    zpos = np.arange(BOX, dtype=f32)[None, None, None, :]
    theta = (f32(-60.0) + f32(120.0) * tilt / f32(TILTS - 1)) * f32(np.pi / 180.0)
    place = (xpos - center) * np.cos(theta) + (zpos - center) * np.sin(theta) + center
    weight = np.maximum(f32(0.0), f32(1.0) - np.abs(place - pixel))
    weight = np.where(tilt < TILTS, weight, f32(0.0)) / f32(TILTS)
    weight = weight.astype(f32).astype(ml_dtypes.bfloat16)
    return weight.reshape(count * BOX, BOX * BOX)


def cyl_matrix_np():
    f32 = np.float32
    center = f32((BOX - 1) / 2.0)
    xpos = np.arange(BOX, dtype=f32)[:, None, None, None]
    zpos = np.arange(BOX, dtype=f32)[None, :, None, None]
    angle = np.arange(ROTS, dtype=f32)[None, None, :, None] * f32(2.0 * np.pi / ROTS)
    radius = (np.arange(CYCLES, dtype=f32)[None, None, None, :] + f32(0.5)) * f32(
        BOX / (2.0 * CYCLES)
    )
    wx = np.maximum(f32(0.0), f32(1.0) - np.abs(xpos - center - radius * np.cos(angle)))
    wz = np.maximum(f32(0.0), f32(1.0) - np.abs(zpos - center - radius * np.sin(angle)))
    sample = (wx * wz).astype(f32).astype(ml_dtypes.bfloat16)
    return sample.reshape(BOX * BOX, ROTS * CYCLES)


@functools.lru_cache(maxsize=None)
def touched_points():
    sample = cyl_matrix_np().astype(np.float32)
    used = np.nonzero(np.abs(sample).sum(axis=1))[0]
    size = -(-len(used) // 128) * 128
    xs = np.full((size,), -100.0, np.float32)
    zs = np.full((size,), -100.0, np.float32)
    xs[: len(used)] = used // BOX
    zs[: len(used)] = used % BOX
    return xs, zs


def back_points(count, xs, zs):
    center = (BOX - 1) / 2.0
    tilt = jnp.arange(count, dtype=jnp.float32)[:, None, None]
    pixel = jnp.arange(BOX, dtype=jnp.float32)[None, :, None]
    theta = (-60.0 + 120.0 * tilt / (TILTS - 1)) * (jnp.pi / 180.0)
    place = (xs[None, None, :] - center) * jnp.cos(theta) + (zs[None, None, :] - center) * jnp.sin(
        theta
    ) + center
    weight = jnp.maximum(0.0, 1.0 - jnp.abs(place - pixel))
    weight = jnp.where(tilt < TILTS, weight, 0.0) / TILTS
    return weight.reshape(count * BOX, xs.shape[0]).astype(jnp.bfloat16)


def sample_points(xs, zs):
    center = (BOX - 1) / 2.0
    angle = jnp.arange(ROTS, dtype=jnp.float32)[None, :, None] * (2.0 * jnp.pi / ROTS)
    radius = (jnp.arange(CYCLES, dtype=jnp.float32)[None, None, :] + 0.5) * (BOX / (2.0 * CYCLES))
    wx = jnp.maximum(0.0, 1.0 - jnp.abs(xs[:, None, None] - center - radius * jnp.cos(angle)))
    wz = jnp.maximum(0.0, 1.0 - jnp.abs(zs[:, None, None] - center - radius * jnp.sin(angle)))
    return (wx * wz).reshape(xs.shape[0], ROTS * CYCLES).astype(jnp.bfloat16)


def shift_table():
    steps = jnp.arange(ROTS, dtype=jnp.int32)
    want = (steps[None, :, None] - steps[:, None, None]) % ROTS
    return (steps[None, None, :] == want).astype(jnp.float32)


def cut_kernel(cap, req_ref, tiles_ref, out_ref):
    ends = out_ref.shape[0]
    width = tiles_ref.shape[2]
    rows = tiles_ref.shape[1]
    span = BOX + 16

    def body(d, carry):
        for s in range(cap):
            k = d * cap + s
            t = req_ref[3 * k]
            r = req_ref[3 * k + 1]
            c = req_ref[3 * k + 2]
            r0 = pl.multiple_of(jnp.minimum((r // 16) * 16, rows - span), 16)
            c0 = pl.multiple_of(jnp.minimum((c // 128) * 128, width - WIN), 128)
            win = tiles_ref[t, pl.ds(r0, span), pl.ds(c0, WIN)].astype(jnp.float32)
            win = pltpu.roll(win, (WIN - (c - c0)) % WIN, 1)[:, :128]
            win = pltpu.roll(win, (span - (r - r0)) % span, 0)
            flip = win[:BOX, :].T
            out_ref[d, :, s * BOX : (s + 1) * BOX] = flip[:BOX, :BOX].astype(out_ref.dtype)
        return carry

    lax.fori_loop(0, ends, body, 0)


def cut_patches(tiles, req, ends, cap):
    flat = req.reshape(-1)
    return pl.pallas_call(
        functools.partial(cut_kernel, cap),
        out_shape=jax.ShapeDtypeStruct((ends, BOX, cap * BOX), tiles.dtype),
        grid_spec=pltpu.PrefetchScalarGridSpec(
            num_scalar_prefetch=1,
            grid=(1,),
            in_specs=[pl.BlockSpec(tiles.shape, lambda i, q: (0, 0, 0))],
            out_specs=pl.BlockSpec((ends, BOX, cap * BOX), lambda i, q: (0, 0, 0)),
        ),
        cost_estimate=pl.CostEstimate(
            flops=ends * cap * BOX * WIN * 64,
            transcendentals=0,
            bytes_accessed=tiles.size * 2 + ends * cap * BOX * BOX * 2,
        ),
    )(flat, tiles)


def per_device(tiles, footprint, classes, rotations, references):
    ndev = lax.axis_size("dev")
    count = footprint.shape[0]
    asks = count * TILTS
    cap = (2 * asks + ndev - 1) // ndev
    held = tiles.shape[0]
    flat = footprint.reshape(asks, 3)
    owner = flat[:, 0] // held
    local = flat[:, 0] - owner * held
    hits = (owner[:, None] == jnp.arange(ndev, dtype=jnp.int32)[None, :]).astype(jnp.int32)
    slot = jnp.sum((jnp.cumsum(hits, axis=0) - hits) * hits, axis=1)
    values = jnp.stack([local, flat[:, 1], flat[:, 2]], axis=-1)
    spot = (owner[None, None, :] == jnp.arange(ndev, dtype=jnp.int32)[:, None, None]) & (
        slot[None, None, :] == jnp.arange(cap, dtype=jnp.int32)[None, :, None]
    )
    wanted = jnp.sum(jnp.where(spot[..., None], values[None, None], 0), axis=2)
    asked = lax.all_to_all(wanted, "dev", split_axis=0, concat_axis=0, tiled=True)
    patches_cut = cut_patches(tiles, asked.reshape(ndev * cap, 3), ndev, cap)
    arrived = lax.all_to_all(patches_cut, "dev", split_axis=0, concat_axis=0, tiled=True)
    rows_of = arrived[owner]
    flipped = sum(
        jnp.where(slot[:, None, None] == s, rows_of[:, :, s * BOX : (s + 1) * BOX], 0)
        for s in range(cap)
    ).reshape(count, TILTS, BOX, BOX)
    padded = TILTS + TILTS % 2
    flipped = jnp.pad(flipped, ((0, 0), (0, padded - TILTS), (0, 0), (0, 0)))
    flipped = flipped.reshape(count, padded * BOX, BOX)
    xs_np, zs_np = touched_points()
    xs, zs = jnp.asarray(xs_np), jnp.asarray(zs_np)
    volume = jnp.einsum(
        "pky,kn->pyn", flipped, back_points(padded, xs, zs), preferred_element_type=jnp.float32
    )
    volume = volume.astype(jnp.bfloat16).reshape(count * BOX, xs.shape[0])
    sample = lax.optimization_barrier(sample_points(xs, zs))
    cyl = jnp.dot(volume, sample, preferred_element_type=jnp.float32)
    cyl = cyl.astype(jnp.bfloat16).reshape(count, BOX, ROTS * CYCLES)
    owned = references.shape[0]
    parts = BOX // owned
    local_t = references.reshape(owned, ROTS, CYCLES).transpose(1, 0, 2).reshape(ROTS, owned * CYCLES)
    gathered = lax.all_gather(local_t[None], "dev", axis=0, tiled=True)
    gathered = gathered.reshape(CLASSES, parts, ROTS, owned * CYCLES)
    ref_float = gathered.astype(jnp.float32)
    ref_power = jnp.mean(ref_float * ref_float, axis=(1, 2, 3))
    cyl_three = (
        cyl.reshape(count, BOX, ROTS, CYCLES)
        .transpose(0, 2, 1, 3)
        .reshape(count, ROTS, parts, owned * CYCLES)
    )
    corr = sum(
        jnp.einsum(
            "pfm,cgm->pfgc", cyl_three[:, :, q], gathered[:, q], preferred_element_type=jnp.float32
        )
        for q in range(parts)
    )
    raw = jnp.einsum("pfgc,kfg->pck", corr, shift_table(), precision=lax.Precision.HIGHEST)
    cyl_float = cyl.astype(jnp.float32)
    power = jnp.mean(cyl_float.reshape(count, -1) ** 2, axis=1)
    total = BOX * ROTS * CYCLES
    scores = raw / jnp.sqrt(
        total * (power[:, None, None] + 1e-06) * (ref_power[None, :, None] + 1e-06)
    )
    scores = scores.reshape(count, CLASSES * ROTS)
    columns = jnp.arange(ROTS * CYCLES, dtype=jnp.int32)
    index = (columns[None, :] + rotations[:, None] * CYCLES) % (ROTS * CYCLES)
    turned = jnp.take_along_axis(cyl, index[:, None, :], axis=2)
    member = (classes[:, None] == jnp.arange(CLASSES, dtype=jnp.int32)[None, :]).astype(
        jnp.bfloat16
    )
    placed = member[:, :, None, None] * turned[:, None, :, :]
    placed = placed.reshape(count, ndev, owned, ROTS * CYCLES)
    landed = lax.all_to_all(placed, "dev", split_axis=1, concat_axis=0, tiled=True)
    class_sums = jnp.sum(landed.astype(jnp.float32), axis=(0, 1))
    return (scores, class_sums)


def solution(mesh):
    in_specs = (P("dev", None, None), P("dev", None, None), P("dev"), P("dev"), P("dev", None))
    out_specs = (P("dev", None), P("dev", None))
    return jax.shard_map(
        per_device, mesh=mesh, in_specs=in_specs, out_specs=out_specs, check_vma=False
    )
```

```python
import functools

import jax
import jax.numpy as jnp
import ml_dtypes
import numpy as np
from jax import lax
from jax.experimental import pallas as pl
from jax.experimental.pallas import tpu as pltpu
from jax.sharding import PartitionSpec as P

TILTS = 21
BOX = 64
CYCLES = 16
ROTS = 32
CLASSES = 16
WIN = 256


def back_matrix_np(count):
    f32 = np.float32
    center = f32((BOX - 1) / 2.0)
    tilt = np.arange(count, dtype=f32)[:, None, None, None]
    pixel = np.arange(BOX, dtype=f32)[None, :, None, None]
    xpos = np.arange(BOX, dtype=f32)[None, None, :, None]
    zpos = np.arange(BOX, dtype=f32)[None, None, None, :]
    theta = (f32(-60.0) + f32(120.0) * tilt / f32(TILTS - 1)) * f32(np.pi / 180.0)
    place = (xpos - center) * np.cos(theta) + (zpos - center) * np.sin(theta) + center
    weight = np.maximum(f32(0.0), f32(1.0) - np.abs(place - pixel))
    weight = np.where(tilt < TILTS, weight, f32(0.0)) / f32(TILTS)
    weight = weight.astype(f32).astype(ml_dtypes.bfloat16)
    return weight.reshape(count * BOX, BOX * BOX)


def cyl_matrix_np():
    f32 = np.float32
    center = f32((BOX - 1) / 2.0)
    xpos = np.arange(BOX, dtype=f32)[:, None, None, None]
    zpos = np.arange(BOX, dtype=f32)[None, :, None, None]
    angle = np.arange(ROTS, dtype=f32)[None, None, :, None] * f32(2.0 * np.pi / ROTS)
    radius = (np.arange(CYCLES, dtype=f32)[None, None, None, :] + f32(0.5)) * f32(
        BOX / (2.0 * CYCLES)
    )
    wx = np.maximum(f32(0.0), f32(1.0) - np.abs(xpos - center - radius * np.cos(angle)))
    wz = np.maximum(f32(0.0), f32(1.0) - np.abs(zpos - center - radius * np.sin(angle)))
    sample = (wx * wz).astype(f32).astype(ml_dtypes.bfloat16)
    return sample.reshape(BOX * BOX, ROTS * CYCLES)


@functools.lru_cache(maxsize=None)
def touched_points():
    sample = cyl_matrix_np().astype(np.float32)
    used = np.nonzero(np.abs(sample).sum(axis=1))[0]
    size = -(-len(used) // 128) * 128
    xs = np.full((size,), -100.0, np.float32)
    zs = np.full((size,), -100.0, np.float32)
    xs[: len(used)] = used // BOX
    zs[: len(used)] = used % BOX
    return xs, zs


def back_points(count, xs, zs):
    center = (BOX - 1) / 2.0
    tilt = jnp.arange(count, dtype=jnp.float32)[:, None, None]
    pixel = jnp.arange(BOX, dtype=jnp.float32)[None, :, None]
    theta = (-60.0 + 120.0 * tilt / (TILTS - 1)) * (jnp.pi / 180.0)
    place = (xs[None, None, :] - center) * jnp.cos(theta) + (zs[None, None, :] - center) * jnp.sin(
        theta
    ) + center
    weight = jnp.maximum(0.0, 1.0 - jnp.abs(place - pixel))
    weight = jnp.where(tilt < TILTS, weight, 0.0) / TILTS
    return weight.reshape(count * BOX, xs.shape[0]).astype(jnp.bfloat16)


def sample_points(xs, zs):
    center = (BOX - 1) / 2.0
    angle = jnp.arange(ROTS, dtype=jnp.float32)[None, :, None] * (2.0 * jnp.pi / ROTS)
    radius = (jnp.arange(CYCLES, dtype=jnp.float32)[None, None, :] + 0.5) * (BOX / (2.0 * CYCLES))
    wx = jnp.maximum(0.0, 1.0 - jnp.abs(xs[:, None, None] - center - radius * jnp.cos(angle)))
    wz = jnp.maximum(0.0, 1.0 - jnp.abs(zs[:, None, None] - center - radius * jnp.sin(angle)))
    return (wx * wz).reshape(xs.shape[0], ROTS * CYCLES).astype(jnp.bfloat16)


def shift_table():
    steps = jnp.arange(ROTS, dtype=jnp.int32)
    want = (steps[None, :, None] - steps[:, None, None]) % ROTS
    return (steps[None, None, :] == want).astype(jnp.float32)


def cut_kernel(cap, req_ref, tiles_ref, out_ref):
    ends = out_ref.shape[0]
    width = tiles_ref.shape[2]
    rows = tiles_ref.shape[1]
    span = BOX + 16

    def body(d, carry):
        for s in range(cap):
            k = d * cap + s
            t = req_ref[3 * k]
            r = req_ref[3 * k + 1]
            c = req_ref[3 * k + 2]
            r0 = pl.multiple_of(jnp.minimum((r // 16) * 16, rows - span), 16)
            c0 = pl.multiple_of(jnp.minimum((c // 128) * 128, width - WIN), 128)
            win = tiles_ref[t, pl.ds(r0, span), pl.ds(c0, WIN)].astype(jnp.float32)
            win = pltpu.roll(win, (WIN - (c - c0)) % WIN, 1)[:, :128]
            win = pltpu.roll(win, (span - (r - r0)) % span, 0)
            flip = win[:BOX, :].T
            out_ref[d, :, s * BOX : (s + 1) * BOX] = flip[:BOX, :BOX].astype(out_ref.dtype)
        return carry

    lax.fori_loop(0, ends, body, 0)


def cut_patches(tiles, req, ends, cap):
    flat = req.reshape(-1)
    return pl.pallas_call(
        functools.partial(cut_kernel, cap),
        out_shape=jax.ShapeDtypeStruct((ends, BOX, cap * BOX), tiles.dtype),
        grid_spec=pltpu.PrefetchScalarGridSpec(
            num_scalar_prefetch=1,
            grid=(1,),
            in_specs=[pl.BlockSpec(tiles.shape, lambda i, q: (0, 0, 0))],
            out_specs=pl.BlockSpec((ends, BOX, cap * BOX), lambda i, q: (0, 0, 0)),
        ),
        cost_estimate=pl.CostEstimate(
            flops=ends * cap * BOX * WIN * 64,
            transcendentals=0,
            bytes_accessed=tiles.size * 2 + ends * cap * BOX * BOX * 2,
        ),
    )(flat, tiles)


def double_gather(block, ndev):
    me = lax.axis_index("dev")
    step = 1
    while step < ndev:
        other = lax.ppermute(block, "dev", perm=[(i, i ^ step) for i in range(ndev)])
        low = (me // step) % 2 == 0
        block = jnp.where(
            low, jnp.concatenate([block, other], axis=0), jnp.concatenate([other, block], axis=0)
        )
        step *= 2
    return block


def per_device(tiles, footprint, classes, rotations, references):
    ndev = lax.axis_size("dev")
    count = footprint.shape[0]
    asks = count * TILTS
    cap = (2 * asks + ndev - 1) // ndev
    held = tiles.shape[0]
    flat = footprint.reshape(asks, 3)
    owner = flat[:, 0] // held
    local = flat[:, 0] - owner * held
    hits = (owner[:, None] == jnp.arange(ndev, dtype=jnp.int32)[None, :]).astype(jnp.int32)
    slot = jnp.sum((jnp.cumsum(hits, axis=0) - hits) * hits, axis=1)
    values = jnp.stack([local, flat[:, 1], flat[:, 2]], axis=-1)
    spot = (owner[None, None, :] == jnp.arange(ndev, dtype=jnp.int32)[:, None, None]) & (
        slot[None, None, :] == jnp.arange(cap, dtype=jnp.int32)[None, :, None]
    )
    wanted = jnp.sum(jnp.where(spot[..., None], values[None, None], 0), axis=2)
    asked = lax.all_to_all(wanted, "dev", split_axis=0, concat_axis=0, tiled=True)
    patches_cut = cut_patches(tiles, asked.reshape(ndev * cap, 3), ndev, cap)
    arrived = lax.all_to_all(patches_cut, "dev", split_axis=0, concat_axis=0, tiled=True)
    rows_of = arrived[owner]
    flipped = sum(
        jnp.where(slot[:, None, None] == s, rows_of[:, :, s * BOX : (s + 1) * BOX], 0)
        for s in range(cap)
    ).reshape(count, TILTS, BOX, BOX)
    padded = TILTS + TILTS % 2
    flipped = jnp.pad(flipped, ((0, 0), (0, padded - TILTS), (0, 0), (0, 0)))
    flipped = flipped.reshape(count, padded * BOX, BOX)
    xs_np, zs_np = touched_points()
    xs, zs = jnp.asarray(xs_np), jnp.asarray(zs_np)
    volume = jnp.einsum(
        "pky,kn->pyn", flipped, back_points(padded, xs, zs), preferred_element_type=jnp.float32
    )
    volume = volume.astype(jnp.bfloat16).reshape(count * BOX, xs.shape[0])
    sample = lax.optimization_barrier(sample_points(xs, zs))
    cyl = jnp.dot(volume, sample, preferred_element_type=jnp.float32)
    cyl = cyl.astype(jnp.bfloat16).reshape(count, BOX, ROTS * CYCLES)
    owned = references.shape[0]
    parts = BOX // owned
    local_t = references.reshape(owned, ROTS, CYCLES).transpose(1, 0, 2).reshape(ROTS, owned * CYCLES)
    gathered = double_gather(local_t[None], ndev)
    gathered = gathered.reshape(CLASSES, parts, ROTS, owned * CYCLES)
    ref_float = gathered.astype(jnp.float32)
    ref_power = jnp.mean(ref_float * ref_float, axis=(1, 2, 3))
    cyl_three = (
        cyl.reshape(count, BOX, ROTS, CYCLES)
        .transpose(0, 2, 1, 3)
        .reshape(count, ROTS, parts, owned * CYCLES)
    )
    corr = sum(
        jnp.einsum(
            "pfm,cgm->pfgc", cyl_three[:, :, q], gathered[:, q], preferred_element_type=jnp.float32
        )
        for q in range(parts)
    )
    raw = jnp.einsum("pfgc,kfg->pck", corr, shift_table(), precision=lax.Precision.HIGHEST)
    cyl_float = cyl.astype(jnp.float32)
    power = jnp.mean(cyl_float.reshape(count, -1) ** 2, axis=1)
    total = BOX * ROTS * CYCLES
    scores = raw / jnp.sqrt(
        total * (power[:, None, None] + 1e-06) * (ref_power[None, :, None] + 1e-06)
    )
    scores = scores.reshape(count, CLASSES * ROTS)
    columns = jnp.arange(ROTS * CYCLES, dtype=jnp.int32)
    index = (columns[None, :] + rotations[:, None] * CYCLES) % (ROTS * CYCLES)
    turned = jnp.take_along_axis(cyl, index[:, None, :], axis=2)
    member = (classes[:, None] == jnp.arange(CLASSES, dtype=jnp.int32)[None, :]).astype(
        jnp.bfloat16
    )
    placed = member[:, :, None, None] * turned[:, None, :, :]
    placed = placed.reshape(count, ndev, owned, ROTS * CYCLES)
    landed = lax.all_to_all(placed, "dev", split_axis=1, concat_axis=0, tiled=True)
    class_sums = jnp.sum(landed.astype(jnp.float32), axis=(0, 1))
    return (scores, class_sums)


def solution(mesh):
    in_specs = (P("dev", None, None), P("dev", None, None), P("dev"), P("dev"), P("dev", None))
    out_specs = (P("dev", None), P("dev", None))
    return jax.shard_map(
        per_device, mesh=mesh, in_specs=in_specs, out_specs=out_specs, check_vma=False
    )
```

```python
import functools

import jax
import jax.numpy as jnp
import ml_dtypes
import numpy as np
from jax import lax
from jax.experimental import pallas as pl
from jax.experimental.pallas import tpu as pltpu
from jax.sharding import PartitionSpec as P

TILTS = 21
BOX = 64
CYCLES = 16
ROTS = 32
CLASSES = 16
WIN = 256


def back_matrix_np(count):
    f32 = np.float32
    center = f32((BOX - 1) / 2.0)
    tilt = np.arange(count, dtype=f32)[:, None, None, None]
    pixel = np.arange(BOX, dtype=f32)[None, :, None, None]
    xpos = np.arange(BOX, dtype=f32)[None, None, :, None]
    zpos = np.arange(BOX, dtype=f32)[None, None, None, :]
    theta = (f32(-60.0) + f32(120.0) * tilt / f32(TILTS - 1)) * f32(np.pi / 180.0)
    place = (xpos - center) * np.cos(theta) + (zpos - center) * np.sin(theta) + center
    weight = np.maximum(f32(0.0), f32(1.0) - np.abs(place - pixel))
    weight = np.where(tilt < TILTS, weight, f32(0.0)) / f32(TILTS)
    weight = weight.astype(f32).astype(ml_dtypes.bfloat16)
    return weight.reshape(count * BOX, BOX * BOX)


def cyl_matrix_np():
    f32 = np.float32
    center = f32((BOX - 1) / 2.0)
    xpos = np.arange(BOX, dtype=f32)[:, None, None, None]
    zpos = np.arange(BOX, dtype=f32)[None, :, None, None]
    angle = np.arange(ROTS, dtype=f32)[None, None, :, None] * f32(2.0 * np.pi / ROTS)
    radius = (np.arange(CYCLES, dtype=f32)[None, None, None, :] + f32(0.5)) * f32(
        BOX / (2.0 * CYCLES)
    )
    wx = np.maximum(f32(0.0), f32(1.0) - np.abs(xpos - center - radius * np.cos(angle)))
    wz = np.maximum(f32(0.0), f32(1.0) - np.abs(zpos - center - radius * np.sin(angle)))
    sample = (wx * wz).astype(f32).astype(ml_dtypes.bfloat16)
    return sample.reshape(BOX * BOX, ROTS * CYCLES)


@functools.lru_cache(maxsize=None)
def touched_points():
    sample = cyl_matrix_np().astype(np.float32)
    used = np.nonzero(np.abs(sample).sum(axis=1))[0]
    size = -(-len(used) // 128) * 128
    xs = np.full((size,), -100.0, np.float32)
    zs = np.full((size,), -100.0, np.float32)
    xs[: len(used)] = used // BOX
    zs[: len(used)] = used % BOX
    return xs, zs


def back_points(count, xs, zs):
    center = (BOX - 1) / 2.0
    tilt = jnp.arange(count, dtype=jnp.float32)[:, None, None]
    pixel = jnp.arange(BOX, dtype=jnp.float32)[None, :, None]
    theta = (-60.0 + 120.0 * tilt / (TILTS - 1)) * (jnp.pi / 180.0)
    place = (xs[None, None, :] - center) * jnp.cos(theta) + (zs[None, None, :] - center) * jnp.sin(
        theta
    ) + center
    weight = jnp.maximum(0.0, 1.0 - jnp.abs(place - pixel))
    weight = jnp.where(tilt < TILTS, weight, 0.0) / TILTS
    return weight.reshape(count * BOX, xs.shape[0]).astype(jnp.bfloat16)


def sample_points(xs, zs):
    center = (BOX - 1) / 2.0
    angle = jnp.arange(ROTS, dtype=jnp.float32)[None, :, None] * (2.0 * jnp.pi / ROTS)
    radius = (jnp.arange(CYCLES, dtype=jnp.float32)[None, None, :] + 0.5) * (BOX / (2.0 * CYCLES))
    wx = jnp.maximum(0.0, 1.0 - jnp.abs(xs[:, None, None] - center - radius * jnp.cos(angle)))
    wz = jnp.maximum(0.0, 1.0 - jnp.abs(zs[:, None, None] - center - radius * jnp.sin(angle)))
    return (wx * wz).reshape(xs.shape[0], ROTS * CYCLES).astype(jnp.bfloat16)


def shift_table():
    steps = jnp.arange(ROTS, dtype=jnp.int32)
    want = (steps[None, :, None] - steps[:, None, None]) % ROTS
    return (steps[None, None, :] == want).astype(jnp.float32)


def cut_kernel(cap, req_ref, tiles_ref, out_ref):
    ends = out_ref.shape[0]
    width = tiles_ref.shape[2]
    rows = tiles_ref.shape[1]
    span = BOX + 16

    def body(d, carry):
        for s in range(cap):
            k = d * cap + s
            t = req_ref[3 * k]
            r = req_ref[3 * k + 1]
            c = req_ref[3 * k + 2]
            r0 = pl.multiple_of(jnp.minimum((r // 16) * 16, rows - span), 16)
            c0 = pl.multiple_of(jnp.minimum((c // 128) * 128, width - WIN), 128)
            win = tiles_ref[t, pl.ds(r0, span), pl.ds(c0, WIN)].astype(jnp.float32)
            win = pltpu.roll(win, (WIN - (c - c0)) % WIN, 1)[:, :128]
            win = pltpu.roll(win, (span - (r - r0)) % span, 0)
            flip = win[:BOX, :].T
            out_ref[d, :, s * BOX : (s + 1) * BOX] = flip[:BOX, :BOX].astype(out_ref.dtype)
        return carry

    lax.fori_loop(0, ends, body, 0)


def cut_patches(tiles, req, ends, cap):
    flat = req.reshape(-1)
    return pl.pallas_call(
        functools.partial(cut_kernel, cap),
        out_shape=jax.ShapeDtypeStruct((ends, BOX, cap * BOX), tiles.dtype),
        grid_spec=pltpu.PrefetchScalarGridSpec(
            num_scalar_prefetch=1,
            grid=(1,),
            in_specs=[pl.BlockSpec(tiles.shape, lambda i, q: (0, 0, 0))],
            out_specs=pl.BlockSpec((ends, BOX, cap * BOX), lambda i, q: (0, 0, 0)),
        ),
        cost_estimate=pl.CostEstimate(
            flops=ends * cap * BOX * WIN * 64,
            transcendentals=0,
            bytes_accessed=tiles.size * 2 + ends * cap * BOX * BOX * 2,
        ),
    )(flat, tiles)


def double_gather(block, ndev):
    me = lax.axis_index("dev")
    bits = ndev.bit_length() - 1
    for level in range(bits):
        step = ndev >> (level + 1)
        other = lax.ppermute(block, "dev", perm=[(i, i ^ step) for i in range(ndev)])
        low = (me // step) % 2 == 0
        block = jnp.where(
            low, jnp.concatenate([block, other], axis=0), jnp.concatenate([other, block], axis=0)
        )
    rest = block.shape[1:]
    block = block.reshape((2,) * bits + rest)
    block = block.transpose(tuple(range(bits))[::-1] + tuple(range(bits, block.ndim)))
    return block.reshape((ndev,) + rest)


def per_device(tiles, footprint, classes, rotations, references):
    ndev = lax.axis_size("dev")
    count = footprint.shape[0]
    asks = count * TILTS
    cap = (2 * asks + ndev - 1) // ndev
    held = tiles.shape[0]
    flat = footprint.reshape(asks, 3)
    owner = flat[:, 0] // held
    local = flat[:, 0] - owner * held
    hits = (owner[:, None] == jnp.arange(ndev, dtype=jnp.int32)[None, :]).astype(jnp.int32)
    slot = jnp.sum((jnp.cumsum(hits, axis=0) - hits) * hits, axis=1)
    values = jnp.stack([local, flat[:, 1], flat[:, 2]], axis=-1)
    spot = (owner[None, None, :] == jnp.arange(ndev, dtype=jnp.int32)[:, None, None]) & (
        slot[None, None, :] == jnp.arange(cap, dtype=jnp.int32)[None, :, None]
    )
    wanted = jnp.sum(jnp.where(spot[..., None], values[None, None], 0), axis=2)
    asked = lax.all_to_all(wanted, "dev", split_axis=0, concat_axis=0, tiled=True)
    patches_cut = cut_patches(tiles, asked.reshape(ndev * cap, 3), ndev, cap)
    arrived = lax.all_to_all(patches_cut, "dev", split_axis=0, concat_axis=0, tiled=True)
    rows_of = arrived[owner]
    flipped = sum(
        jnp.where(slot[:, None, None] == s, rows_of[:, :, s * BOX : (s + 1) * BOX], 0)
        for s in range(cap)
    ).reshape(count, TILTS, BOX, BOX)
    padded = TILTS + TILTS % 2
    flipped = jnp.pad(flipped, ((0, 0), (0, padded - TILTS), (0, 0), (0, 0)))
    flipped = flipped.reshape(count, padded * BOX, BOX)
    xs_np, zs_np = touched_points()
    xs, zs = jnp.asarray(xs_np), jnp.asarray(zs_np)
    volume = jnp.einsum(
        "pky,kn->pyn", flipped, back_points(padded, xs, zs), preferred_element_type=jnp.float32
    )
    volume = volume.astype(jnp.bfloat16).reshape(count * BOX, xs.shape[0])
    sample = lax.optimization_barrier(sample_points(xs, zs))
    cyl = jnp.dot(volume, sample, preferred_element_type=jnp.float32)
    cyl = cyl.astype(jnp.bfloat16).reshape(count, BOX, ROTS * CYCLES)
    owned = references.shape[0]
    parts = BOX // owned
    local_t = references.reshape(owned, ROTS, CYCLES).transpose(1, 0, 2).reshape(ROTS, owned * CYCLES)
    gathered = double_gather(local_t[None], ndev)
    gathered = gathered.reshape(CLASSES, parts, ROTS, owned * CYCLES)
    ref_float = gathered.astype(jnp.float32)
    ref_power = jnp.mean(ref_float * ref_float, axis=(1, 2, 3))
    cyl_three = (
        cyl.reshape(count, BOX, ROTS, CYCLES)
        .transpose(0, 2, 1, 3)
        .reshape(count, ROTS, parts, owned * CYCLES)
    )
    corr = sum(
        jnp.einsum(
            "pfm,cgm->pfgc", cyl_three[:, :, q], gathered[:, q], preferred_element_type=jnp.float32
        )
        for q in range(parts)
    )
    raw = jnp.einsum("pfgc,kfg->pck", corr, shift_table(), precision=lax.Precision.HIGHEST)
    cyl_float = cyl.astype(jnp.float32)
    power = jnp.mean(cyl_float.reshape(count, -1) ** 2, axis=1)
    total = BOX * ROTS * CYCLES
    scores = raw / jnp.sqrt(
        total * (power[:, None, None] + 1e-06) * (ref_power[None, :, None] + 1e-06)
    )
    scores = scores.reshape(count, CLASSES * ROTS)
    columns = jnp.arange(ROTS * CYCLES, dtype=jnp.int32)
    index = (columns[None, :] + rotations[:, None] * CYCLES) % (ROTS * CYCLES)
    turned = jnp.take_along_axis(cyl, index[:, None, :], axis=2)
    member = (classes[:, None] == jnp.arange(CLASSES, dtype=jnp.int32)[None, :]).astype(
        jnp.bfloat16
    )
    placed = member[:, :, None, None] * turned[:, None, :, :]
    placed = placed.reshape(count, ndev, owned, ROTS * CYCLES)
    landed = lax.all_to_all(placed, "dev", split_axis=1, concat_axis=0, tiled=True)
    class_sums = jnp.sum(landed.astype(jnp.float32), axis=(0, 1))
    return (scores, class_sums)


def solution(mesh):
    in_specs = (P("dev", None, None), P("dev", None, None), P("dev"), P("dev"), P("dev", None))
    out_specs = (P("dev", None), P("dev", None))
    return jax.shard_map(
        per_device, mesh=mesh, in_specs=in_specs, out_specs=out_specs, check_vma=False
    )
```

```python
import functools

import jax
import jax.numpy as jnp
import ml_dtypes
import numpy as np
from jax import lax
from jax.experimental import pallas as pl
from jax.experimental.pallas import tpu as pltpu
from jax.sharding import PartitionSpec as P

TILTS = 21
BOX = 64
CYCLES = 16
ROTS = 32
CLASSES = 16
WIN = 256


def back_matrix_np(count):
    f32 = np.float32
    center = f32((BOX - 1) / 2.0)
    tilt = np.arange(count, dtype=f32)[:, None, None, None]
    pixel = np.arange(BOX, dtype=f32)[None, :, None, None]
    xpos = np.arange(BOX, dtype=f32)[None, None, :, None]
    zpos = np.arange(BOX, dtype=f32)[None, None, None, :]
    theta = (f32(-60.0) + f32(120.0) * tilt / f32(TILTS - 1)) * f32(np.pi / 180.0)
    place = (xpos - center) * np.cos(theta) + (zpos - center) * np.sin(theta) + center
    weight = np.maximum(f32(0.0), f32(1.0) - np.abs(place - pixel))
    weight = np.where(tilt < TILTS, weight, f32(0.0)) / f32(TILTS)
    weight = weight.astype(f32).astype(ml_dtypes.bfloat16)
    return weight.reshape(count * BOX, BOX * BOX)


def cyl_matrix_np():
    f32 = np.float32
    center = f32((BOX - 1) / 2.0)
    xpos = np.arange(BOX, dtype=f32)[:, None, None, None]
    zpos = np.arange(BOX, dtype=f32)[None, :, None, None]
    angle = np.arange(ROTS, dtype=f32)[None, None, :, None] * f32(2.0 * np.pi / ROTS)
    radius = (np.arange(CYCLES, dtype=f32)[None, None, None, :] + f32(0.5)) * f32(
        BOX / (2.0 * CYCLES)
    )
    wx = np.maximum(f32(0.0), f32(1.0) - np.abs(xpos - center - radius * np.cos(angle)))
    wz = np.maximum(f32(0.0), f32(1.0) - np.abs(zpos - center - radius * np.sin(angle)))
    sample = (wx * wz).astype(f32).astype(ml_dtypes.bfloat16)
    return sample.reshape(BOX * BOX, ROTS * CYCLES)


@functools.lru_cache(maxsize=None)
def touched_points():
    sample = cyl_matrix_np().astype(np.float32)
    used = np.nonzero(np.abs(sample).sum(axis=1))[0]
    size = -(-len(used) // 128) * 128
    xs = np.full((size,), -100.0, np.float32)
    zs = np.full((size,), -100.0, np.float32)
    xs[: len(used)] = used // BOX
    zs[: len(used)] = used % BOX
    return xs, zs


def back_points(count, xs, zs):
    center = (BOX - 1) / 2.0
    tilt = jnp.arange(count, dtype=jnp.float32)[:, None, None]
    pixel = jnp.arange(BOX, dtype=jnp.float32)[None, :, None]
    theta = (-60.0 + 120.0 * tilt / (TILTS - 1)) * (jnp.pi / 180.0)
    place = (xs[None, None, :] - center) * jnp.cos(theta) + (zs[None, None, :] - center) * jnp.sin(
        theta
    ) + center
    weight = jnp.maximum(0.0, 1.0 - jnp.abs(place - pixel))
    weight = jnp.where(tilt < TILTS, weight, 0.0) / TILTS
    return weight.reshape(count * BOX, xs.shape[0]).astype(jnp.bfloat16)


def sample_points(xs, zs):
    center = (BOX - 1) / 2.0
    angle = jnp.arange(ROTS, dtype=jnp.float32)[None, :, None] * (2.0 * jnp.pi / ROTS)
    radius = (jnp.arange(CYCLES, dtype=jnp.float32)[None, None, :] + 0.5) * (BOX / (2.0 * CYCLES))
    wx = jnp.maximum(0.0, 1.0 - jnp.abs(xs[:, None, None] - center - radius * jnp.cos(angle)))
    wz = jnp.maximum(0.0, 1.0 - jnp.abs(zs[:, None, None] - center - radius * jnp.sin(angle)))
    return (wx * wz).reshape(xs.shape[0], ROTS * CYCLES).astype(jnp.bfloat16)


def shift_table():
    steps = jnp.arange(ROTS, dtype=jnp.int32)
    want = (steps[None, :, None] - steps[:, None, None]) % ROTS
    return (steps[None, None, :] == want).astype(jnp.float32)


def cut_kernel(cap, req_ref, tiles_ref, out_ref):
    ends = out_ref.shape[0]
    width = tiles_ref.shape[2]
    rows = tiles_ref.shape[1]
    span = BOX + 16

    def body(d, carry):
        for s in range(cap):
            k = d * cap + s
            t = req_ref[3 * k]
            r = req_ref[3 * k + 1]
            c = req_ref[3 * k + 2]
            r0 = pl.multiple_of(jnp.minimum((r // 16) * 16, rows - span), 16)
            c0 = pl.multiple_of(jnp.minimum((c // 128) * 128, width - WIN), 128)
            win = tiles_ref[t, pl.ds(r0, span), pl.ds(c0, WIN)].astype(jnp.float32)
            win = pltpu.roll(win, (WIN - (c - c0)) % WIN, 1)[:, :128]
            win = pltpu.roll(win, (span - (r - r0)) % span, 0)
            flip = win[:BOX, :].T
            out_ref[d, :, s * BOX : (s + 1) * BOX] = flip[:BOX, :BOX].astype(out_ref.dtype)
        return carry

    lax.fori_loop(0, ends, body, 0)


def cut_patches(tiles, req, ends, cap):
    flat = req.reshape(-1)
    return pl.pallas_call(
        functools.partial(cut_kernel, cap),
        out_shape=jax.ShapeDtypeStruct((ends, BOX, cap * BOX), tiles.dtype),
        grid_spec=pltpu.PrefetchScalarGridSpec(
            num_scalar_prefetch=1,
            grid=(1,),
            in_specs=[pl.BlockSpec(tiles.shape, lambda i, q: (0, 0, 0))],
            out_specs=pl.BlockSpec((ends, BOX, cap * BOX), lambda i, q: (0, 0, 0)),
        ),
        cost_estimate=pl.CostEstimate(
            flops=ends * cap * BOX * WIN * 64,
            transcendentals=0,
            bytes_accessed=tiles.size * 2 + ends * cap * BOX * BOX * 2,
        ),
    )(flat, tiles)


def double_gather(block, ndev):
    me = lax.axis_index("dev")
    bits = ndev.bit_length() - 1
    for level in range(bits):
        step = ndev >> (level + 1)
        other = lax.ppermute(block, "dev", perm=[(i, i ^ step) for i in range(ndev)])
        low = (me // step) % 2 == 0
        block = jnp.where(
            low, jnp.concatenate([block, other], axis=0), jnp.concatenate([other, block], axis=0)
        )
    rest = block.shape[1:]
    block = block.reshape((2,) * bits + rest)
    block = block.transpose(tuple(range(bits))[::-1] + tuple(range(bits, block.ndim)))
    return block.reshape((ndev,) + rest)


def per_device(tiles, footprint, classes, rotations, references):
    ndev = lax.axis_size("dev")
    count = footprint.shape[0]
    asks = count * TILTS
    cap = (2 * asks + ndev - 1) // ndev
    held = tiles.shape[0]
    flat = footprint.reshape(asks, 3)
    owner = flat[:, 0] // held
    local = flat[:, 0] - owner * held
    hits = (owner[:, None] == jnp.arange(ndev, dtype=jnp.int32)[None, :]).astype(jnp.int32)
    slot = jnp.sum((jnp.cumsum(hits, axis=0) - hits) * hits, axis=1)
    values = jnp.stack([local, flat[:, 1], flat[:, 2]], axis=-1)
    spot = (owner[None, None, :] == jnp.arange(ndev, dtype=jnp.int32)[:, None, None]) & (
        slot[None, None, :] == jnp.arange(cap, dtype=jnp.int32)[None, :, None]
    )
    wanted = jnp.sum(jnp.where(spot[..., None], values[None, None], 0), axis=2)
    asked = lax.all_to_all(wanted, "dev", split_axis=0, concat_axis=0, tiled=True)
    patches_cut = cut_patches(tiles, asked.reshape(ndev * cap, 3), ndev, cap)
    xs_np, zs_np = touched_points()
    xs, zs, patches_cut = lax.optimization_barrier(
        (jnp.asarray(xs_np), jnp.asarray(zs_np), patches_cut)
    )
    arrived = lax.all_to_all(patches_cut, "dev", split_axis=0, concat_axis=0, tiled=True)
    rows_of = arrived[owner]
    flipped = sum(
        jnp.where(slot[:, None, None] == s, rows_of[:, :, s * BOX : (s + 1) * BOX], 0)
        for s in range(cap)
    ).reshape(count, TILTS, BOX, BOX)
    padded = TILTS + TILTS % 2
    flipped = jnp.pad(flipped, ((0, 0), (0, padded - TILTS), (0, 0), (0, 0)))
    flipped = flipped.reshape(count, padded * BOX, BOX)
    volume = jnp.einsum(
        "pky,kn->pyn", flipped, back_points(padded, xs, zs), preferred_element_type=jnp.float32
    )
    volume = volume.astype(jnp.bfloat16).reshape(count * BOX, xs.shape[0])
    sample = lax.optimization_barrier(sample_points(xs, zs))
    cyl = jnp.dot(volume, sample, preferred_element_type=jnp.float32)
    cyl = cyl.astype(jnp.bfloat16).reshape(count, BOX, ROTS * CYCLES)
    owned = references.shape[0]
    parts = BOX // owned
    local_t = references.reshape(owned, ROTS, CYCLES).transpose(1, 0, 2).reshape(ROTS, owned * CYCLES)
    gathered = double_gather(local_t[None], ndev)
    gathered = gathered.reshape(CLASSES, parts, ROTS, owned * CYCLES)
    ref_float = gathered.astype(jnp.float32)
    ref_power = jnp.mean(ref_float * ref_float, axis=(1, 2, 3))
    cyl_three = (
        cyl.reshape(count, BOX, ROTS, CYCLES)
        .transpose(0, 2, 1, 3)
        .reshape(count, ROTS, parts, owned * CYCLES)
    )
    corr = sum(
        jnp.einsum(
            "pfm,cgm->pfgc", cyl_three[:, :, q], gathered[:, q], preferred_element_type=jnp.float32
        )
        for q in range(parts)
    )
    raw = jnp.einsum("pfgc,kfg->pck", corr, shift_table(), precision=lax.Precision.HIGHEST)
    cyl_float = cyl.astype(jnp.float32)
    power = jnp.mean(cyl_float.reshape(count, -1) ** 2, axis=1)
    total = BOX * ROTS * CYCLES
    scores = raw / jnp.sqrt(
        total * (power[:, None, None] + 1e-06) * (ref_power[None, :, None] + 1e-06)
    )
    scores = scores.reshape(count, CLASSES * ROTS)
    columns = jnp.arange(ROTS * CYCLES, dtype=jnp.int32)
    index = (columns[None, :] + rotations[:, None] * CYCLES) % (ROTS * CYCLES)
    turned = jnp.take_along_axis(cyl, index[:, None, :], axis=2)
    member = (classes[:, None] == jnp.arange(CLASSES, dtype=jnp.int32)[None, :]).astype(
        jnp.bfloat16
    )
    placed = member[:, :, None, None] * turned[:, None, :, :]
    placed = placed.reshape(count, ndev, owned, ROTS * CYCLES)
    landed = lax.all_to_all(placed, "dev", split_axis=1, concat_axis=0, tiled=True)
    class_sums = jnp.sum(landed.astype(jnp.float32), axis=(0, 1))
    return (scores, class_sums)


def solution(mesh):
    in_specs = (P("dev", None, None), P("dev", None, None), P("dev"), P("dev"), P("dev", None))
    out_specs = (P("dev", None), P("dev", None))
    return jax.shard_map(
        per_device, mesh=mesh, in_specs=in_specs, out_specs=out_specs, check_vma=False
    )
```

```python
import functools

import jax
import jax.numpy as jnp
import ml_dtypes
import numpy as np
from jax import lax
from jax.experimental import pallas as pl
from jax.experimental.pallas import tpu as pltpu
from jax.sharding import PartitionSpec as P

TILTS = 21
BOX = 64
CYCLES = 16
ROTS = 32
CLASSES = 16
WIN = 256


def back_matrix_np(count):
    f32 = np.float32
    center = f32((BOX - 1) / 2.0)
    tilt = np.arange(count, dtype=f32)[:, None, None, None]
    pixel = np.arange(BOX, dtype=f32)[None, :, None, None]
    xpos = np.arange(BOX, dtype=f32)[None, None, :, None]
    zpos = np.arange(BOX, dtype=f32)[None, None, None, :]
    theta = (f32(-60.0) + f32(120.0) * tilt / f32(TILTS - 1)) * f32(np.pi / 180.0)
    place = (xpos - center) * np.cos(theta) + (zpos - center) * np.sin(theta) + center
    weight = np.maximum(f32(0.0), f32(1.0) - np.abs(place - pixel))
    weight = np.where(tilt < TILTS, weight, f32(0.0)) / f32(TILTS)
    weight = weight.astype(f32).astype(ml_dtypes.bfloat16)
    return weight.reshape(count * BOX, BOX * BOX)


def cyl_matrix_np():
    f32 = np.float32
    center = f32((BOX - 1) / 2.0)
    xpos = np.arange(BOX, dtype=f32)[:, None, None, None]
    zpos = np.arange(BOX, dtype=f32)[None, :, None, None]
    angle = np.arange(ROTS, dtype=f32)[None, None, :, None] * f32(2.0 * np.pi / ROTS)
    radius = (np.arange(CYCLES, dtype=f32)[None, None, None, :] + f32(0.5)) * f32(
        BOX / (2.0 * CYCLES)
    )
    wx = np.maximum(f32(0.0), f32(1.0) - np.abs(xpos - center - radius * np.cos(angle)))
    wz = np.maximum(f32(0.0), f32(1.0) - np.abs(zpos - center - radius * np.sin(angle)))
    sample = (wx * wz).astype(f32).astype(ml_dtypes.bfloat16)
    return sample.reshape(BOX * BOX, ROTS * CYCLES)


@functools.lru_cache(maxsize=None)
def touched_points():
    sample = cyl_matrix_np().astype(np.float32)
    used = np.nonzero(np.abs(sample).sum(axis=1))[0]
    size = -(-len(used) // 128) * 128
    xs = np.full((size,), -100.0, np.float32)
    zs = np.full((size,), -100.0, np.float32)
    xs[: len(used)] = used // BOX
    zs[: len(used)] = used % BOX
    return xs, zs


def back_points(count, xs, zs):
    center = (BOX - 1) / 2.0
    tilt = jnp.arange(count, dtype=jnp.float32)[:, None, None]
    pixel = jnp.arange(BOX, dtype=jnp.float32)[None, :, None]
    theta = (-60.0 + 120.0 * tilt / (TILTS - 1)) * (jnp.pi / 180.0)
    place = (xs[None, None, :] - center) * jnp.cos(theta) + (zs[None, None, :] - center) * jnp.sin(
        theta
    ) + center
    weight = jnp.maximum(0.0, 1.0 - jnp.abs(place - pixel))
    weight = jnp.where(tilt < TILTS, weight, 0.0) / TILTS
    return weight.reshape(count * BOX, xs.shape[0]).astype(jnp.bfloat16)


def sample_points(xs, zs):
    center = (BOX - 1) / 2.0
    angle = jnp.arange(ROTS, dtype=jnp.float32)[None, :, None] * (2.0 * jnp.pi / ROTS)
    radius = (jnp.arange(CYCLES, dtype=jnp.float32)[None, None, :] + 0.5) * (BOX / (2.0 * CYCLES))
    wx = jnp.maximum(0.0, 1.0 - jnp.abs(xs[:, None, None] - center - radius * jnp.cos(angle)))
    wz = jnp.maximum(0.0, 1.0 - jnp.abs(zs[:, None, None] - center - radius * jnp.sin(angle)))
    return (wx * wz).reshape(xs.shape[0], ROTS * CYCLES).astype(jnp.bfloat16)


def shift_table():
    steps = jnp.arange(ROTS, dtype=jnp.int32)
    want = (steps[None, :, None] - steps[:, None, None]) % ROTS
    return (steps[None, None, :] == want).astype(jnp.float32)


def cut_kernel(cap, req_ref, tiles_ref, out_ref):
    ends = out_ref.shape[0]
    width = tiles_ref.shape[2]
    rows = tiles_ref.shape[1]
    span = BOX + 16

    def body(d, carry):
        for s in range(cap):
            k = d * cap + s
            t = req_ref[3 * k]
            r = req_ref[3 * k + 1]
            c = req_ref[3 * k + 2]
            r0 = pl.multiple_of(jnp.minimum((r // 16) * 16, rows - span), 16)
            c0 = pl.multiple_of(jnp.minimum((c // 128) * 128, width - WIN), 128)
            win = tiles_ref[t, pl.ds(r0, span), pl.ds(c0, WIN)].astype(jnp.float32)
            win = pltpu.roll(win, (WIN - (c - c0)) % WIN, 1)[:, :128]
            win = pltpu.roll(win, (span - (r - r0)) % span, 0)
            flip = win[:BOX, :].T
            out_ref[d, :, s * BOX : (s + 1) * BOX] = flip[:BOX, :BOX].astype(out_ref.dtype)
        return carry

    lax.fori_loop(0, ends, body, 0, unroll=2)


def cut_patches(tiles, req, ends, cap):
    flat = req.reshape(-1)
    return pl.pallas_call(
        functools.partial(cut_kernel, cap),
        out_shape=jax.ShapeDtypeStruct((ends, BOX, cap * BOX), tiles.dtype),
        grid_spec=pltpu.PrefetchScalarGridSpec(
            num_scalar_prefetch=1,
            grid=(1,),
            in_specs=[pl.BlockSpec(tiles.shape, lambda i, q: (0, 0, 0))],
            out_specs=pl.BlockSpec((ends, BOX, cap * BOX), lambda i, q: (0, 0, 0)),
        ),
        cost_estimate=pl.CostEstimate(
            flops=ends * cap * BOX * WIN * 64,
            transcendentals=0,
            bytes_accessed=tiles.size * 2 + ends * cap * BOX * BOX * 2,
        ),
    )(flat, tiles)


def double_gather(block, ndev):
    me = lax.axis_index("dev")
    bits = ndev.bit_length() - 1
    for level in range(bits):
        step = ndev >> (level + 1)
        other = lax.ppermute(block, "dev", perm=[(i, i ^ step) for i in range(ndev)])
        low = (me // step) % 2 == 0
        block = jnp.where(
            low, jnp.concatenate([block, other], axis=0), jnp.concatenate([other, block], axis=0)
        )
    rest = block.shape[1:]
    block = block.reshape((2,) * bits + rest)
    block = block.transpose(tuple(range(bits))[::-1] + tuple(range(bits, block.ndim)))
    return block.reshape((ndev,) + rest)


def per_device(tiles, footprint, classes, rotations, references):
    ndev = lax.axis_size("dev")
    count = footprint.shape[0]
    asks = count * TILTS
    cap = (2 * asks + ndev - 1) // ndev
    held = tiles.shape[0]
    flat = footprint.reshape(asks, 3)
    owner = flat[:, 0] // held
    local = flat[:, 0] - owner * held
    hits = (owner[:, None] == jnp.arange(ndev, dtype=jnp.int32)[None, :]).astype(jnp.int32)
    slot = jnp.sum((jnp.cumsum(hits, axis=0) - hits) * hits, axis=1)
    values = jnp.stack([local, flat[:, 1], flat[:, 2]], axis=-1)
    spot = (owner[None, None, :] == jnp.arange(ndev, dtype=jnp.int32)[:, None, None]) & (
        slot[None, None, :] == jnp.arange(cap, dtype=jnp.int32)[None, :, None]
    )
    wanted = jnp.sum(jnp.where(spot[..., None], values[None, None], 0), axis=2)
    asked = lax.all_to_all(wanted, "dev", split_axis=0, concat_axis=0, tiled=True)
    patches_cut = cut_patches(tiles, asked.reshape(ndev * cap, 3), ndev, cap)
    xs_np, zs_np = touched_points()
    xs, zs, patches_cut = lax.optimization_barrier(
        (jnp.asarray(xs_np), jnp.asarray(zs_np), patches_cut)
    )
    arrived = lax.all_to_all(patches_cut, "dev", split_axis=0, concat_axis=0, tiled=True)
    rows_of = arrived[owner]
    flipped = sum(
        jnp.where(slot[:, None, None] == s, rows_of[:, :, s * BOX : (s + 1) * BOX], 0)
        for s in range(cap)
    ).reshape(count, TILTS, BOX, BOX)
    padded = TILTS + TILTS % 2
    flipped = jnp.pad(flipped, ((0, 0), (0, padded - TILTS), (0, 0), (0, 0)))
    flipped = flipped.reshape(count, padded * BOX, BOX)
    volume = jnp.einsum(
        "pky,kn->pyn", flipped, back_points(padded, xs, zs), preferred_element_type=jnp.float32
    )
    volume = volume.astype(jnp.bfloat16).reshape(count * BOX, xs.shape[0])
    sample = lax.optimization_barrier(sample_points(xs, zs))
    cyl = jnp.dot(volume, sample, preferred_element_type=jnp.float32)
    cyl = cyl.astype(jnp.bfloat16).reshape(count, BOX, ROTS * CYCLES)
    owned = references.shape[0]
    parts = BOX // owned
    local_t = references.reshape(owned, ROTS, CYCLES).transpose(1, 0, 2).reshape(ROTS, owned * CYCLES)
    gathered = double_gather(local_t[None], ndev)
    gathered = gathered.reshape(CLASSES, parts, ROTS, owned * CYCLES)
    ref_float = gathered.astype(jnp.float32)
    ref_power = jnp.mean(ref_float * ref_float, axis=(1, 2, 3))
    cyl_three = (
        cyl.reshape(count, BOX, ROTS, CYCLES)
        .transpose(0, 2, 1, 3)
        .reshape(count, ROTS, parts, owned * CYCLES)
    )
    corr = sum(
        jnp.einsum(
            "pfm,cgm->pfgc", cyl_three[:, :, q], gathered[:, q], preferred_element_type=jnp.float32
        )
        for q in range(parts)
    )
    raw = jnp.einsum("pfgc,kfg->pck", corr, shift_table(), precision=lax.Precision.HIGHEST)
    cyl_float = cyl.astype(jnp.float32)
    power = jnp.mean(cyl_float.reshape(count, -1) ** 2, axis=1)
    total = BOX * ROTS * CYCLES
    scores = raw / jnp.sqrt(
        total * (power[:, None, None] + 1e-06) * (ref_power[None, :, None] + 1e-06)
    )
    scores = scores.reshape(count, CLASSES * ROTS)
    columns = jnp.arange(ROTS * CYCLES, dtype=jnp.int32)
    index = (columns[None, :] + rotations[:, None] * CYCLES) % (ROTS * CYCLES)
    turned = jnp.take_along_axis(cyl, index[:, None, :], axis=2)
    member = (classes[:, None] == jnp.arange(CLASSES, dtype=jnp.int32)[None, :]).astype(
        jnp.bfloat16
    )
    placed = member[:, :, None, None] * turned[:, None, :, :]
    placed = placed.reshape(count, ndev, owned, ROTS * CYCLES)
    landed = lax.all_to_all(placed, "dev", split_axis=1, concat_axis=0, tiled=True)
    class_sums = jnp.sum(landed.astype(jnp.float32), axis=(0, 1))
    return (scores, class_sums)


def solution(mesh):
    in_specs = (P("dev", None, None), P("dev", None, None), P("dev"), P("dev"), P("dev", None))
    out_specs = (P("dev", None), P("dev", None))
    return jax.shard_map(
        per_device, mesh=mesh, in_specs=in_specs, out_specs=out_specs, check_vma=False
    )
```

```python
import functools

import jax
import jax.numpy as jnp
import ml_dtypes
import numpy as np
from jax import lax
from jax.experimental import pallas as pl
from jax.experimental.pallas import tpu as pltpu
from jax.sharding import PartitionSpec as P

TILTS = 21
BOX = 64
CYCLES = 16
ROTS = 32
CLASSES = 16
WIN = 256


def back_matrix_np(count):
    f32 = np.float32
    center = f32((BOX - 1) / 2.0)
    tilt = np.arange(count, dtype=f32)[:, None, None, None]
    pixel = np.arange(BOX, dtype=f32)[None, :, None, None]
    xpos = np.arange(BOX, dtype=f32)[None, None, :, None]
    zpos = np.arange(BOX, dtype=f32)[None, None, None, :]
    theta = (f32(-60.0) + f32(120.0) * tilt / f32(TILTS - 1)) * f32(np.pi / 180.0)
    place = (xpos - center) * np.cos(theta) + (zpos - center) * np.sin(theta) + center
    weight = np.maximum(f32(0.0), f32(1.0) - np.abs(place - pixel))
    weight = np.where(tilt < TILTS, weight, f32(0.0)) / f32(TILTS)
    weight = weight.astype(f32).astype(ml_dtypes.bfloat16)
    return weight.reshape(count * BOX, BOX * BOX)


def cyl_matrix_np():
    f32 = np.float32
    center = f32((BOX - 1) / 2.0)
    xpos = np.arange(BOX, dtype=f32)[:, None, None, None]
    zpos = np.arange(BOX, dtype=f32)[None, :, None, None]
    angle = np.arange(ROTS, dtype=f32)[None, None, :, None] * f32(2.0 * np.pi / ROTS)
    radius = (np.arange(CYCLES, dtype=f32)[None, None, None, :] + f32(0.5)) * f32(
        BOX / (2.0 * CYCLES)
    )
    wx = np.maximum(f32(0.0), f32(1.0) - np.abs(xpos - center - radius * np.cos(angle)))
    wz = np.maximum(f32(0.0), f32(1.0) - np.abs(zpos - center - radius * np.sin(angle)))
    sample = (wx * wz).astype(f32).astype(ml_dtypes.bfloat16)
    return sample.reshape(BOX * BOX, ROTS * CYCLES)


@functools.lru_cache(maxsize=None)
def touched_points():
    sample = cyl_matrix_np().astype(np.float32)
    used = np.nonzero(np.abs(sample).sum(axis=1))[0]
    size = -(-len(used) // 128) * 128
    xs = np.full((size,), -100.0, np.float32)
    zs = np.full((size,), -100.0, np.float32)
    xs[: len(used)] = used // BOX
    zs[: len(used)] = used % BOX
    return xs, zs


def back_points(count, xs, zs):
    center = (BOX - 1) / 2.0
    tilt = jnp.arange(count, dtype=jnp.float32)[:, None, None]
    pixel = jnp.arange(BOX, dtype=jnp.float32)[None, :, None]
    theta = (-60.0 + 120.0 * tilt / (TILTS - 1)) * (jnp.pi / 180.0)
    place = (xs[None, None, :] - center) * jnp.cos(theta) + (zs[None, None, :] - center) * jnp.sin(
        theta
    ) + center
    weight = jnp.maximum(0.0, 1.0 - jnp.abs(place - pixel))
    weight = jnp.where(tilt < TILTS, weight, 0.0) / TILTS
    return weight.reshape(count * BOX, xs.shape[0]).astype(jnp.bfloat16)


def sample_points(xs, zs):
    center = (BOX - 1) / 2.0
    angle = jnp.arange(ROTS, dtype=jnp.float32)[None, :, None] * (2.0 * jnp.pi / ROTS)
    radius = (jnp.arange(CYCLES, dtype=jnp.float32)[None, None, :] + 0.5) * (BOX / (2.0 * CYCLES))
    wx = jnp.maximum(0.0, 1.0 - jnp.abs(xs[:, None, None] - center - radius * jnp.cos(angle)))
    wz = jnp.maximum(0.0, 1.0 - jnp.abs(zs[:, None, None] - center - radius * jnp.sin(angle)))
    return (wx * wz).reshape(xs.shape[0], ROTS * CYCLES).astype(jnp.bfloat16)


def shift_table():
    steps = jnp.arange(ROTS, dtype=jnp.int32)
    want = (steps[None, :, None] - steps[:, None, None]) % ROTS
    return (steps[None, None, :] == want).astype(jnp.float32)


def cut_kernel(cap, req_ref, tiles_ref, out_ref):
    ends = out_ref.shape[0]
    width = tiles_ref.shape[2]
    rows = tiles_ref.shape[1]
    span = BOX + 16

    def body(d, carry):
        for s in range(cap):
            k = d * cap + s
            t = req_ref[3 * k]
            r = req_ref[3 * k + 1]
            c = req_ref[3 * k + 2]
            r0 = pl.multiple_of(jnp.minimum((r // 16) * 16, rows - span), 16)
            c0 = pl.multiple_of(jnp.minimum((c // 128) * 128, width - WIN), 128)
            win = tiles_ref[t, pl.ds(r0, span), pl.ds(c0, WIN)].astype(jnp.float32)
            win = pltpu.roll(win, (WIN - (c - c0)) % WIN, 1)[:, :128]
            win = pltpu.roll(win, (span - (r - r0)) % span, 0)
            flip = win[:BOX, :].T
            out_ref[d, :, s * BOX : (s + 1) * BOX] = flip[:BOX, :BOX].astype(out_ref.dtype)
        return carry

    lax.fori_loop(0, ends, body, 0, unroll=4)


def cut_patches(tiles, req, ends, cap):
    flat = req.reshape(-1)
    return pl.pallas_call(
        functools.partial(cut_kernel, cap),
        out_shape=jax.ShapeDtypeStruct((ends, BOX, cap * BOX), tiles.dtype),
        grid_spec=pltpu.PrefetchScalarGridSpec(
            num_scalar_prefetch=1,
            grid=(1,),
            in_specs=[pl.BlockSpec(tiles.shape, lambda i, q: (0, 0, 0))],
            out_specs=pl.BlockSpec((ends, BOX, cap * BOX), lambda i, q: (0, 0, 0)),
        ),
        cost_estimate=pl.CostEstimate(
            flops=ends * cap * BOX * WIN * 64,
            transcendentals=0,
            bytes_accessed=tiles.size * 2 + ends * cap * BOX * BOX * 2,
        ),
    )(flat, tiles)


def double_gather(block, ndev):
    me = lax.axis_index("dev")
    bits = ndev.bit_length() - 1
    for level in range(bits):
        step = ndev >> (level + 1)
        other = lax.ppermute(block, "dev", perm=[(i, i ^ step) for i in range(ndev)])
        low = (me // step) % 2 == 0
        block = jnp.where(
            low, jnp.concatenate([block, other], axis=0), jnp.concatenate([other, block], axis=0)
        )
    rest = block.shape[1:]
    block = block.reshape((2,) * bits + rest)
    block = block.transpose(tuple(range(bits))[::-1] + tuple(range(bits, block.ndim)))
    return block.reshape((ndev,) + rest)


def per_device(tiles, footprint, classes, rotations, references):
    ndev = lax.axis_size("dev")
    count = footprint.shape[0]
    asks = count * TILTS
    cap = (2 * asks + ndev - 1) // ndev
    held = tiles.shape[0]
    flat = footprint.reshape(asks, 3)
    owner = flat[:, 0] // held
    local = flat[:, 0] - owner * held
    hits = (owner[:, None] == jnp.arange(ndev, dtype=jnp.int32)[None, :]).astype(jnp.int32)
    slot = jnp.sum((jnp.cumsum(hits, axis=0) - hits) * hits, axis=1)
    values = jnp.stack([local, flat[:, 1], flat[:, 2]], axis=-1)
    spot = (owner[None, None, :] == jnp.arange(ndev, dtype=jnp.int32)[:, None, None]) & (
        slot[None, None, :] == jnp.arange(cap, dtype=jnp.int32)[None, :, None]
    )
    wanted = jnp.sum(jnp.where(spot[..., None], values[None, None], 0), axis=2)
    asked = lax.all_to_all(wanted, "dev", split_axis=0, concat_axis=0, tiled=True)
    patches_cut = cut_patches(tiles, asked.reshape(ndev * cap, 3), ndev, cap)
    xs_np, zs_np = touched_points()
    xs, zs, patches_cut = lax.optimization_barrier(
        (jnp.asarray(xs_np), jnp.asarray(zs_np), patches_cut)
    )
    arrived = lax.all_to_all(patches_cut, "dev", split_axis=0, concat_axis=0, tiled=True)
    rows_of = arrived[owner]
    flipped = sum(
        jnp.where(slot[:, None, None] == s, rows_of[:, :, s * BOX : (s + 1) * BOX], 0)
        for s in range(cap)
    ).reshape(count, TILTS, BOX, BOX)
    padded = TILTS + TILTS % 2
    flipped = jnp.pad(flipped, ((0, 0), (0, padded - TILTS), (0, 0), (0, 0)))
    flipped = flipped.reshape(count, padded * BOX, BOX)
    volume = jnp.einsum(
        "pky,kn->pyn", flipped, back_points(padded, xs, zs), preferred_element_type=jnp.float32
    )
    volume = volume.astype(jnp.bfloat16).reshape(count * BOX, xs.shape[0])
    sample = lax.optimization_barrier(sample_points(xs, zs))
    cyl = jnp.dot(volume, sample, preferred_element_type=jnp.float32)
    cyl = cyl.astype(jnp.bfloat16).reshape(count, BOX, ROTS * CYCLES)
    owned = references.shape[0]
    parts = BOX // owned
    local_t = references.reshape(owned, ROTS, CYCLES).transpose(1, 0, 2).reshape(ROTS, owned * CYCLES)
    gathered = double_gather(local_t[None], ndev)
    gathered = gathered.reshape(CLASSES, parts, ROTS, owned * CYCLES)
    ref_float = gathered.astype(jnp.float32)
    ref_power = jnp.mean(ref_float * ref_float, axis=(1, 2, 3))
    cyl_three = (
        cyl.reshape(count, BOX, ROTS, CYCLES)
        .transpose(0, 2, 1, 3)
        .reshape(count, ROTS, parts, owned * CYCLES)
    )
    corr = sum(
        jnp.einsum(
            "pfm,cgm->pfgc", cyl_three[:, :, q], gathered[:, q], preferred_element_type=jnp.float32
        )
        for q in range(parts)
    )
    raw = jnp.einsum("pfgc,kfg->pck", corr, shift_table(), precision=lax.Precision.HIGHEST)
    cyl_float = cyl.astype(jnp.float32)
    power = jnp.mean(cyl_float.reshape(count, -1) ** 2, axis=1)
    total = BOX * ROTS * CYCLES
    scores = raw / jnp.sqrt(
        total * (power[:, None, None] + 1e-06) * (ref_power[None, :, None] + 1e-06)
    )
    scores = scores.reshape(count, CLASSES * ROTS)
    columns = jnp.arange(ROTS * CYCLES, dtype=jnp.int32)
    index = (columns[None, :] + rotations[:, None] * CYCLES) % (ROTS * CYCLES)
    turned = jnp.take_along_axis(cyl, index[:, None, :], axis=2)
    member = (classes[:, None] == jnp.arange(CLASSES, dtype=jnp.int32)[None, :]).astype(
        jnp.bfloat16
    )
    placed = member[:, :, None, None] * turned[:, None, :, :]
    placed = placed.reshape(count, ndev, owned, ROTS * CYCLES)
    landed = lax.all_to_all(placed, "dev", split_axis=1, concat_axis=0, tiled=True)
    class_sums = jnp.sum(landed.astype(jnp.float32), axis=(0, 1))
    return (scores, class_sums)


def solution(mesh):
    in_specs = (P("dev", None, None), P("dev", None, None), P("dev"), P("dev"), P("dev", None))
    out_specs = (P("dev", None), P("dev", None))
    return jax.shard_map(
        per_device, mesh=mesh, in_specs=in_specs, out_specs=out_specs, check_vma=False
    )
```

```python
import functools

import jax
import jax.numpy as jnp
import ml_dtypes
import numpy as np
from jax import lax
from jax.experimental import pallas as pl
from jax.experimental.pallas import tpu as pltpu
from jax.sharding import PartitionSpec as P

TILTS = 21
BOX = 64
CYCLES = 16
ROTS = 32
CLASSES = 16
WIN = 256


def back_matrix_np(count):
    f32 = np.float32
    center = f32((BOX - 1) / 2.0)
    tilt = np.arange(count, dtype=f32)[:, None, None, None]
    pixel = np.arange(BOX, dtype=f32)[None, :, None, None]
    xpos = np.arange(BOX, dtype=f32)[None, None, :, None]
    zpos = np.arange(BOX, dtype=f32)[None, None, None, :]
    theta = (f32(-60.0) + f32(120.0) * tilt / f32(TILTS - 1)) * f32(np.pi / 180.0)
    place = (xpos - center) * np.cos(theta) + (zpos - center) * np.sin(theta) + center
    weight = np.maximum(f32(0.0), f32(1.0) - np.abs(place - pixel))
    weight = np.where(tilt < TILTS, weight, f32(0.0)) / f32(TILTS)
    weight = weight.astype(f32).astype(ml_dtypes.bfloat16)
    return weight.reshape(count * BOX, BOX * BOX)


def cyl_matrix_np():
    f32 = np.float32
    center = f32((BOX - 1) / 2.0)
    xpos = np.arange(BOX, dtype=f32)[:, None, None, None]
    zpos = np.arange(BOX, dtype=f32)[None, :, None, None]
    angle = np.arange(ROTS, dtype=f32)[None, None, :, None] * f32(2.0 * np.pi / ROTS)
    radius = (np.arange(CYCLES, dtype=f32)[None, None, None, :] + f32(0.5)) * f32(
        BOX / (2.0 * CYCLES)
    )
    wx = np.maximum(f32(0.0), f32(1.0) - np.abs(xpos - center - radius * np.cos(angle)))
    wz = np.maximum(f32(0.0), f32(1.0) - np.abs(zpos - center - radius * np.sin(angle)))
    sample = (wx * wz).astype(f32).astype(ml_dtypes.bfloat16)
    return sample.reshape(BOX * BOX, ROTS * CYCLES)


@functools.lru_cache(maxsize=None)
def touched_points():
    sample = cyl_matrix_np().astype(np.float32)
    used = np.nonzero(np.abs(sample).sum(axis=1))[0]
    size = -(-len(used) // 128) * 128
    xs = np.full((size,), -100.0, np.float32)
    zs = np.full((size,), -100.0, np.float32)
    xs[: len(used)] = used // BOX
    zs[: len(used)] = used % BOX
    return xs, zs


def back_points(count, xs, zs):
    center = (BOX - 1) / 2.0
    tilt = jnp.arange(count, dtype=jnp.float32)[:, None, None]
    pixel = jnp.arange(BOX, dtype=jnp.float32)[None, :, None]
    theta = (-60.0 + 120.0 * tilt / (TILTS - 1)) * (jnp.pi / 180.0)
    place = (xs[None, None, :] - center) * jnp.cos(theta) + (zs[None, None, :] - center) * jnp.sin(
        theta
    ) + center
    weight = jnp.maximum(0.0, 1.0 - jnp.abs(place - pixel))
    weight = jnp.where(tilt < TILTS, weight, 0.0) / TILTS
    return weight.reshape(count * BOX, xs.shape[0]).astype(jnp.bfloat16)


def sample_points(xs, zs, turn=0):
    center = (BOX - 1) / 2.0
    steps = (jnp.arange(ROTS, dtype=jnp.int32) + turn) % ROTS
    angle = steps.astype(jnp.float32)[None, :, None] * (2.0 * jnp.pi / ROTS)
    radius = (jnp.arange(CYCLES, dtype=jnp.float32)[None, None, :] + 0.5) * (BOX / (2.0 * CYCLES))
    wx = jnp.maximum(0.0, 1.0 - jnp.abs(xs[:, None, None] - center - radius * jnp.cos(angle)))
    wz = jnp.maximum(0.0, 1.0 - jnp.abs(zs[:, None, None] - center - radius * jnp.sin(angle)))
    return (wx * wz).reshape(xs.shape[0], ROTS * CYCLES).astype(jnp.bfloat16)


def shift_table():
    steps = jnp.arange(ROTS, dtype=jnp.int32)
    want = (steps[None, :, None] - steps[:, None, None]) % ROTS
    return (steps[None, None, :] == want).astype(jnp.float32)


def cut_kernel(cap, req_ref, tiles_ref, out_ref):
    ends = out_ref.shape[0]
    width = tiles_ref.shape[2]
    rows = tiles_ref.shape[1]
    span = BOX + 16

    def body(d, carry):
        for s in range(cap):
            k = d * cap + s
            t = req_ref[3 * k]
            r = req_ref[3 * k + 1]
            c = req_ref[3 * k + 2]
            r0 = pl.multiple_of(jnp.minimum((r // 16) * 16, rows - span), 16)
            c0 = pl.multiple_of(jnp.minimum((c // 128) * 128, width - WIN), 128)
            win = tiles_ref[t, pl.ds(r0, span), pl.ds(c0, WIN)].astype(jnp.float32)
            win = pltpu.roll(win, (WIN - (c - c0)) % WIN, 1)[:, :128]
            win = pltpu.roll(win, (span - (r - r0)) % span, 0)
            flip = win[:BOX, :].T
            out_ref[d, :, s * BOX : (s + 1) * BOX] = flip[:BOX, :BOX].astype(out_ref.dtype)
        return carry

    lax.fori_loop(0, ends, body, 0, unroll=2)


def cut_patches(tiles, req, ends, cap):
    flat = req.reshape(-1)
    return pl.pallas_call(
        functools.partial(cut_kernel, cap),
        out_shape=jax.ShapeDtypeStruct((ends, BOX, cap * BOX), tiles.dtype),
        grid_spec=pltpu.PrefetchScalarGridSpec(
            num_scalar_prefetch=1,
            grid=(1,),
            in_specs=[pl.BlockSpec(tiles.shape, lambda i, q: (0, 0, 0))],
            out_specs=pl.BlockSpec((ends, BOX, cap * BOX), lambda i, q: (0, 0, 0)),
        ),
        cost_estimate=pl.CostEstimate(
            flops=ends * cap * BOX * WIN * 64,
            transcendentals=0,
            bytes_accessed=tiles.size * 2 + ends * cap * BOX * BOX * 2,
        ),
    )(flat, tiles)


def double_gather(block, ndev):
    me = lax.axis_index("dev")
    bits = ndev.bit_length() - 1
    for level in range(bits):
        step = ndev >> (level + 1)
        other = lax.ppermute(block, "dev", perm=[(i, i ^ step) for i in range(ndev)])
        low = (me // step) % 2 == 0
        block = jnp.where(
            low, jnp.concatenate([block, other], axis=0), jnp.concatenate([other, block], axis=0)
        )
    rest = block.shape[1:]
    block = block.reshape((2,) * bits + rest)
    block = block.transpose(tuple(range(bits))[::-1] + tuple(range(bits, block.ndim)))
    return block.reshape((ndev,) + rest)


def per_device(tiles, footprint, classes, rotations, references):
    ndev = lax.axis_size("dev")
    count = footprint.shape[0]
    asks = count * TILTS
    cap = (2 * asks + ndev - 1) // ndev
    held = tiles.shape[0]
    flat = footprint.reshape(asks, 3)
    owner = flat[:, 0] // held
    local = flat[:, 0] - owner * held
    hits = (owner[:, None] == jnp.arange(ndev, dtype=jnp.int32)[None, :]).astype(jnp.int32)
    slot = jnp.sum((jnp.cumsum(hits, axis=0) - hits) * hits, axis=1)
    values = jnp.stack([local, flat[:, 1], flat[:, 2]], axis=-1)
    spot = (owner[None, None, :] == jnp.arange(ndev, dtype=jnp.int32)[:, None, None]) & (
        slot[None, None, :] == jnp.arange(cap, dtype=jnp.int32)[None, :, None]
    )
    wanted = jnp.sum(jnp.where(spot[..., None], values[None, None], 0), axis=2)
    asked = lax.all_to_all(wanted, "dev", split_axis=0, concat_axis=0, tiled=True)
    patches_cut = cut_patches(tiles, asked.reshape(ndev * cap, 3), ndev, cap)
    xs_np, zs_np = touched_points()
    xs, zs, patches_cut = lax.optimization_barrier(
        (jnp.asarray(xs_np), jnp.asarray(zs_np), patches_cut)
    )
    arrived = lax.all_to_all(patches_cut, "dev", split_axis=0, concat_axis=0, tiled=True)
    rows_of = arrived[owner]
    flipped = sum(
        jnp.where(slot[:, None, None] == s, rows_of[:, :, s * BOX : (s + 1) * BOX], 0)
        for s in range(cap)
    ).reshape(count, TILTS, BOX, BOX)
    padded = TILTS + TILTS % 2
    flipped = jnp.pad(flipped, ((0, 0), (0, padded - TILTS), (0, 0), (0, 0)))
    flipped = flipped.reshape(count, padded * BOX, BOX)
    volume = jnp.einsum(
        "pky,kn->pyn", flipped, back_points(padded, xs, zs), preferred_element_type=jnp.float32
    )
    volume = volume.astype(jnp.bfloat16).reshape(count * BOX, xs.shape[0])
    sample, turned_sample = lax.optimization_barrier(
        (sample_points(xs, zs), jnp.stack([sample_points(xs, zs, q) for q in rotations]))
    )
    cyl = jnp.dot(volume, sample, preferred_element_type=jnp.float32)
    turned = jnp.einsum(
        "pyk,pkn->pyn",
        volume.reshape(count, BOX, xs.shape[0]),
        turned_sample,
        preferred_element_type=jnp.float32,
    ).astype(jnp.bfloat16)
    cyl = cyl.astype(jnp.bfloat16).reshape(count, BOX, ROTS * CYCLES)
    owned = references.shape[0]
    parts = BOX // owned
    local_t = references.reshape(owned, ROTS, CYCLES).transpose(1, 0, 2).reshape(ROTS, owned * CYCLES)
    gathered = double_gather(local_t[None], ndev)
    gathered = gathered.reshape(CLASSES, parts, ROTS, owned * CYCLES)
    ref_float = gathered.astype(jnp.float32)
    ref_power = jnp.mean(ref_float * ref_float, axis=(1, 2, 3))
    cyl_three = (
        cyl.reshape(count, BOX, ROTS, CYCLES)
        .transpose(0, 2, 1, 3)
        .reshape(count, ROTS, parts, owned * CYCLES)
    )
    corr = sum(
        jnp.einsum(
            "pfm,cgm->pfgc", cyl_three[:, :, q], gathered[:, q], preferred_element_type=jnp.float32
        )
        for q in range(parts)
    )
    raw = jnp.einsum("pfgc,kfg->pck", corr, shift_table(), precision=lax.Precision.HIGHEST)
    cyl_float = cyl.astype(jnp.float32)
    power = jnp.mean(cyl_float.reshape(count, -1) ** 2, axis=1)
    total = BOX * ROTS * CYCLES
    scores = raw / jnp.sqrt(
        total * (power[:, None, None] + 1e-06) * (ref_power[None, :, None] + 1e-06)
    )
    scores = scores.reshape(count, CLASSES * ROTS)
    member = (classes[:, None] == jnp.arange(CLASSES, dtype=jnp.int32)[None, :]).astype(
        jnp.bfloat16
    )
    placed = member[:, :, None, None] * turned[:, None, :, :]
    placed = placed.reshape(count, ndev, owned, ROTS * CYCLES)
    landed = lax.all_to_all(placed, "dev", split_axis=1, concat_axis=0, tiled=True)
    class_sums = jnp.sum(landed.astype(jnp.float32), axis=(0, 1))
    return (scores, class_sums)


def solution(mesh):
    in_specs = (P("dev", None, None), P("dev", None, None), P("dev"), P("dev"), P("dev", None))
    out_specs = (P("dev", None), P("dev", None))
    return jax.shard_map(
        per_device, mesh=mesh, in_specs=in_specs, out_specs=out_specs, check_vma=False
    )
```

```python
import functools

import jax
import jax.numpy as jnp
import ml_dtypes
import numpy as np
from jax import lax
from jax.experimental import pallas as pl
from jax.experimental.pallas import tpu as pltpu
from jax.sharding import PartitionSpec as P

TILTS = 21
BOX = 64
CYCLES = 16
ROTS = 32
CLASSES = 16
WIN = 256


def back_matrix_np(count):
    f32 = np.float32
    center = f32((BOX - 1) / 2.0)
    tilt = np.arange(count, dtype=f32)[:, None, None, None]
    pixel = np.arange(BOX, dtype=f32)[None, :, None, None]
    xpos = np.arange(BOX, dtype=f32)[None, None, :, None]
    zpos = np.arange(BOX, dtype=f32)[None, None, None, :]
    theta = (f32(-60.0) + f32(120.0) * tilt / f32(TILTS - 1)) * f32(np.pi / 180.0)
    place = (xpos - center) * np.cos(theta) + (zpos - center) * np.sin(theta) + center
    weight = np.maximum(f32(0.0), f32(1.0) - np.abs(place - pixel))
    weight = np.where(tilt < TILTS, weight, f32(0.0)) / f32(TILTS)
    weight = weight.astype(f32).astype(ml_dtypes.bfloat16)
    return weight.reshape(count * BOX, BOX * BOX)


def cyl_matrix_np():
    f32 = np.float32
    center = f32((BOX - 1) / 2.0)
    xpos = np.arange(BOX, dtype=f32)[:, None, None, None]
    zpos = np.arange(BOX, dtype=f32)[None, :, None, None]
    angle = np.arange(ROTS, dtype=f32)[None, None, :, None] * f32(2.0 * np.pi / ROTS)
    radius = (np.arange(CYCLES, dtype=f32)[None, None, None, :] + f32(0.5)) * f32(
        BOX / (2.0 * CYCLES)
    )
    wx = np.maximum(f32(0.0), f32(1.0) - np.abs(xpos - center - radius * np.cos(angle)))
    wz = np.maximum(f32(0.0), f32(1.0) - np.abs(zpos - center - radius * np.sin(angle)))
    sample = (wx * wz).astype(f32).astype(ml_dtypes.bfloat16)
    return sample.reshape(BOX * BOX, ROTS * CYCLES)


@functools.lru_cache(maxsize=None)
def touched_points():
    sample = cyl_matrix_np().astype(np.float32)
    used = np.nonzero(np.abs(sample).sum(axis=1))[0]
    size = -(-len(used) // 128) * 128
    xs = np.full((size,), -100.0, np.float32)
    zs = np.full((size,), -100.0, np.float32)
    xs[: len(used)] = used // BOX
    zs[: len(used)] = used % BOX
    return xs, zs


def back_points(count, xs, zs):
    center = (BOX - 1) / 2.0
    tilt = jnp.arange(count, dtype=jnp.float32)[:, None, None]
    pixel = jnp.arange(BOX, dtype=jnp.float32)[None, :, None]
    theta = (-60.0 + 120.0 * tilt / (TILTS - 1)) * (jnp.pi / 180.0)
    place = (xs[None, None, :] - center) * jnp.cos(theta) + (zs[None, None, :] - center) * jnp.sin(
        theta
    ) + center
    weight = jnp.maximum(0.0, 1.0 - jnp.abs(place - pixel))
    weight = jnp.where(tilt < TILTS, weight, 0.0) / TILTS
    return weight.reshape(count * BOX, xs.shape[0]).astype(jnp.bfloat16)


def sample_points(xs, zs):
    center = (BOX - 1) / 2.0
    angle = jnp.arange(ROTS, dtype=jnp.float32)[None, :, None] * (2.0 * jnp.pi / ROTS)
    radius = (jnp.arange(CYCLES, dtype=jnp.float32)[None, None, :] + 0.5) * (BOX / (2.0 * CYCLES))
    wx = jnp.maximum(0.0, 1.0 - jnp.abs(xs[:, None, None] - center - radius * jnp.cos(angle)))
    wz = jnp.maximum(0.0, 1.0 - jnp.abs(zs[:, None, None] - center - radius * jnp.sin(angle)))
    return (wx * wz).reshape(xs.shape[0], ROTS * CYCLES).astype(jnp.bfloat16)


def shift_table():
    steps = jnp.arange(ROTS, dtype=jnp.int32)
    want = (steps[None, :, None] - steps[:, None, None]) % ROTS
    return (steps[None, None, :] == want).astype(jnp.float32)


def cut_kernel(cap, req_ref, tiles_ref, out_ref):
    ends = out_ref.shape[0]
    width = tiles_ref.shape[2]
    rows = tiles_ref.shape[1]
    span = BOX + 16

    def body(d, carry):
        for s in range(cap):
            k = d * cap + s
            t = req_ref[3 * k]
            r = req_ref[3 * k + 1]
            c = req_ref[3 * k + 2]
            r0 = pl.multiple_of(jnp.minimum((r // 16) * 16, rows - span), 16)
            c0 = pl.multiple_of(jnp.minimum((c // 128) * 128, width - WIN), 128)
            win = tiles_ref[t, pl.ds(r0, span), pl.ds(c0, WIN)]
            win = pltpu.roll(win, (WIN - (c - c0)) % WIN, 1)[:, :128].astype(jnp.float32)
            win = pltpu.roll(win, (span - (r - r0)) % span, 0)
            flip = win[:BOX, :].T
            out_ref[d, :, s * BOX : (s + 1) * BOX] = flip[:BOX, :BOX].astype(out_ref.dtype)
        return carry

    lax.fori_loop(0, ends, body, 0, unroll=2)


def cut_patches(tiles, req, ends, cap):
    flat = req.reshape(-1)
    return pl.pallas_call(
        functools.partial(cut_kernel, cap),
        out_shape=jax.ShapeDtypeStruct((ends, BOX, cap * BOX), tiles.dtype),
        grid_spec=pltpu.PrefetchScalarGridSpec(
            num_scalar_prefetch=1,
            grid=(1,),
            in_specs=[pl.BlockSpec(tiles.shape, lambda i, q: (0, 0, 0))],
            out_specs=pl.BlockSpec((ends, BOX, cap * BOX), lambda i, q: (0, 0, 0)),
        ),
        cost_estimate=pl.CostEstimate(
            flops=ends * cap * BOX * WIN * 64,
            transcendentals=0,
            bytes_accessed=tiles.size * 2 + ends * cap * BOX * BOX * 2,
        ),
    )(flat, tiles)


def double_gather(block, ndev):
    me = lax.axis_index("dev")
    bits = ndev.bit_length() - 1
    for level in range(bits):
        step = ndev >> (level + 1)
        other = lax.ppermute(block, "dev", perm=[(i, i ^ step) for i in range(ndev)])
        low = (me // step) % 2 == 0
        block = jnp.where(
            low, jnp.concatenate([block, other], axis=0), jnp.concatenate([other, block], axis=0)
        )
    rest = block.shape[1:]
    block = block.reshape((2,) * bits + rest)
    block = block.transpose(tuple(range(bits))[::-1] + tuple(range(bits, block.ndim)))
    return block.reshape((ndev,) + rest)


def per_device(tiles, footprint, classes, rotations, references):
    ndev = lax.axis_size("dev")
    count = footprint.shape[0]
    asks = count * TILTS
    cap = (2 * asks + ndev - 1) // ndev
    held = tiles.shape[0]
    flat = footprint.reshape(asks, 3)
    owner = flat[:, 0] // held
    local = flat[:, 0] - owner * held
    hits = (owner[:, None] == jnp.arange(ndev, dtype=jnp.int32)[None, :]).astype(jnp.int32)
    slot = jnp.sum((jnp.cumsum(hits, axis=0) - hits) * hits, axis=1)
    values = jnp.stack([local, flat[:, 1], flat[:, 2]], axis=-1)
    spot = (owner[None, None, :] == jnp.arange(ndev, dtype=jnp.int32)[:, None, None]) & (
        slot[None, None, :] == jnp.arange(cap, dtype=jnp.int32)[None, :, None]
    )
    wanted = jnp.sum(jnp.where(spot[..., None], values[None, None], 0), axis=2)
    asked = lax.all_to_all(wanted, "dev", split_axis=0, concat_axis=0, tiled=True)
    patches_cut = cut_patches(tiles, asked.reshape(ndev * cap, 3), ndev, cap)
    xs_np, zs_np = touched_points()
    xs, zs, patches_cut = lax.optimization_barrier(
        (jnp.asarray(xs_np), jnp.asarray(zs_np), patches_cut)
    )
    arrived = lax.all_to_all(patches_cut, "dev", split_axis=0, concat_axis=0, tiled=True)
    rows_of = arrived[owner]
    flipped = sum(
        jnp.where(slot[:, None, None] == s, rows_of[:, :, s * BOX : (s + 1) * BOX], 0)
        for s in range(cap)
    ).reshape(count, TILTS, BOX, BOX)
    padded = TILTS + TILTS % 2
    flipped = jnp.pad(flipped, ((0, 0), (0, padded - TILTS), (0, 0), (0, 0)))
    flipped = flipped.reshape(count, padded * BOX, BOX)
    volume = jnp.einsum(
        "pky,kn->pyn", flipped, back_points(padded, xs, zs), preferred_element_type=jnp.float32
    )
    volume = volume.astype(jnp.bfloat16).reshape(count * BOX, xs.shape[0])
    sample = lax.optimization_barrier(sample_points(xs, zs))
    cyl = jnp.dot(volume, sample, preferred_element_type=jnp.float32)
    cyl = cyl.astype(jnp.bfloat16).reshape(count, BOX, ROTS * CYCLES)
    owned = references.shape[0]
    parts = BOX // owned
    local_t = references.reshape(owned, ROTS, CYCLES).transpose(1, 0, 2).reshape(ROTS, owned * CYCLES)
    gathered = double_gather(local_t[None], ndev)
    gathered = gathered.reshape(CLASSES, parts, ROTS, owned * CYCLES)
    ref_float = gathered.astype(jnp.float32)
    ref_power = jnp.mean(ref_float * ref_float, axis=(1, 2, 3))
    cyl_three = (
        cyl.reshape(count, BOX, ROTS, CYCLES)
        .transpose(0, 2, 1, 3)
        .reshape(count, ROTS, parts, owned * CYCLES)
    )
    corr = sum(
        jnp.einsum(
            "pfm,cgm->pfgc", cyl_three[:, :, q], gathered[:, q], preferred_element_type=jnp.float32
        )
        for q in range(parts)
    )
    raw = jnp.einsum("pfgc,kfg->pck", corr, shift_table(), precision=lax.Precision.HIGHEST)
    cyl_float = cyl.astype(jnp.float32)
    power = jnp.mean(cyl_float.reshape(count, -1) ** 2, axis=1)
    total = BOX * ROTS * CYCLES
    scores = raw / jnp.sqrt(
        total * (power[:, None, None] + 1e-06) * (ref_power[None, :, None] + 1e-06)
    )
    scores = scores.reshape(count, CLASSES * ROTS)
    columns = jnp.arange(ROTS * CYCLES, dtype=jnp.int32)
    index = (columns[None, :] + rotations[:, None] * CYCLES) % (ROTS * CYCLES)
    turned = jnp.take_along_axis(cyl, index[:, None, :], axis=2)
    member = (classes[:, None] == jnp.arange(CLASSES, dtype=jnp.int32)[None, :]).astype(
        jnp.bfloat16
    )
    placed = member[:, :, None, None] * turned[:, None, :, :]
    placed = placed.reshape(count, ndev, owned, ROTS * CYCLES)
    landed = lax.all_to_all(placed, "dev", split_axis=1, concat_axis=0, tiled=True)
    class_sums = jnp.sum(landed.astype(jnp.float32), axis=(0, 1))
    return (scores, class_sums)


def solution(mesh):
    in_specs = (P("dev", None, None), P("dev", None, None), P("dev"), P("dev"), P("dev", None))
    out_specs = (P("dev", None), P("dev", None))
    return jax.shard_map(
        per_device, mesh=mesh, in_specs=in_specs, out_specs=out_specs, check_vma=False
    )
```

```python
import functools

import jax
import jax.numpy as jnp
import ml_dtypes
import numpy as np
from jax import lax
from jax.experimental import pallas as pl
from jax.experimental.pallas import tpu as pltpu
from jax.sharding import PartitionSpec as P

TILTS = 21
BOX = 64
CYCLES = 16
ROTS = 32
CLASSES = 16
WIN = 256


def back_matrix_np(count):
    f32 = np.float32
    center = f32((BOX - 1) / 2.0)
    tilt = np.arange(count, dtype=f32)[:, None, None, None]
    pixel = np.arange(BOX, dtype=f32)[None, :, None, None]
    xpos = np.arange(BOX, dtype=f32)[None, None, :, None]
    zpos = np.arange(BOX, dtype=f32)[None, None, None, :]
    theta = (f32(-60.0) + f32(120.0) * tilt / f32(TILTS - 1)) * f32(np.pi / 180.0)
    place = (xpos - center) * np.cos(theta) + (zpos - center) * np.sin(theta) + center
    weight = np.maximum(f32(0.0), f32(1.0) - np.abs(place - pixel))
    weight = np.where(tilt < TILTS, weight, f32(0.0)) / f32(TILTS)
    weight = weight.astype(f32).astype(ml_dtypes.bfloat16)
    return weight.reshape(count * BOX, BOX * BOX)


def cyl_matrix_np():
    f32 = np.float32
    center = f32((BOX - 1) / 2.0)
    xpos = np.arange(BOX, dtype=f32)[:, None, None, None]
    zpos = np.arange(BOX, dtype=f32)[None, :, None, None]
    angle = np.arange(ROTS, dtype=f32)[None, None, :, None] * f32(2.0 * np.pi / ROTS)
    radius = (np.arange(CYCLES, dtype=f32)[None, None, None, :] + f32(0.5)) * f32(
        BOX / (2.0 * CYCLES)
    )
    wx = np.maximum(f32(0.0), f32(1.0) - np.abs(xpos - center - radius * np.cos(angle)))
    wz = np.maximum(f32(0.0), f32(1.0) - np.abs(zpos - center - radius * np.sin(angle)))
    sample = (wx * wz).astype(f32).astype(ml_dtypes.bfloat16)
    return sample.reshape(BOX * BOX, ROTS * CYCLES)


@functools.lru_cache(maxsize=None)
def touched_points():
    sample = cyl_matrix_np().astype(np.float32)
    used = np.nonzero(np.abs(sample).sum(axis=1))[0]
    size = -(-len(used) // 128) * 128
    xs = np.full((size,), -100.0, np.float32)
    zs = np.full((size,), -100.0, np.float32)
    xs[: len(used)] = used // BOX
    zs[: len(used)] = used % BOX
    return xs, zs


def back_points(count, xs, zs):
    center = (BOX - 1) / 2.0
    tilt = jnp.arange(count, dtype=jnp.float32)[:, None, None]
    pixel = jnp.arange(BOX, dtype=jnp.float32)[None, :, None]
    theta = (-60.0 + 120.0 * tilt / (TILTS - 1)) * (jnp.pi / 180.0)
    place = (xs[None, None, :] - center) * jnp.cos(theta) + (zs[None, None, :] - center) * jnp.sin(
        theta
    ) + center
    weight = jnp.maximum(0.0, 1.0 - jnp.abs(place - pixel))
    weight = jnp.where(tilt < TILTS, weight, 0.0) / TILTS
    return weight.reshape(count * BOX, xs.shape[0]).astype(jnp.bfloat16)


def sample_points(xs, zs):
    center = (BOX - 1) / 2.0
    angle = jnp.arange(ROTS, dtype=jnp.float32)[None, :, None] * (2.0 * jnp.pi / ROTS)
    radius = (jnp.arange(CYCLES, dtype=jnp.float32)[None, None, :] + 0.5) * (BOX / (2.0 * CYCLES))
    wx = jnp.maximum(0.0, 1.0 - jnp.abs(xs[:, None, None] - center - radius * jnp.cos(angle)))
    wz = jnp.maximum(0.0, 1.0 - jnp.abs(zs[:, None, None] - center - radius * jnp.sin(angle)))
    return (wx * wz).reshape(xs.shape[0], ROTS * CYCLES).astype(jnp.bfloat16)


def shift_table():
    steps = jnp.arange(ROTS, dtype=jnp.int32)
    want = (steps[None, :, None] - steps[:, None, None]) % ROTS
    return (steps[None, None, :] == want).astype(jnp.float32)


def cut_kernel(cap, req_ref, tiles_ref, out_ref):
    ends = out_ref.shape[0]
    width = tiles_ref.shape[2]
    rows = tiles_ref.shape[1]
    span = BOX + 16

    def body(d, carry):
        for s in range(cap):
            k = d * cap + s
            t = req_ref[3 * k]
            r = req_ref[3 * k + 1]
            c = req_ref[3 * k + 2]
            r0 = pl.multiple_of(jnp.minimum((r // 16) * 16, rows - span), 16)
            c0 = pl.multiple_of(jnp.minimum((c // 128) * 128, width - WIN), 128)
            win = tiles_ref[t, pl.ds(r0, span), pl.ds(c0, WIN)].astype(jnp.float32)
            win = pltpu.roll(win, (WIN - (c - c0)) % WIN, 1)[:, :128]
            win = pltpu.roll(win, (span - (r - r0)) % span, 0)
            flip = win[:BOX, :].T
            out_ref[d, :, s * BOX : (s + 1) * BOX] = flip[:BOX, :BOX].astype(out_ref.dtype)
        return carry

    lax.fori_loop(0, ends, body, 0, unroll=2)


def cut_patches(tiles, req, ends, cap):
    flat = req.reshape(-1)
    return pl.pallas_call(
        functools.partial(cut_kernel, cap),
        out_shape=jax.ShapeDtypeStruct((ends, BOX, cap * BOX), tiles.dtype),
        grid_spec=pltpu.PrefetchScalarGridSpec(
            num_scalar_prefetch=1,
            grid=(1,),
            in_specs=[pl.BlockSpec(tiles.shape, lambda i, q: (0, 0, 0))],
            out_specs=pl.BlockSpec((ends, BOX, cap * BOX), lambda i, q: (0, 0, 0)),
        ),
        cost_estimate=pl.CostEstimate(
            flops=ends * cap * BOX * WIN * 64,
            transcendentals=0,
            bytes_accessed=tiles.size * 2 + ends * cap * BOX * BOX * 2,
        ),
    )(flat, tiles)


def double_gather(block, ndev):
    me = lax.axis_index("dev")
    bits = ndev.bit_length() - 1
    for level in range(bits):
        step = ndev >> (level + 1)
        other = lax.ppermute(block, "dev", perm=[(i, i ^ step) for i in range(ndev)])
        low = (me // step) % 2 == 0
        block = jnp.where(
            low, jnp.concatenate([block, other], axis=0), jnp.concatenate([other, block], axis=0)
        )
    rest = block.shape[1:]
    block = block.reshape((2,) * bits + rest)
    block = block.transpose(tuple(range(bits))[::-1] + tuple(range(bits, block.ndim)))
    return block.reshape((ndev,) + rest)


def per_device(tiles, footprint, classes, rotations, references):
    ndev = lax.axis_size("dev")
    count = footprint.shape[0]
    asks = count * TILTS
    cap = (2 * asks + ndev - 1) // ndev
    held = tiles.shape[0]
    flat = footprint.reshape(asks, 3)
    owner = flat[:, 0] // held
    local = flat[:, 0] - owner * held
    hits = (owner[:, None] == jnp.arange(ndev, dtype=jnp.int32)[None, :]).astype(jnp.int32)
    slot = jnp.sum((jnp.cumsum(hits, axis=0) - hits) * hits, axis=1)
    values = jnp.stack([local, flat[:, 1], flat[:, 2]], axis=-1)
    spot = (owner[None, None, :] == jnp.arange(ndev, dtype=jnp.int32)[:, None, None]) & (
        slot[None, None, :] == jnp.arange(cap, dtype=jnp.int32)[None, :, None]
    )
    wanted = jnp.sum(jnp.where(spot[..., None], values[None, None], 0), axis=2)
    asked = lax.all_to_all(wanted, "dev", split_axis=0, concat_axis=0, tiled=True)
    patches_cut = cut_patches(tiles, asked.reshape(ndev * cap, 3), ndev, cap)
    xs_np, zs_np = touched_points()
    xs, zs, patches_cut = lax.optimization_barrier(
        (jnp.asarray(xs_np), jnp.asarray(zs_np), patches_cut)
    )
    arrived = lax.all_to_all(patches_cut, "dev", split_axis=0, concat_axis=0, tiled=True)
    rows_of = arrived[owner]
    flipped = sum(
        jnp.where(slot[:, None, None] == s, rows_of[:, :, s * BOX : (s + 1) * BOX], 0)
        for s in range(cap)
    ).reshape(count, TILTS, BOX, BOX)
    padded = TILTS + TILTS % 2
    flipped = jnp.pad(flipped, ((0, 0), (0, padded - TILTS), (0, 0), (0, 0)))
    flipped = flipped.reshape(count, padded * BOX, BOX)
    volume = jnp.einsum(
        "pky,kn->pyn", flipped, back_points(padded, xs, zs), preferred_element_type=jnp.float32
    )
    volume = volume.astype(jnp.bfloat16).reshape(count * BOX, xs.shape[0])
    sample = lax.optimization_barrier(sample_points(xs, zs))
    cyl = jnp.dot(volume, sample, preferred_element_type=jnp.float32)
    cyl = cyl.astype(jnp.bfloat16).reshape(count, BOX, ROTS * CYCLES)
    owned = references.shape[0]
    parts = BOX // owned
    local_t = references.reshape(owned, ROTS, CYCLES).transpose(1, 0, 2).reshape(ROTS, owned * CYCLES)
    gathered = double_gather(local_t[None], ndev)
    gathered = gathered.reshape(CLASSES, parts, ROTS, owned * CYCLES)
    ref_float = gathered.astype(jnp.float32)
    ref_power = jnp.mean(ref_float * ref_float, axis=(1, 2, 3))
    cyl_three = (
        cyl.reshape(count, BOX, ROTS, CYCLES)
        .transpose(0, 2, 1, 3)
        .reshape(count, ROTS, parts, owned * CYCLES)
    )
    corr = sum(
        jnp.einsum(
            "pfm,cgm->pfgc", cyl_three[:, :, q], gathered[:, q], preferred_element_type=jnp.float32
        )
        for q in range(parts)
    )
    raw = jnp.einsum("pfgc,kfg->pck", corr, shift_table(), precision=lax.Precision.HIGHEST)
    cyl_float = cyl.astype(jnp.float32)
    power = jnp.mean(cyl_float.reshape(count, -1) ** 2, axis=1)
    total = BOX * ROTS * CYCLES
    scores = raw / jnp.sqrt(
        total * (power[:, None, None] + 1e-06) * (ref_power[None, :, None] + 1e-06)
    )
    scores = scores.reshape(count, CLASSES * ROTS)
    doubled = jnp.concatenate([cyl, cyl], axis=2)
    turned = jnp.stack(
        [
            lax.dynamic_slice_in_dim(doubled[p], rotations[p] * CYCLES, ROTS * CYCLES, axis=1)
            for p in range(count)
        ]
    )
    member = (classes[:, None] == jnp.arange(CLASSES, dtype=jnp.int32)[None, :]).astype(
        jnp.bfloat16
    )
    placed = member[:, :, None, None] * turned[:, None, :, :]
    placed = placed.reshape(count, ndev, owned, ROTS * CYCLES)
    landed = lax.all_to_all(placed, "dev", split_axis=1, concat_axis=0, tiled=True)
    class_sums = jnp.sum(landed.astype(jnp.float32), axis=(0, 1))
    return (scores, class_sums)


def solution(mesh):
    in_specs = (P("dev", None, None), P("dev", None, None), P("dev"), P("dev"), P("dev", None))
    out_specs = (P("dev", None), P("dev", None))
    return jax.shard_map(
        per_device, mesh=mesh, in_specs=in_specs, out_specs=out_specs, check_vma=False
    )
```

```python
import functools

import jax
import jax.numpy as jnp
import ml_dtypes
import numpy as np
from jax import lax
from jax.experimental import pallas as pl
from jax.experimental.pallas import tpu as pltpu
from jax.sharding import PartitionSpec as P

TILTS = 21
BOX = 64
CYCLES = 16
ROTS = 32
CLASSES = 16
WIN = 256


def back_matrix_np(count):
    f32 = np.float32
    center = f32((BOX - 1) / 2.0)
    tilt = np.arange(count, dtype=f32)[:, None, None, None]
    pixel = np.arange(BOX, dtype=f32)[None, :, None, None]
    xpos = np.arange(BOX, dtype=f32)[None, None, :, None]
    zpos = np.arange(BOX, dtype=f32)[None, None, None, :]
    theta = (f32(-60.0) + f32(120.0) * tilt / f32(TILTS - 1)) * f32(np.pi / 180.0)
    place = (xpos - center) * np.cos(theta) + (zpos - center) * np.sin(theta) + center
    weight = np.maximum(f32(0.0), f32(1.0) - np.abs(place - pixel))
    weight = np.where(tilt < TILTS, weight, f32(0.0)) / f32(TILTS)
    weight = weight.astype(f32).astype(ml_dtypes.bfloat16)
    return weight.reshape(count * BOX, BOX * BOX)


def cyl_matrix_np():
    f32 = np.float32
    center = f32((BOX - 1) / 2.0)
    xpos = np.arange(BOX, dtype=f32)[:, None, None, None]
    zpos = np.arange(BOX, dtype=f32)[None, :, None, None]
    angle = np.arange(ROTS, dtype=f32)[None, None, :, None] * f32(2.0 * np.pi / ROTS)
    radius = (np.arange(CYCLES, dtype=f32)[None, None, None, :] + f32(0.5)) * f32(
        BOX / (2.0 * CYCLES)
    )
    wx = np.maximum(f32(0.0), f32(1.0) - np.abs(xpos - center - radius * np.cos(angle)))
    wz = np.maximum(f32(0.0), f32(1.0) - np.abs(zpos - center - radius * np.sin(angle)))
    sample = (wx * wz).astype(f32).astype(ml_dtypes.bfloat16)
    return sample.reshape(BOX * BOX, ROTS * CYCLES)


@functools.lru_cache(maxsize=None)
def touched_points():
    sample = cyl_matrix_np().astype(np.float32)
    used = np.nonzero(np.abs(sample).sum(axis=1))[0]
    size = -(-len(used) // 128) * 128
    xs = np.full((size,), -100.0, np.float32)
    zs = np.full((size,), -100.0, np.float32)
    xs[: len(used)] = used // BOX
    zs[: len(used)] = used % BOX
    return xs, zs


def back_points(count, xs, zs):
    center = (BOX - 1) / 2.0
    tilt = jnp.arange(count, dtype=jnp.float32)[:, None, None]
    pixel = jnp.arange(BOX, dtype=jnp.float32)[None, :, None]
    theta = (-60.0 + 120.0 * tilt / (TILTS - 1)) * (jnp.pi / 180.0)
    place = (xs[None, None, :] - center) * jnp.cos(theta) + (zs[None, None, :] - center) * jnp.sin(
        theta
    ) + center
    weight = jnp.maximum(0.0, 1.0 - jnp.abs(place - pixel))
    weight = jnp.where(tilt < TILTS, weight, 0.0) / TILTS
    return weight.reshape(count * BOX, xs.shape[0]).astype(jnp.bfloat16)


def sample_points(xs, zs):
    center = (BOX - 1) / 2.0
    angle = jnp.arange(ROTS, dtype=jnp.float32)[None, :, None] * (2.0 * jnp.pi / ROTS)
    radius = (jnp.arange(CYCLES, dtype=jnp.float32)[None, None, :] + 0.5) * (BOX / (2.0 * CYCLES))
    wx = jnp.maximum(0.0, 1.0 - jnp.abs(xs[:, None, None] - center - radius * jnp.cos(angle)))
    wz = jnp.maximum(0.0, 1.0 - jnp.abs(zs[:, None, None] - center - radius * jnp.sin(angle)))
    return (wx * wz).reshape(xs.shape[0], ROTS * CYCLES).astype(jnp.bfloat16)


def shift_table():
    steps = jnp.arange(ROTS, dtype=jnp.int32)
    want = (steps[None, :, None] - steps[:, None, None]) % ROTS
    return (steps[None, None, :] == want).astype(jnp.float32)


def cut_kernel(cap, req_ref, tiles_ref, out_ref):
    ends = out_ref.shape[0]
    width = tiles_ref.shape[2]
    rows = tiles_ref.shape[1]
    span = BOX + 16

    def body(d, carry):
        for s in range(cap):
            t = req_ref[d, s, 0]
            r = req_ref[d, s, 1]
            c = req_ref[d, s, 2]
            r0 = pl.multiple_of(jnp.minimum((r // 16) * 16, rows - span), 16)
            c0 = pl.multiple_of(jnp.minimum((c // 128) * 128, width - WIN), 128)
            win = tiles_ref[t, pl.ds(r0, span), pl.ds(c0, WIN)].astype(jnp.float32)
            win = pltpu.roll(win, (WIN - (c - c0)) % WIN, 1)[:, :128]
            win = pltpu.roll(win, (span - (r - r0)) % span, 0)
            flip = win[:BOX, :].T
            out_ref[d, :, s * BOX : (s + 1) * BOX] = flip[:BOX, :BOX].astype(out_ref.dtype)
        return carry

    lax.fori_loop(0, ends, body, 0, unroll=2)


def cut_patches(tiles, req, ends, cap):
    return pl.pallas_call(
        functools.partial(cut_kernel, cap),
        out_shape=jax.ShapeDtypeStruct((ends, BOX, cap * BOX), tiles.dtype),
        grid_spec=pltpu.PrefetchScalarGridSpec(
            num_scalar_prefetch=1,
            grid=(1,),
            in_specs=[pl.BlockSpec(tiles.shape, lambda i, q: (0, 0, 0))],
            out_specs=pl.BlockSpec((ends, BOX, cap * BOX), lambda i, q: (0, 0, 0)),
        ),
        cost_estimate=pl.CostEstimate(
            flops=ends * cap * BOX * WIN * 64,
            transcendentals=0,
            bytes_accessed=tiles.size * 2 + ends * cap * BOX * BOX * 2,
        ),
    )(req, tiles)


def double_gather(block, ndev):
    me = lax.axis_index("dev")
    bits = ndev.bit_length() - 1
    for level in range(bits):
        step = ndev >> (level + 1)
        other = lax.ppermute(block, "dev", perm=[(i, i ^ step) for i in range(ndev)])
        low = (me // step) % 2 == 0
        block = jnp.where(
            low, jnp.concatenate([block, other], axis=0), jnp.concatenate([other, block], axis=0)
        )
    rest = block.shape[1:]
    block = block.reshape((2,) * bits + rest)
    block = block.transpose(tuple(range(bits))[::-1] + tuple(range(bits, block.ndim)))
    return block.reshape((ndev,) + rest)


def per_device(tiles, footprint, classes, rotations, references):
    ndev = lax.axis_size("dev")
    count = footprint.shape[0]
    asks = count * TILTS
    cap = (2 * asks + ndev - 1) // ndev
    held = tiles.shape[0]
    flat = footprint.reshape(asks, 3)
    owner = flat[:, 0] // held
    local = flat[:, 0] - owner * held
    hits = (owner[:, None] == jnp.arange(ndev, dtype=jnp.int32)[None, :]).astype(jnp.int32)
    slot = jnp.sum((jnp.cumsum(hits, axis=0) - hits) * hits, axis=1)
    values = jnp.stack([local, flat[:, 1], flat[:, 2]], axis=-1)
    spot = (owner[None, None, :] == jnp.arange(ndev, dtype=jnp.int32)[:, None, None]) & (
        slot[None, None, :] == jnp.arange(cap, dtype=jnp.int32)[None, :, None]
    )
    wanted = jnp.sum(jnp.where(spot[..., None], values[None, None], 0), axis=2)
    asked = lax.all_to_all(wanted, "dev", split_axis=0, concat_axis=0, tiled=True)
    patches_cut = cut_patches(tiles, asked, ndev, cap)
    xs_np, zs_np = touched_points()
    xs, zs, patches_cut = lax.optimization_barrier(
        (jnp.asarray(xs_np), jnp.asarray(zs_np), patches_cut)
    )
    arrived = lax.all_to_all(patches_cut, "dev", split_axis=0, concat_axis=0, tiled=True)
    rows_of = arrived[owner]
    flipped = sum(
        jnp.where(slot[:, None, None] == s, rows_of[:, :, s * BOX : (s + 1) * BOX], 0)
        for s in range(cap)
    ).reshape(count, TILTS, BOX, BOX)
    padded = TILTS + TILTS % 2
    flipped = jnp.pad(flipped, ((0, 0), (0, padded - TILTS), (0, 0), (0, 0)))
    flipped = flipped.reshape(count, padded * BOX, BOX)
    volume = jnp.einsum(
        "pky,kn->pyn", flipped, back_points(padded, xs, zs), preferred_element_type=jnp.float32
    )
    volume = volume.astype(jnp.bfloat16).reshape(count * BOX, xs.shape[0])
    sample = lax.optimization_barrier(sample_points(xs, zs))
    cyl = jnp.dot(volume, sample, preferred_element_type=jnp.float32)
    cyl = cyl.astype(jnp.bfloat16).reshape(count, BOX, ROTS * CYCLES)
    owned = references.shape[0]
    parts = BOX // owned
    local_t = references.reshape(owned, ROTS, CYCLES).transpose(1, 0, 2).reshape(ROTS, owned * CYCLES)
    gathered = double_gather(local_t[None], ndev)
    gathered = gathered.reshape(CLASSES, parts, ROTS, owned * CYCLES)
    ref_float = gathered.astype(jnp.float32)
    ref_power = jnp.mean(ref_float * ref_float, axis=(1, 2, 3))
    cyl_three = (
        cyl.reshape(count, BOX, ROTS, CYCLES)
        .transpose(0, 2, 1, 3)
        .reshape(count, ROTS, parts, owned * CYCLES)
    )
    corr = sum(
        jnp.einsum(
            "pfm,cgm->pfgc", cyl_three[:, :, q], gathered[:, q], preferred_element_type=jnp.float32
        )
        for q in range(parts)
    )
    raw = jnp.einsum("pfgc,kfg->pck", corr, shift_table(), precision=lax.Precision.HIGHEST)
    cyl_float = cyl.astype(jnp.float32)
    power = jnp.mean(cyl_float.reshape(count, -1) ** 2, axis=1)
    total = BOX * ROTS * CYCLES
    scores = raw / jnp.sqrt(
        total * (power[:, None, None] + 1e-06) * (ref_power[None, :, None] + 1e-06)
    )
    scores = scores.reshape(count, CLASSES * ROTS)
    doubled = jnp.concatenate([cyl, cyl], axis=2)
    turned = jnp.stack(
        [
            lax.dynamic_slice_in_dim(doubled[p], rotations[p] * CYCLES, ROTS * CYCLES, axis=1)
            for p in range(count)
        ]
    )
    member = (classes[:, None] == jnp.arange(CLASSES, dtype=jnp.int32)[None, :]).astype(
        jnp.bfloat16
    )
    placed = member[:, :, None, None] * turned[:, None, :, :]
    placed = placed.reshape(count, ndev, owned, ROTS * CYCLES)
    landed = lax.all_to_all(placed, "dev", split_axis=1, concat_axis=0, tiled=True)
    class_sums = jnp.sum(landed.astype(jnp.float32), axis=(0, 1))
    return (scores, class_sums)


def solution(mesh):
    in_specs = (P("dev", None, None), P("dev", None, None), P("dev"), P("dev"), P("dev", None))
    out_specs = (P("dev", None), P("dev", None))
    return jax.shard_map(
        per_device, mesh=mesh, in_specs=in_specs, out_specs=out_specs, check_vma=False
    )
```

```python
import functools

import jax
import jax.numpy as jnp
import ml_dtypes
import numpy as np
from jax import lax
from jax.experimental import pallas as pl
from jax.experimental.pallas import tpu as pltpu
from jax.sharding import PartitionSpec as P

TILTS = 21
BOX = 64
CYCLES = 16
ROTS = 32
CLASSES = 16
WIN = 256


def back_matrix_np(count):
    f32 = np.float32
    center = f32((BOX - 1) / 2.0)
    tilt = np.arange(count, dtype=f32)[:, None, None, None]
    pixel = np.arange(BOX, dtype=f32)[None, :, None, None]
    xpos = np.arange(BOX, dtype=f32)[None, None, :, None]
    zpos = np.arange(BOX, dtype=f32)[None, None, None, :]
    theta = (f32(-60.0) + f32(120.0) * tilt / f32(TILTS - 1)) * f32(np.pi / 180.0)
    place = (xpos - center) * np.cos(theta) + (zpos - center) * np.sin(theta) + center
    weight = np.maximum(f32(0.0), f32(1.0) - np.abs(place - pixel))
    weight = np.where(tilt < TILTS, weight, f32(0.0)) / f32(TILTS)
    weight = weight.astype(f32).astype(ml_dtypes.bfloat16)
    return weight.reshape(count * BOX, BOX * BOX)


def cyl_matrix_np():
    f32 = np.float32
    center = f32((BOX - 1) / 2.0)
    xpos = np.arange(BOX, dtype=f32)[:, None, None, None]
    zpos = np.arange(BOX, dtype=f32)[None, :, None, None]
    angle = np.arange(ROTS, dtype=f32)[None, None, :, None] * f32(2.0 * np.pi / ROTS)
    radius = (np.arange(CYCLES, dtype=f32)[None, None, None, :] + f32(0.5)) * f32(
        BOX / (2.0 * CYCLES)
    )
    wx = np.maximum(f32(0.0), f32(1.0) - np.abs(xpos - center - radius * np.cos(angle)))
    wz = np.maximum(f32(0.0), f32(1.0) - np.abs(zpos - center - radius * np.sin(angle)))
    sample = (wx * wz).astype(f32).astype(ml_dtypes.bfloat16)
    return sample.reshape(BOX * BOX, ROTS * CYCLES)


@functools.lru_cache(maxsize=None)
def touched_points():
    sample = cyl_matrix_np().astype(np.float32)
    used = np.nonzero(np.abs(sample).sum(axis=1))[0]
    size = -(-len(used) // 128) * 128
    xs = np.full((size,), -100.0, np.float32)
    zs = np.full((size,), -100.0, np.float32)
    xs[: len(used)] = used // BOX
    zs[: len(used)] = used % BOX
    return xs, zs


def back_points(count, xs, zs):
    center = (BOX - 1) / 2.0
    tilt = jnp.arange(count, dtype=jnp.float32)[:, None, None]
    pixel = jnp.arange(BOX, dtype=jnp.float32)[None, :, None]
    theta = (-60.0 + 120.0 * tilt / (TILTS - 1)) * (jnp.pi / 180.0)
    place = (xs[None, None, :] - center) * jnp.cos(theta) + (zs[None, None, :] - center) * jnp.sin(
        theta
    ) + center
    weight = jnp.maximum(0.0, 1.0 - jnp.abs(place - pixel))
    weight = jnp.where(tilt < TILTS, weight, 0.0) / TILTS
    return weight.reshape(count * BOX, xs.shape[0]).astype(jnp.bfloat16)


def sample_points(xs, zs):
    center = (BOX - 1) / 2.0
    angle = jnp.arange(ROTS, dtype=jnp.float32)[None, :, None] * (2.0 * jnp.pi / ROTS)
    radius = (jnp.arange(CYCLES, dtype=jnp.float32)[None, None, :] + 0.5) * (BOX / (2.0 * CYCLES))
    wx = jnp.maximum(0.0, 1.0 - jnp.abs(xs[:, None, None] - center - radius * jnp.cos(angle)))
    wz = jnp.maximum(0.0, 1.0 - jnp.abs(zs[:, None, None] - center - radius * jnp.sin(angle)))
    return (wx * wz).reshape(xs.shape[0], ROTS * CYCLES).astype(jnp.bfloat16)


def shift_table():
    steps = jnp.arange(ROTS, dtype=jnp.int32)
    want = (steps[None, :, None] - steps[:, None, None]) % ROTS
    return (steps[None, None, :] == want).astype(jnp.float32)


def cut_kernel(cap, req_ref, tiles_ref, out_ref):
    ends = out_ref.shape[0]
    width = tiles_ref.shape[2]
    rows = tiles_ref.shape[1]
    span = BOX + 8

    def body(d, carry):
        for s in range(cap):
            k = d * cap + s
            t = req_ref[3 * k]
            r = req_ref[3 * k + 1]
            c = req_ref[3 * k + 2]
            r0 = pl.multiple_of(jnp.minimum((r // 8) * 8, rows - span), 8)
            c0 = pl.multiple_of(jnp.minimum((c // 128) * 128, width - WIN), 128)
            win = tiles_ref[t, pl.ds(r0, span), pl.ds(c0, WIN)].astype(jnp.float32)
            win = pltpu.roll(win, (WIN - (c - c0)) % WIN, 1)[:, :128]
            win = pltpu.roll(win, (span - (r - r0)) % span, 0)
            flip = win[:BOX, :].T
            out_ref[d, :, s * BOX : (s + 1) * BOX] = flip[:BOX, :BOX].astype(out_ref.dtype)
        return carry

    lax.fori_loop(0, ends, body, 0, unroll=2)


def cut_patches(tiles, req, ends, cap):
    flat = req.reshape(-1)
    return pl.pallas_call(
        functools.partial(cut_kernel, cap),
        out_shape=jax.ShapeDtypeStruct((ends, BOX, cap * BOX), tiles.dtype),
        grid_spec=pltpu.PrefetchScalarGridSpec(
            num_scalar_prefetch=1,
            grid=(1,),
            in_specs=[pl.BlockSpec(tiles.shape, lambda i, q: (0, 0, 0))],
            out_specs=pl.BlockSpec((ends, BOX, cap * BOX), lambda i, q: (0, 0, 0)),
        ),
        cost_estimate=pl.CostEstimate(
            flops=ends * cap * BOX * WIN * 64,
            transcendentals=0,
            bytes_accessed=tiles.size * 2 + ends * cap * BOX * BOX * 2,
        ),
    )(flat, tiles)


def double_gather(block, ndev):
    me = lax.axis_index("dev")
    bits = ndev.bit_length() - 1
    for level in range(bits):
        step = ndev >> (level + 1)
        other = lax.ppermute(block, "dev", perm=[(i, i ^ step) for i in range(ndev)])
        low = (me // step) % 2 == 0
        block = jnp.where(
            low, jnp.concatenate([block, other], axis=0), jnp.concatenate([other, block], axis=0)
        )
    rest = block.shape[1:]
    block = block.reshape((2,) * bits + rest)
    block = block.transpose(tuple(range(bits))[::-1] + tuple(range(bits, block.ndim)))
    return block.reshape((ndev,) + rest)


def per_device(tiles, footprint, classes, rotations, references):
    ndev = lax.axis_size("dev")
    count = footprint.shape[0]
    asks = count * TILTS
    cap = (2 * asks + ndev - 1) // ndev
    held = tiles.shape[0]
    flat = footprint.reshape(asks, 3)
    owner = flat[:, 0] // held
    local = flat[:, 0] - owner * held
    hits = (owner[:, None] == jnp.arange(ndev, dtype=jnp.int32)[None, :]).astype(jnp.int32)
    slot = jnp.sum((jnp.cumsum(hits, axis=0) - hits) * hits, axis=1)
    values = jnp.stack([local, flat[:, 1], flat[:, 2]], axis=-1)
    spot = (owner[None, None, :] == jnp.arange(ndev, dtype=jnp.int32)[:, None, None]) & (
        slot[None, None, :] == jnp.arange(cap, dtype=jnp.int32)[None, :, None]
    )
    wanted = jnp.sum(jnp.where(spot[..., None], values[None, None], 0), axis=2)
    asked = lax.all_to_all(wanted, "dev", split_axis=0, concat_axis=0, tiled=True)
    patches_cut = cut_patches(tiles, asked.reshape(ndev * cap, 3), ndev, cap)
    xs_np, zs_np = touched_points()
    xs, zs, patches_cut = lax.optimization_barrier(
        (jnp.asarray(xs_np), jnp.asarray(zs_np), patches_cut)
    )
    arrived = lax.all_to_all(patches_cut, "dev", split_axis=0, concat_axis=0, tiled=True)
    rows_of = arrived[owner]
    flipped = sum(
        jnp.where(slot[:, None, None] == s, rows_of[:, :, s * BOX : (s + 1) * BOX], 0)
        for s in range(cap)
    ).reshape(count, TILTS, BOX, BOX)
    padded = TILTS + TILTS % 2
    flipped = jnp.pad(flipped, ((0, 0), (0, padded - TILTS), (0, 0), (0, 0)))
    flipped = flipped.reshape(count, padded * BOX, BOX)
    volume = jnp.einsum(
        "pky,kn->pyn", flipped, back_points(padded, xs, zs), preferred_element_type=jnp.float32
    )
    volume = volume.astype(jnp.bfloat16).reshape(count * BOX, xs.shape[0])
    sample = lax.optimization_barrier(sample_points(xs, zs))
    cyl = jnp.dot(volume, sample, preferred_element_type=jnp.float32)
    cyl = cyl.astype(jnp.bfloat16).reshape(count, BOX, ROTS * CYCLES)
    owned = references.shape[0]
    parts = BOX // owned
    local_t = references.reshape(owned, ROTS, CYCLES).transpose(1, 0, 2).reshape(ROTS, owned * CYCLES)
    gathered = double_gather(local_t[None], ndev)
    gathered = gathered.reshape(CLASSES, parts, ROTS, owned * CYCLES)
    ref_float = gathered.astype(jnp.float32)
    ref_power = jnp.mean(ref_float * ref_float, axis=(1, 2, 3))
    cyl_three = (
        cyl.reshape(count, BOX, ROTS, CYCLES)
        .transpose(0, 2, 1, 3)
        .reshape(count, ROTS, parts, owned * CYCLES)
    )
    corr = sum(
        jnp.einsum(
            "pfm,cgm->pfgc", cyl_three[:, :, q], gathered[:, q], preferred_element_type=jnp.float32
        )
        for q in range(parts)
    )
    raw = jnp.einsum("pfgc,kfg->pck", corr, shift_table(), precision=lax.Precision.HIGHEST)
    cyl_float = cyl.astype(jnp.float32)
    power = jnp.mean(cyl_float.reshape(count, -1) ** 2, axis=1)
    total = BOX * ROTS * CYCLES
    scores = raw / jnp.sqrt(
        total * (power[:, None, None] + 1e-06) * (ref_power[None, :, None] + 1e-06)
    )
    scores = scores.reshape(count, CLASSES * ROTS)
    doubled = jnp.concatenate([cyl, cyl], axis=2)
    turned = jnp.stack(
        [
            lax.dynamic_slice_in_dim(doubled[p], rotations[p] * CYCLES, ROTS * CYCLES, axis=1)
            for p in range(count)
        ]
    )
    member = (classes[:, None] == jnp.arange(CLASSES, dtype=jnp.int32)[None, :]).astype(
        jnp.bfloat16
    )
    placed = member[:, :, None, None] * turned[:, None, :, :]
    placed = placed.reshape(count, ndev, owned, ROTS * CYCLES)
    landed = lax.all_to_all(placed, "dev", split_axis=1, concat_axis=0, tiled=True)
    class_sums = jnp.sum(landed.astype(jnp.float32), axis=(0, 1))
    return (scores, class_sums)


def solution(mesh):
    in_specs = (P("dev", None, None), P("dev", None, None), P("dev"), P("dev"), P("dev", None))
    out_specs = (P("dev", None), P("dev", None))
    return jax.shard_map(
        per_device, mesh=mesh, in_specs=in_specs, out_specs=out_specs, check_vma=False
    )
```

```python
import functools

import jax
import jax.numpy as jnp
import ml_dtypes
import numpy as np
from jax import lax
from jax.experimental import pallas as pl
from jax.experimental.pallas import tpu as pltpu
from jax.sharding import PartitionSpec as P

TILTS = 21
BOX = 64
CYCLES = 16
ROTS = 32
CLASSES = 16
WIN = 256


def back_matrix_np(count):
    f32 = np.float32
    center = f32((BOX - 1) / 2.0)
    tilt = np.arange(count, dtype=f32)[:, None, None, None]
    pixel = np.arange(BOX, dtype=f32)[None, :, None, None]
    xpos = np.arange(BOX, dtype=f32)[None, None, :, None]
    zpos = np.arange(BOX, dtype=f32)[None, None, None, :]
    theta = (f32(-60.0) + f32(120.0) * tilt / f32(TILTS - 1)) * f32(np.pi / 180.0)
    place = (xpos - center) * np.cos(theta) + (zpos - center) * np.sin(theta) + center
    weight = np.maximum(f32(0.0), f32(1.0) - np.abs(place - pixel))
    weight = np.where(tilt < TILTS, weight, f32(0.0)) / f32(TILTS)
    weight = weight.astype(f32).astype(ml_dtypes.bfloat16)
    return weight.reshape(count * BOX, BOX * BOX)


def cyl_matrix_np():
    f32 = np.float32
    center = f32((BOX - 1) / 2.0)
    xpos = np.arange(BOX, dtype=f32)[:, None, None, None]
    zpos = np.arange(BOX, dtype=f32)[None, :, None, None]
    angle = np.arange(ROTS, dtype=f32)[None, None, :, None] * f32(2.0 * np.pi / ROTS)
    radius = (np.arange(CYCLES, dtype=f32)[None, None, None, :] + f32(0.5)) * f32(
        BOX / (2.0 * CYCLES)
    )
    wx = np.maximum(f32(0.0), f32(1.0) - np.abs(xpos - center - radius * np.cos(angle)))
    wz = np.maximum(f32(0.0), f32(1.0) - np.abs(zpos - center - radius * np.sin(angle)))
    sample = (wx * wz).astype(f32).astype(ml_dtypes.bfloat16)
    return sample.reshape(BOX * BOX, ROTS * CYCLES)


@functools.lru_cache(maxsize=None)
def touched_points():
    sample = cyl_matrix_np().astype(np.float32)
    used = np.nonzero(np.abs(sample).sum(axis=1))[0]
    size = -(-len(used) // 128) * 128
    xs = np.full((size,), -100.0, np.float32)
    zs = np.full((size,), -100.0, np.float32)
    xs[: len(used)] = used // BOX
    zs[: len(used)] = used % BOX
    return xs, zs


def back_points(count, xs, zs):
    center = (BOX - 1) / 2.0
    tilt = jnp.arange(count, dtype=jnp.float32)[:, None, None]
    pixel = jnp.arange(BOX, dtype=jnp.float32)[None, :, None]
    theta = (-60.0 + 120.0 * tilt / (TILTS - 1)) * (jnp.pi / 180.0)
    place = (xs[None, None, :] - center) * jnp.cos(theta) + (zs[None, None, :] - center) * jnp.sin(
        theta
    ) + center
    weight = jnp.maximum(0.0, 1.0 - jnp.abs(place - pixel))
    weight = jnp.where(tilt < TILTS, weight, 0.0) / TILTS
    return weight.reshape(count * BOX, xs.shape[0]).astype(jnp.bfloat16)


def sample_points(xs, zs):
    center = (BOX - 1) / 2.0
    angle = jnp.arange(ROTS, dtype=jnp.float32)[None, :, None] * (2.0 * jnp.pi / ROTS)
    radius = (jnp.arange(CYCLES, dtype=jnp.float32)[None, None, :] + 0.5) * (BOX / (2.0 * CYCLES))
    wx = jnp.maximum(0.0, 1.0 - jnp.abs(xs[:, None, None] - center - radius * jnp.cos(angle)))
    wz = jnp.maximum(0.0, 1.0 - jnp.abs(zs[:, None, None] - center - radius * jnp.sin(angle)))
    return (wx * wz).reshape(xs.shape[0], ROTS * CYCLES).astype(jnp.bfloat16)


def shift_table():
    steps = jnp.arange(ROTS, dtype=jnp.int32)
    want = (steps[None, :, None] - steps[:, None, None]) % ROTS
    return (steps[None, None, :] == want).astype(jnp.float32)


def cut_kernel(cap, req_ref, tiles_ref, out_ref):
    ends = out_ref.shape[0]
    width = tiles_ref.shape[2]
    rows = tiles_ref.shape[1]
    span = BOX + 8

    def body(d, carry):
        for s in range(cap):
            k = d * cap + s
            t = req_ref[3 * k]
            r = req_ref[3 * k + 1]
            c = req_ref[3 * k + 2]
            r0 = pl.multiple_of(jnp.minimum((r // 8) * 8, rows - span), 8)
            c0 = pl.multiple_of(jnp.minimum((c // 128) * 128, width - WIN), 128)
            win = tiles_ref[t, pl.ds(r0, span), pl.ds(c0, WIN)].astype(jnp.float32)
            win = pltpu.roll(win, (WIN - (c - c0)) % WIN, 1)[:, :128]
            win = pltpu.roll(win, (span - (r - r0)) % span, 0)
            flip = win[:BOX, :].T
            out_ref[d, :, s * BOX : (s + 1) * BOX] = flip[:BOX, :BOX].astype(out_ref.dtype)
        return carry

    lax.fori_loop(0, ends, body, 0, unroll=2)


def cut_patches(tiles, req, ends, cap):
    flat = req.reshape(-1)
    return pl.pallas_call(
        functools.partial(cut_kernel, cap),
        out_shape=jax.ShapeDtypeStruct((ends, BOX, cap * BOX), tiles.dtype),
        grid_spec=pltpu.PrefetchScalarGridSpec(
            num_scalar_prefetch=1,
            grid=(1,),
            in_specs=[pl.BlockSpec(tiles.shape, lambda i, q: (0, 0, 0))],
            out_specs=pl.BlockSpec((ends, BOX, cap * BOX), lambda i, q: (0, 0, 0)),
        ),
        cost_estimate=pl.CostEstimate(
            flops=ends * cap * BOX * WIN * 64,
            transcendentals=0,
            bytes_accessed=tiles.size * 2 + ends * cap * BOX * BOX * 2,
        ),
    )(flat, tiles)


def double_gather(block, ndev):
    me = lax.axis_index("dev")
    bits = ndev.bit_length() - 1
    for level in range(bits):
        step = ndev >> (level + 1)
        other = lax.ppermute(block, "dev", perm=[(i, i ^ step) for i in range(ndev)])
        low = (me // step) % 2 == 0
        block = jnp.where(
            low, jnp.concatenate([block, other], axis=0), jnp.concatenate([other, block], axis=0)
        )
    rest = block.shape[1:]
    block = block.reshape((2,) * bits + rest)
    block = block.transpose(tuple(range(bits))[::-1] + tuple(range(bits, block.ndim)))
    return block.reshape((ndev,) + rest)


def per_device(tiles, footprint, classes, rotations, references):
    ndev = lax.axis_size("dev")
    count = footprint.shape[0]
    asks = count * TILTS
    cap = (2 * asks + ndev - 1) // ndev
    held = tiles.shape[0]
    flat = footprint.reshape(asks, 3)
    owner = flat[:, 0] // held
    local = flat[:, 0] - owner * held
    hits = (owner[:, None] == jnp.arange(ndev, dtype=jnp.int32)[None, :]).astype(jnp.int32)
    slot = jnp.sum((jnp.cumsum(hits, axis=0) - hits) * hits, axis=1)
    values = jnp.stack([local, flat[:, 1], flat[:, 2]], axis=-1)
    spot = (owner[None, None, :] == jnp.arange(ndev, dtype=jnp.int32)[:, None, None]) & (
        slot[None, None, :] == jnp.arange(cap, dtype=jnp.int32)[None, :, None]
    )
    wanted = jnp.sum(jnp.where(spot[..., None], values[None, None], 0), axis=2)
    asked = lax.all_to_all(wanted, "dev", split_axis=0, concat_axis=0, tiled=True)
    patches_cut = cut_patches(tiles, asked.reshape(ndev * cap, 3), ndev, cap)
    xs_np, zs_np = touched_points()
    xs, zs, patches_cut = lax.optimization_barrier(
        (jnp.asarray(xs_np), jnp.asarray(zs_np), patches_cut)
    )
    arrived = lax.all_to_all(patches_cut, "dev", split_axis=0, concat_axis=0, tiled=True)
    rows_of = arrived[owner]
    flipped = sum(
        jnp.where(slot[:, None, None] == s, rows_of[:, :, s * BOX : (s + 1) * BOX], 0)
        for s in range(cap)
    ).reshape(count, TILTS, BOX, BOX)
    padded = TILTS + TILTS % 2
    flipped = jnp.pad(flipped, ((0, 0), (0, padded - TILTS), (0, 0), (0, 0)))
    flipped = flipped.reshape(count, padded * BOX, BOX)
    volume = jnp.einsum(
        "pky,kn->pyn", flipped, back_points(padded, xs, zs), preferred_element_type=jnp.float32
    )
    volume = volume.astype(jnp.bfloat16).reshape(count * BOX, xs.shape[0])
    sample = lax.optimization_barrier(sample_points(xs, zs))
    cyl = jnp.dot(volume, sample, preferred_element_type=jnp.float32)
    cyl = cyl.astype(jnp.bfloat16).reshape(count, BOX, ROTS * CYCLES)
    owned = references.shape[0]
    doubled = jnp.concatenate([cyl, cyl], axis=2)
    turned = jnp.stack(
        [
            lax.dynamic_slice_in_dim(doubled[p], rotations[p] * CYCLES, ROTS * CYCLES, axis=1)
            for p in range(count)
        ]
    )
    member = (classes[:, None] == jnp.arange(CLASSES, dtype=jnp.int32)[None, :]).astype(
        jnp.bfloat16
    )
    placed = member[:, :, None, None] * turned[:, None, :, :]
    placed = placed.reshape(count, ndev, owned, ROTS * CYCLES)
    parts = BOX // owned
    local_t = references.reshape(owned, ROTS, CYCLES).transpose(1, 0, 2).reshape(ROTS, owned * CYCLES)
    gathered = double_gather(local_t[None], ndev)
    gathered = gathered.reshape(CLASSES, parts, ROTS, owned * CYCLES)
    ref_float = gathered.astype(jnp.float32)
    ref_power = jnp.mean(ref_float * ref_float, axis=(1, 2, 3))
    cyl_three = (
        cyl.reshape(count, BOX, ROTS, CYCLES)
        .transpose(0, 2, 1, 3)
        .reshape(count, ROTS, parts, owned * CYCLES)
    )
    corr = sum(
        jnp.einsum(
            "pfm,cgm->pfgc", cyl_three[:, :, q], gathered[:, q], preferred_element_type=jnp.float32
        )
        for q in range(parts)
    )
    raw = jnp.einsum("pfgc,kfg->pck", corr, shift_table(), precision=lax.Precision.HIGHEST)
    cyl_late, _ = lax.optimization_barrier((cyl, placed))
    cyl_float = cyl_late.astype(jnp.float32)
    power = jnp.mean(cyl_float.reshape(count, -1) ** 2, axis=1)
    total = BOX * ROTS * CYCLES
    scores = raw / jnp.sqrt(
        total * (power[:, None, None] + 1e-06) * (ref_power[None, :, None] + 1e-06)
    )
    scores = scores.reshape(count, CLASSES * ROTS)
    landed = lax.all_to_all(placed, "dev", split_axis=1, concat_axis=0, tiled=True)
    class_sums = jnp.sum(landed.astype(jnp.float32), axis=(0, 1))
    return (scores, class_sums)


def solution(mesh):
    in_specs = (P("dev", None, None), P("dev", None, None), P("dev"), P("dev"), P("dev", None))
    out_specs = (P("dev", None), P("dev", None))
    return jax.shard_map(
        per_device, mesh=mesh, in_specs=in_specs, out_specs=out_specs, check_vma=False
    )
```

```python
import functools

import jax
import jax.numpy as jnp
import ml_dtypes
import numpy as np
from jax import lax
from jax.experimental import pallas as pl
from jax.experimental.pallas import tpu as pltpu
from jax.sharding import PartitionSpec as P

TILTS = 21
BOX = 64
CYCLES = 16
ROTS = 32
CLASSES = 16
WIN = 256


def back_matrix_np(count):
    f32 = np.float32
    center = f32((BOX - 1) / 2.0)
    tilt = np.arange(count, dtype=f32)[:, None, None, None]
    pixel = np.arange(BOX, dtype=f32)[None, :, None, None]
    xpos = np.arange(BOX, dtype=f32)[None, None, :, None]
    zpos = np.arange(BOX, dtype=f32)[None, None, None, :]
    theta = (f32(-60.0) + f32(120.0) * tilt / f32(TILTS - 1)) * f32(np.pi / 180.0)
    place = (xpos - center) * np.cos(theta) + (zpos - center) * np.sin(theta) + center
    weight = np.maximum(f32(0.0), f32(1.0) - np.abs(place - pixel))
    weight = np.where(tilt < TILTS, weight, f32(0.0)) / f32(TILTS)
    weight = weight.astype(f32).astype(ml_dtypes.bfloat16)
    return weight.reshape(count * BOX, BOX * BOX)


def cyl_matrix_np():
    f32 = np.float32
    center = f32((BOX - 1) / 2.0)
    xpos = np.arange(BOX, dtype=f32)[:, None, None, None]
    zpos = np.arange(BOX, dtype=f32)[None, :, None, None]
    angle = np.arange(ROTS, dtype=f32)[None, None, :, None] * f32(2.0 * np.pi / ROTS)
    radius = (np.arange(CYCLES, dtype=f32)[None, None, None, :] + f32(0.5)) * f32(
        BOX / (2.0 * CYCLES)
    )
    wx = np.maximum(f32(0.0), f32(1.0) - np.abs(xpos - center - radius * np.cos(angle)))
    wz = np.maximum(f32(0.0), f32(1.0) - np.abs(zpos - center - radius * np.sin(angle)))
    sample = (wx * wz).astype(f32).astype(ml_dtypes.bfloat16)
    return sample.reshape(BOX * BOX, ROTS * CYCLES)


@functools.lru_cache(maxsize=None)
def touched_points():
    sample = cyl_matrix_np().astype(np.float32)
    used = np.nonzero(np.abs(sample).sum(axis=1))[0]
    size = -(-len(used) // 128) * 128
    xs = np.full((size,), -100.0, np.float32)
    zs = np.full((size,), -100.0, np.float32)
    xs[: len(used)] = used // BOX
    zs[: len(used)] = used % BOX
    return xs, zs


def back_points(count, xs, zs):
    center = (BOX - 1) / 2.0
    tilt = jnp.arange(count, dtype=jnp.float32)[:, None, None]
    pixel = jnp.arange(BOX, dtype=jnp.float32)[None, :, None]
    theta = (-60.0 + 120.0 * tilt / (TILTS - 1)) * (jnp.pi / 180.0)
    place = (xs[None, None, :] - center) * jnp.cos(theta) + (zs[None, None, :] - center) * jnp.sin(
        theta
    ) + center
    weight = jnp.maximum(0.0, 1.0 - jnp.abs(place - pixel))
    weight = jnp.where(tilt < TILTS, weight, 0.0) / TILTS
    return weight.reshape(count * BOX, xs.shape[0]).astype(jnp.bfloat16)


def sample_points(xs, zs):
    center = (BOX - 1) / 2.0
    angle = jnp.arange(ROTS, dtype=jnp.float32)[None, :, None] * (2.0 * jnp.pi / ROTS)
    radius = (jnp.arange(CYCLES, dtype=jnp.float32)[None, None, :] + 0.5) * (BOX / (2.0 * CYCLES))
    wx = jnp.maximum(0.0, 1.0 - jnp.abs(xs[:, None, None] - center - radius * jnp.cos(angle)))
    wz = jnp.maximum(0.0, 1.0 - jnp.abs(zs[:, None, None] - center - radius * jnp.sin(angle)))
    return (wx * wz).reshape(xs.shape[0], ROTS * CYCLES).astype(jnp.bfloat16)


def shift_table():
    steps = jnp.arange(ROTS, dtype=jnp.int32)
    want = (steps[None, :, None] - steps[:, None, None]) % ROTS
    return (steps[None, None, :] == want).astype(jnp.float32)


def cut_kernel(cap, req_ref, tiles_ref, out_ref):
    ends = out_ref.shape[0]
    width = tiles_ref.shape[2]
    rows = tiles_ref.shape[1]
    span = BOX + 8

    def body(d, carry):
        for s in range(cap):
            k = d * cap + s
            t = req_ref[3 * k]
            r = req_ref[3 * k + 1]
            c = req_ref[3 * k + 2]
            r0 = pl.multiple_of(jnp.minimum((r // 8) * 8, rows - span), 8)
            c0 = pl.multiple_of(jnp.minimum((c // 128) * 128, width - WIN), 128)
            win = tiles_ref[t, pl.ds(r0, span), pl.ds(c0, WIN)].astype(jnp.float32)
            win = pltpu.roll(win, (WIN - (c - c0)) % WIN, 1)[:, :128]
            win = pltpu.roll(win, (span - (r - r0)) % span, 0)
            flip = win[:BOX, :].T
            out_ref[d, :, s * BOX : (s + 1) * BOX] = flip[:BOX, :BOX].astype(out_ref.dtype)
        return carry

    lax.fori_loop(0, ends, body, 0, unroll=2)


def cut_patches(tiles, req, ends, cap):
    flat = req.reshape(-1)
    return pl.pallas_call(
        functools.partial(cut_kernel, cap),
        out_shape=jax.ShapeDtypeStruct((ends, BOX, cap * BOX), tiles.dtype),
        grid_spec=pltpu.PrefetchScalarGridSpec(
            num_scalar_prefetch=1,
            grid=(1,),
            in_specs=[pl.BlockSpec(tiles.shape, lambda i, q: (0, 0, 0))],
            out_specs=pl.BlockSpec((ends, BOX, cap * BOX), lambda i, q: (0, 0, 0)),
        ),
        cost_estimate=pl.CostEstimate(
            flops=ends * cap * BOX * WIN * 64,
            transcendentals=0,
            bytes_accessed=tiles.size * 2 + ends * cap * BOX * BOX * 2,
        ),
    )(flat, tiles)


def double_gather(block, ndev):
    me = lax.axis_index("dev")
    bits = ndev.bit_length() - 1
    for level in range(bits):
        step = ndev >> (level + 1)
        other = lax.ppermute(block, "dev", perm=[(i, i ^ step) for i in range(ndev)])
        low = (me // step) % 2 == 0
        block = jnp.where(
            low, jnp.concatenate([block, other], axis=0), jnp.concatenate([other, block], axis=0)
        )
    rest = block.shape[1:]
    block = block.reshape((2,) * bits + rest)
    block = block.transpose(tuple(range(bits))[::-1] + tuple(range(bits, block.ndim)))
    return block.reshape((ndev,) + rest)


def per_device(tiles, footprint, classes, rotations, references):
    ndev = lax.axis_size("dev")
    count = footprint.shape[0]
    asks = count * TILTS
    cap = (2 * asks + ndev - 1) // ndev
    held = tiles.shape[0]
    flat = footprint.reshape(asks, 3)
    owner = flat[:, 0] // held
    local = flat[:, 0] - owner * held
    hits = (owner[:, None] == jnp.arange(ndev, dtype=jnp.int32)[None, :]).astype(jnp.int32)
    slot = jnp.sum((jnp.cumsum(hits, axis=0) - hits) * hits, axis=1)
    values = jnp.stack([local, flat[:, 1], flat[:, 2]], axis=-1)
    spot = (owner[None, None, :] == jnp.arange(ndev, dtype=jnp.int32)[:, None, None]) & (
        slot[None, None, :] == jnp.arange(cap, dtype=jnp.int32)[None, :, None]
    )
    wanted = jnp.sum(jnp.where(spot[..., None], values[None, None], 0), axis=2)
    asked = lax.all_to_all(wanted, "dev", split_axis=0, concat_axis=0, tiled=True)
    patches_cut = cut_patches(tiles, asked.reshape(ndev * cap, 3), ndev, cap)
    xs_np, zs_np = touched_points()
    xs, zs, patches_cut = lax.optimization_barrier(
        (jnp.asarray(xs_np), jnp.asarray(zs_np), patches_cut)
    )
    arrived = lax.all_to_all(patches_cut, "dev", split_axis=0, concat_axis=0, tiled=True)
    rows_of = arrived[owner]
    flipped = sum(
        jnp.where(slot[:, None, None] == s, rows_of[:, :, s * BOX : (s + 1) * BOX], 0)
        for s in range(cap)
    ).reshape(count, TILTS, BOX, BOX)
    padded = TILTS
    flipped = jnp.pad(flipped, ((0, 0), (0, padded - TILTS), (0, 0), (0, 0)))
    flipped = flipped.reshape(count, padded * BOX, BOX)
    volume = jnp.einsum(
        "pky,kn->pyn", flipped, back_points(padded, xs, zs), preferred_element_type=jnp.float32
    )
    volume = volume.astype(jnp.bfloat16).reshape(count * BOX, xs.shape[0])
    sample = lax.optimization_barrier(sample_points(xs, zs))
    cyl = jnp.dot(volume, sample, preferred_element_type=jnp.float32)
    cyl = cyl.astype(jnp.bfloat16).reshape(count, BOX, ROTS * CYCLES)
    owned = references.shape[0]
    doubled = jnp.concatenate([cyl, cyl], axis=2)
    turned = jnp.stack(
        [
            lax.dynamic_slice_in_dim(doubled[p], rotations[p] * CYCLES, ROTS * CYCLES, axis=1)
            for p in range(count)
        ]
    )
    member = (classes[:, None] == jnp.arange(CLASSES, dtype=jnp.int32)[None, :]).astype(
        jnp.bfloat16
    )
    placed = member[:, :, None, None] * turned[:, None, :, :]
    placed = placed.reshape(count, ndev, owned, ROTS * CYCLES)
    parts = BOX // owned
    local_t = references.reshape(owned, ROTS, CYCLES).transpose(1, 0, 2).reshape(ROTS, owned * CYCLES)
    gathered = double_gather(local_t[None], ndev)
    gathered = gathered.reshape(CLASSES, parts, ROTS, owned * CYCLES)
    ref_float = gathered.astype(jnp.float32)
    ref_power = jnp.mean(ref_float * ref_float, axis=(1, 2, 3))
    cyl_three = (
        cyl.reshape(count, BOX, ROTS, CYCLES)
        .transpose(0, 2, 1, 3)
        .reshape(count, ROTS, parts, owned * CYCLES)
    )
    corr = sum(
        jnp.einsum(
            "pfm,cgm->pfgc", cyl_three[:, :, q], gathered[:, q], preferred_element_type=jnp.float32
        )
        for q in range(parts)
    )
    raw = jnp.einsum("pfgc,kfg->pck", corr, shift_table(), precision=lax.Precision.HIGHEST)
    cyl_late, _ = lax.optimization_barrier((cyl, placed))
    cyl_float = cyl_late.astype(jnp.float32)
    power = jnp.mean(cyl_float.reshape(count, -1) ** 2, axis=1)
    total = BOX * ROTS * CYCLES
    scores = raw / jnp.sqrt(
        total * (power[:, None, None] + 1e-06) * (ref_power[None, :, None] + 1e-06)
    )
    scores = scores.reshape(count, CLASSES * ROTS)
    landed = lax.all_to_all(placed, "dev", split_axis=1, concat_axis=0, tiled=True)
    class_sums = jnp.sum(landed.astype(jnp.float32), axis=(0, 1))
    return (scores, class_sums)


def solution(mesh):
    in_specs = (P("dev", None, None), P("dev", None, None), P("dev"), P("dev"), P("dev", None))
    out_specs = (P("dev", None), P("dev", None))
    return jax.shard_map(
        per_device, mesh=mesh, in_specs=in_specs, out_specs=out_specs, check_vma=False
    )
```
